32 devices in a mesh: seq: 8 (over z, y), batch: 4 (over x, core).
Axes of the slice: x: 2, y: 2, z: 4, core: 2. Of those that a mesh axis runs over, the one named last changes fastest.
Arguments:
- query_rows: bfloat16 [8192, 2048], P(('batch', 'seq')), parts along dimension 0, may hold values from -6 to 6
- key_rows: bfloat16 [8192, 2048], P(('batch', 'seq')), parts along dimension 0, may hold values from -6 to 6
- value_rows: bfloat16 [8192, 2048], P(('batch', 'seq')), parts along dimension 0, may hold values from -6 to 6
- out_grad: bfloat16 [8192, 2048], P(('batch', 'seq')), parts along dimension 0, may hold values from -6 to 6
Outputs:
- attended: bfloat16 [8192, 2048], P(('batch', 'seq')), parts along dimension 0
- query_grad: bfloat16 [8192, 2048], P(('batch', 'seq')), parts along dimension 0
- key_grad: bfloat16 [8192, 2048], P(('batch', 'seq')), parts along dimension 0
- value_grad: bfloat16 [8192, 2048], P(('batch', 'seq')), parts along dimension 0
The draws below stay inside these ranges and needn't reach their ends.
There are 4 independent parts, one for each index of `batch`. The reference program is written for one: setup_inputs(seed, part) draws one part's arguments, and reference() takes and returns one part's arrays. A program takes and returns all parts, laid end to end along the dimension named above; each array names one. Nothing has to cross between parts.
All inputs are finite; a program needn't handle non-finite values.
Results may differ from the reference program's by a relative error of at most 0.025.
Values may be sent and summed in bfloat16 or wider, within the bound.
No kernel may reach another device: no remote copies, remote signals or barrier semaphores. Data moves between devices by JAX's collectives and lax.ppermute only.
A program may use at most 128 MiB of HBM per device.

```python
import functools
import math
import jax
import jax.numpy as jnp
from jax import lax

HEADS = 16
HEAD_DIM = 128
D = 2048
LEAF = 256
POOLED = 128
LEVELS = 3
SEQ = 2048
N_SEQ = 8


def paired_rows(key):
    base_key = jax.random.fold_in(key, 31)
    query_key, other_key = jax.random.split(base_key, 2)
    queries = jnp.clip(1.5 * jax.random.normal(query_key, (SEQ, D), jnp.float32), -6.0, 6.0)
    keys_drawn = jnp.clip(1.5 * jax.random.normal(other_key, (SEQ, D), jnp.float32), -6.0, 6.0)
    return (queries, keys_drawn)


def draw_query_rows(key, part):
    return paired_rows(key)[0].astype(jnp.bfloat16)


def draw_key_rows(key, part):
    return paired_rows(key)[1].astype(jnp.bfloat16)


def steps_of(stream_key, shape, shards, least, largest):
    level, own = 1.0, jax.random.fold_in(stream_key, 6)
    for position, shards_of in shards:
        heights = jnp.exp(jax.random.uniform(jax.random.fold_in(own, position), (shards_of,), jnp.float32, least / len(shards), largest / len(shards)))
        level = level * jnp.repeat(heights, shape[position] // shards_of).reshape([-1 if axis == position else 1 for axis in range(len(shape))])
    return level


def noise(key, extent, width, bound, shards=(), kind=jnp.bfloat16):
    level = steps_of(key, extent, shards, -0.22, 0.18) if shards else 1.0
    drawn = jax.random.normal(key, extent, jnp.float32) * width * level
    return jnp.minimum(jnp.maximum(drawn, -bound), bound).astype(kind)


def setup_inputs(seed: int = 0, part: int = 0) -> dict:
    splits = jax.random.split(jax.random.key(seed), 5)
    part_splits = jax.random.split(jax.random.fold_in(splits[4], part), 5)
    return {
        "query_rows": draw_query_rows(jax.random.fold_in(jax.random.fold_in(splits[4], part), 71), part),
        "key_rows": draw_key_rows(jax.random.fold_in(jax.random.fold_in(splits[4], part), 71), part),
        "value_rows": noise(part_splits[2], (SEQ, D), 1.0, 6.0, ((0, 8),)),
        "out_grad": noise(part_splits[3], (SEQ, D), 1.0, 6.0, ((0, 8),)),
    }


def round_trip(values):
    return lax.optimization_barrier(values.astype(jnp.bfloat16)).astype(jnp.float32)


def pooled_levels(source):
    results = []
    for step_level in range(1, LEVELS):
        pool_size = (LEAF // POOLED) * 2 ** step_level
        results.append(jnp.mean(source.astype(jnp.float32).reshape(SEQ // pool_size, pool_size, D), axis=1))
    return results


def block_pass(block_id, query_rows, key_rows, value_rows, out_grad, pooled_keys, pooled_values):
    first_row = (block_id * LEAF).astype(jnp.int32)
    sibling_row = ((block_id + 1 - 2 * (block_id % 2)) * LEAF).astype(jnp.int32)
    queries = lax.dynamic_slice_in_dim(query_rows, first_row, LEAF, 0).astype(jnp.float32)
    grads = lax.dynamic_slice_in_dim(out_grad, first_row, LEAF, 0).astype(jnp.float32)
    key_parts = [lax.dynamic_slice_in_dim(key_rows, first_row, LEAF, 0).astype(jnp.float32),
                 lax.dynamic_slice_in_dim(key_rows, sibling_row, LEAF, 0).astype(jnp.float32)]
    value_parts = [lax.dynamic_slice_in_dim(value_rows, first_row, LEAF, 0).astype(jnp.float32),
                   lax.dynamic_slice_in_dim(value_rows, sibling_row, LEAF, 0).astype(jnp.float32)]
    bias_parts = [jnp.zeros((2 * LEAF,), jnp.float32)]
    for step_level in range(1, LEVELS):
        half_index = block_id // (2 ** step_level)
        partner = half_index + 1 - 2 * (half_index % 2)
        far_first = (partner * POOLED).astype(jnp.int32)
        key_parts.append(round_trip(lax.dynamic_slice_in_dim(pooled_keys[step_level - 1], far_first, POOLED, 0)))
        value_parts.append(round_trip(lax.dynamic_slice_in_dim(pooled_values[step_level - 1], far_first, POOLED, 0)))
        bias_parts.append(jnp.full((POOLED,), math.log((LEAF // POOLED) * 2 ** step_level), jnp.float32))
    all_keys = jnp.concatenate(key_parts, axis=0)
    all_values = jnp.concatenate(value_parts, axis=0)
    key_bias = jnp.concatenate(bias_parts, axis=0)
    key_count = all_keys.shape[0]
    score_scale = HEAD_DIM ** -0.5
    query_heads = queries.reshape(LEAF, HEADS, HEAD_DIM)
    grad_heads = grads.reshape(LEAF, HEADS, HEAD_DIM)
    key_heads = all_keys.reshape(key_count, HEADS, HEAD_DIM)
    value_heads = all_values.reshape(key_count, HEADS, HEAD_DIM)
    scores = jnp.einsum("qhd,khd->hqk", query_heads, key_heads) * score_scale + key_bias
    row_max = jnp.max(scores, axis=-1, keepdims=True)
    log_total = row_max + jnp.log(jnp.sum(jnp.exp(scores - row_max), axis=-1, keepdims=True))
    weights = jnp.exp(scores - log_total)
    weights_low = round_trip(weights)
    attended = jnp.einsum("hqk,khd->qhd", weights_low, value_heads).astype(jnp.bfloat16)
    row_dot = jnp.einsum("qhd,qhd->hq", grad_heads, attended.astype(jnp.float32))[..., None]
    weight_grad = jnp.einsum("qhd,khd->hqk", grad_heads, value_heads)
    score_grad = round_trip(weights * (weight_grad - row_dot))
    query_grad = (jnp.einsum("hqk,khd->qhd", score_grad, key_heads) * score_scale).astype(jnp.bfloat16)
    key_terms = jnp.einsum("hqk,qhd->khd", score_grad, query_heads) * score_scale
    value_terms = jnp.einsum("hqk,qhd->khd", weights_low, grad_heads)
    return (attended.reshape(LEAF, D), query_grad.reshape(LEAF, D),
            key_terms.reshape(key_count, D), value_terms.reshape(key_count, D))


def gather_terms(key_terms):
    own_part = key_terms[:, :LEAF]
    sibling_part = round_trip(key_terms[:, LEAF:2 * LEAF])
    from_sibling = sibling_part.reshape(N_SEQ // 2, 2, LEAF, D)[:, ::-1].reshape(N_SEQ, LEAF, D)
    summed = (own_part + from_sibling).reshape(SEQ, D)
    for step_level in range(1, LEVELS):
        blocks_per_half = 2 ** step_level
        first_col = 2 * LEAF + (step_level - 1) * POOLED
        level_part = key_terms[:, first_col:first_col + POOLED]
        by_half = jnp.sum(level_part.reshape(N_SEQ // blocks_per_half, blocks_per_half, POOLED, D), axis=1)
        swapped = by_half.reshape(N_SEQ // (2 * blocks_per_half), 2, POOLED, D)[:, ::-1]
        level_rows = swapped.reshape(-1, D)
        pool_size = (LEAF // POOLED) * blocks_per_half
        spread = jnp.broadcast_to(level_rows[:, None, :] / pool_size, (level_rows.shape[0], pool_size, D))
        summed = summed + spread.reshape(SEQ, D)
    return summed.astype(jnp.bfloat16)


def reference(query_rows, key_rows, value_rows, out_grad):
    pass_fn = functools.partial(block_pass, query_rows=query_rows, key_rows=key_rows, value_rows=value_rows,
                                out_grad=out_grad, pooled_keys=pooled_levels(key_rows),
                                pooled_values=pooled_levels(value_rows))
    attended, query_grad, key_terms, value_terms = lax.map(pass_fn, jnp.arange(N_SEQ, dtype=jnp.int32))
    return (attended.reshape(SEQ, D), query_grad.reshape(SEQ, D),
            gather_terms(key_terms), gather_terms(value_terms))
```

```python
import functools
import math

import jax
import jax.numpy as jnp
from jax import lax
from jax.experimental import pallas as pl
from jax.sharding import PartitionSpec as P

HEAD_DIM = 128
POOLED = 128


def partner_2(block, axis, stride):
    count = lax.axis_size(axis)
    route = []
    for low in range(count):
        high = low | 1 << stride
        if high != low and high < count:
            route += [(low, high), (high, low)]
    return lax.ppermute(block, axis, route)


def combine_halves(mine, other, bit_level, position):
    upper_bit = position // 2**bit_level % 2 == 1
    lower_half = jnp.where(upper_bit, other, mine)
    upper_half = jnp.where(upper_bit, mine, other)
    joined = jnp.concatenate((lower_half, upper_half), axis=1)
    return jnp.mean(joined.reshape(mine.shape[0], mine.shape[1], 2, mine.shape[2]), axis=2)


def attention_kernel(bias_ref, q_ref, do_ref, k_ref, v_ref, o_ref, dq_ref, dk_ref, dv_ref, *, scale):
    q = q_ref[...]
    do = do_ref[...]
    k = k_ref[...]
    v = v_ref[...]
    scores = (
        lax.dot_general(q, k, (((1,), (1,)), ((), ())), preferred_element_type=jnp.float32) * scale
        + bias_ref[...]
    )
    row_max = jnp.max(scores, axis=-1, keepdims=True)
    log_total = row_max + jnp.log(jnp.sum(jnp.exp(scores - row_max), axis=-1, keepdims=True))
    weights = jnp.exp(scores - log_total)
    weights_low = weights.astype(jnp.bfloat16)
    attended = jnp.dot(weights_low, v, preferred_element_type=jnp.float32).astype(jnp.bfloat16)
    o_ref[...] = attended
    row_dot = jnp.sum(
        do.astype(jnp.float32) * attended.astype(jnp.float32), axis=-1, keepdims=True
    )
    weight_grad = lax.dot_general(do, v, (((1,), (1,)), ((), ())), preferred_element_type=jnp.float32)
    score_grad = (weights * (weight_grad - row_dot)).astype(jnp.bfloat16)
    dq_ref[...] = (
        jnp.dot(score_grad, k, preferred_element_type=jnp.float32) * scale
    ).astype(jnp.bfloat16)
    dk_ref[...] = jnp.dot(score_grad.T, q, preferred_element_type=jnp.float32) * scale
    dv_ref[...] = jnp.dot(weights_low.T, do, preferred_element_type=jnp.float32)


def attention(query_rows, out_grad, all_keys, all_values, key_bias, score_scale):
    leaf_rows, model_width = query_rows.shape
    key_count = all_keys.shape[0]
    heads = model_width // HEAD_DIM
    row_block = pl.BlockSpec((leaf_rows, HEAD_DIM), lambda h: (0, h))
    key_block = pl.BlockSpec((key_count, HEAD_DIM), lambda h: (0, h))
    flops = 12 * leaf_rows * key_count * model_width
    io_bytes = 2 * (4 * leaf_rows + 2 * key_count) * model_width + 8 * key_count * model_width
    return pl.pallas_call(
        functools.partial(attention_kernel, scale=score_scale),
        grid=(heads,),
        in_specs=[
            pl.BlockSpec((1, key_count), lambda h: (0, 0)),
            row_block,
            row_block,
            key_block,
            key_block,
        ],
        out_specs=[row_block, row_block, key_block, key_block],
        out_shape=[
            jax.ShapeDtypeStruct((leaf_rows, model_width), jnp.bfloat16),
            jax.ShapeDtypeStruct((leaf_rows, model_width), jnp.bfloat16),
            jax.ShapeDtypeStruct((key_count, model_width), jnp.float32),
            jax.ShapeDtypeStruct((key_count, model_width), jnp.float32),
        ],
        cost_estimate=pl.CostEstimate(
            flops=flops, transcendentals=2 * leaf_rows * key_count * heads, bytes_accessed=io_bytes
        ),
    )(key_bias.reshape(1, key_count), query_rows, out_grad, all_keys, all_values)


def body(query_rows, key_rows, value_rows, out_grad):
    leaf_rows = query_rows.shape[0]
    model_width = query_rows.shape[1]
    seq_count = lax.axis_size("seq")
    levels = seq_count.bit_length() - 1
    position = lax.axis_index("seq")
    pool_ratio = leaf_rows // POOLED
    head_count = model_width // HEAD_DIM
    score_scale = HEAD_DIM ** (-0.5)
    paired = jnp.stack((key_rows, value_rows))
    sibling = partner_2(paired, "seq", 0)
    own_summary = jnp.mean(
        paired.reshape(2, POOLED, pool_ratio, model_width), axis=2, dtype=jnp.float32
    )
    sibling_summary = jnp.mean(
        sibling.reshape(2, POOLED, pool_ratio, model_width), axis=2, dtype=jnp.float32
    )
    summary = combine_halves(own_summary, sibling_summary, 0, position)
    far_parts = []
    for step_level in range(1, levels):
        partner = partner_2(summary.astype(jnp.bfloat16), "seq", step_level).astype(summary.dtype)
        far_parts.append(partner)
        if step_level + 1 < levels:
            summary = combine_halves(summary, partner, step_level, position)
    far_rows = jnp.concatenate(far_parts, axis=1).astype(jnp.bfloat16)
    all_keys = jnp.concatenate((key_rows, sibling[0], far_rows[0]), axis=0)
    all_values = jnp.concatenate((value_rows, sibling[1], far_rows[1]), axis=0)
    bias_parts = [jnp.zeros((2 * leaf_rows,), jnp.float32)]
    for step_level in range(1, levels):
        bias_parts.append(jnp.full((POOLED,), math.log(pool_ratio * 2**step_level), jnp.float32))
    key_bias = jnp.concatenate(bias_parts, axis=0)
    near_last = 2 * leaf_rows
    attended, query_grad, key_all, value_all = attention(
        query_rows, out_grad, all_keys, all_values, key_bias, score_scale
    )
    near_key = key_all[:near_last]
    far_key = key_all[near_last:]
    near_value = value_all[:near_last]
    far_value = value_all[near_last:]
    to_sibling = jnp.stack((near_key[leaf_rows:], near_value[leaf_rows:])).astype(jnp.bfloat16)
    from_sibling = partner_2(to_sibling, "seq", 0)
    own_terms = jnp.stack((near_key[:leaf_rows], near_value[:leaf_rows]))
    near_total = own_terms + from_sibling.astype(jnp.float32)
    far_grads = jnp.stack((far_key, far_value)).reshape(2, levels - 1, POOLED, model_width)
    summary_grad = jnp.zeros((2, POOLED, model_width), jnp.float32)
    for step_level in reversed(range(levels)):
        spread = jnp.broadcast_to(
            0.5 * summary_grad[:, :, None, :], (2, POOLED, 2, model_width)
        ).reshape(2, 2 * POOLED, model_width)
        upper_bit = position // 2**step_level % 2 == 1
        lower_half = spread[:, :POOLED]
        upper_half = spread[:, POOLED:]
        own_share = jnp.where(upper_bit, upper_half, lower_half)
        other_share = jnp.where(upper_bit, lower_half, upper_half)
        outgoing = other_share + far_grads[:, step_level - 1] if step_level >= 1 else other_share
        returned = partner_2(outgoing.astype(jnp.bfloat16), "seq", step_level).astype(
            outgoing.dtype
        )
        summary_grad = own_share + returned
    far_tokens = jnp.broadcast_to(
        summary_grad[:, :, None, :] / pool_ratio, (2, POOLED, pool_ratio, model_width)
    ).reshape(2, leaf_rows, model_width)
    grads_total = near_total + far_tokens
    return (
        attended,
        query_grad,
        grads_total[0].astype(jnp.bfloat16),
        grads_total[1].astype(jnp.bfloat16),
    )


def solution(mesh):
    return jax.shard_map(
        body,
        mesh=mesh,
        in_specs=(
            P(("batch", "seq"), None),
            P(("batch", "seq"), None),
            P(("batch", "seq"), None),
            P(("batch", "seq"), None),
        ),
        out_specs=(
            P(("batch", "seq"), None),
            P(("batch", "seq"), None),
            P(("batch", "seq"), None),
            P(("batch", "seq"), None),
        ),
        check_vma=False,
    )
```

```python
import functools
import math

import jax
import jax.numpy as jnp
from jax import lax
from jax.experimental import pallas as pl
from jax.sharding import PartitionSpec as P

HEAD_DIM = 128
POOLED = 128
CHUNKS = 4


def partner_2(block, axis, stride):
    count = lax.axis_size(axis)
    route = []
    for low in range(count):
        high = low | 1 << stride
        if high != low and high < count:
            route += [(low, high), (high, low)]
    return lax.ppermute(block, axis, route)


def attention_kernel(bias_ref, q_ref, do_ref, k_ref, v_ref, o_ref, dq_ref, dk_ref, dv_ref, *, scale):
    q = q_ref[...]
    do = do_ref[...]
    k = k_ref[...]
    v = v_ref[...]
    scores = (
        lax.dot_general(q, k, (((1,), (1,)), ((), ())), preferred_element_type=jnp.float32) * scale
        + bias_ref[...]
    )
    row_max = jnp.max(scores, axis=-1, keepdims=True)
    log_total = row_max + jnp.log(jnp.sum(jnp.exp(scores - row_max), axis=-1, keepdims=True))
    weights = jnp.exp(scores - log_total)
    weights_low = weights.astype(jnp.bfloat16)
    attended = jnp.dot(weights_low, v, preferred_element_type=jnp.float32).astype(jnp.bfloat16)
    o_ref[...] = attended
    row_dot = jnp.sum(
        do.astype(jnp.float32) * attended.astype(jnp.float32), axis=-1, keepdims=True
    )
    weight_grad = lax.dot_general(do, v, (((1,), (1,)), ((), ())), preferred_element_type=jnp.float32)
    score_grad = (weights * (weight_grad - row_dot)).astype(jnp.bfloat16)
    dq_ref[...] = (
        jnp.dot(score_grad, k, preferred_element_type=jnp.float32) * scale
    ).astype(jnp.bfloat16)
    dk_ref[...] = jnp.dot(score_grad.T, q, preferred_element_type=jnp.float32) * scale
    dv_ref[...] = jnp.dot(weights_low.T, do, preferred_element_type=jnp.float32)


def attention(query_rows, out_grad, keys, values, key_bias, score_scale, head_offset):
    leaf_rows = query_rows.shape[0]
    key_count, width = keys.shape
    heads = width // HEAD_DIM
    row_in = pl.BlockSpec((leaf_rows, HEAD_DIM), lambda h: (0, h + head_offset))
    row_out = pl.BlockSpec((leaf_rows, HEAD_DIM), lambda h: (0, h))
    key_block = pl.BlockSpec((key_count, HEAD_DIM), lambda h: (0, h))
    flops = 12 * leaf_rows * key_count * width
    io_bytes = 2 * (4 * leaf_rows + 2 * key_count) * width + 8 * key_count * width
    return pl.pallas_call(
        functools.partial(attention_kernel, scale=score_scale),
        grid=(heads,),
        in_specs=[
            pl.BlockSpec((1, key_count), lambda h: (0, 0)),
            row_in,
            row_in,
            key_block,
            key_block,
        ],
        out_specs=[row_out, row_out, key_block, key_block],
        out_shape=[
            jax.ShapeDtypeStruct((leaf_rows, width), jnp.bfloat16),
            jax.ShapeDtypeStruct((leaf_rows, width), jnp.bfloat16),
            jax.ShapeDtypeStruct((key_count, width), jnp.float32),
            jax.ShapeDtypeStruct((key_count, width), jnp.float32),
        ],
        cost_estimate=pl.CostEstimate(
            flops=flops, transcendentals=2 * leaf_rows * key_count * heads, bytes_accessed=io_bytes
        ),
    )(key_bias.reshape(1, key_count), query_rows, out_grad, keys, values)


def placed_pool(rows_in, upper):
    run = rows_in // (POOLED // 2)
    out_row = lax.broadcasted_iota(jnp.int32, (POOLED, rows_in), 0)
    in_row = lax.broadcasted_iota(jnp.int32, (POOLED, rows_in), 1)
    offset = upper * (POOLED // 2)
    return jnp.where(out_row - offset == in_row // run, 1.0 / run, 0.0).astype(jnp.float32)


def apply(matrix, rows):
    return jnp.dot(
        matrix, rows.astype(jnp.float32), precision=lax.Precision.HIGHEST,
        preferred_element_type=jnp.float32,
    )


def body(query_rows, key_rows, value_rows, out_grad):
    leaf_rows, model_width = query_rows.shape
    seq_count = lax.axis_size("seq")
    levels = seq_count.bit_length() - 1
    position = lax.axis_index("seq")
    pool_ratio = leaf_rows // POOLED
    score_scale = HEAD_DIM ** (-0.5)
    chunk_width = model_width // CHUNKS
    bias_parts = [jnp.zeros((2 * leaf_rows,), jnp.float32)]
    for step_level in range(1, levels):
        bias_parts.append(jnp.full((POOLED,), math.log(pool_ratio * 2**step_level), jnp.float32))
    key_bias = jnp.concatenate(bias_parts, axis=0)
    bits = [position // 2**step_level % 2 for step_level in range(levels)]
    mine = [placed_pool(leaf_rows if s == 0 else POOLED, bits[s]) for s in range(levels)]
    other = [placed_pool(leaf_rows if s == 0 else POOLED, 1 - bits[s]) for s in range(levels)]
    far_first = 2 * leaf_rows
    pieces = [[], [], [], []]
    for chunk in range(CHUNKS):
        columns = slice(chunk * chunk_width, (chunk + 1) * chunk_width)
        own = (key_rows[:, columns], value_rows[:, columns])
        sibling = partner_2(own, "seq", 0)
        summary = [apply(mine[0], own[i]) + apply(other[0], sibling[i]) for i in range(2)]
        far = []
        for step_level in range(1, levels):
            partner = partner_2(tuple(x.astype(jnp.bfloat16) for x in summary), "seq", step_level)
            far.append(partner)
            if step_level + 1 < levels:
                summary = [
                    apply(mine[step_level], summary[i]) + apply(other[step_level], partner[i])
                    for i in range(2)
                ]
        keys = jnp.concatenate([own[0], sibling[0]] + [f[0] for f in far], axis=0)
        values = jnp.concatenate([own[1], sibling[1]] + [f[1] for f in far], axis=0)
        attended, query_grad, key_all, value_all = attention(
            query_rows, out_grad, keys, values, key_bias, score_scale,
            chunk * (chunk_width // HEAD_DIM),
        )
        terms = (key_all, value_all)
        grad = None
        for step_level in reversed(range(1, levels)):
            first = far_first + (step_level - 1) * POOLED
            outgoing = [terms[i][first:first + POOLED] for i in range(2)]
            if grad is not None:
                outgoing = [outgoing[i] + apply(other[step_level].T, grad[i]) for i in range(2)]
            returned = partner_2(tuple(x.astype(jnp.bfloat16) for x in outgoing), "seq", step_level)
            if grad is None:
                grad = [returned[i].astype(jnp.float32) for i in range(2)]
            else:
                grad = [apply(mine[step_level].T, grad[i]) + returned[i] for i in range(2)]
        to_sibling = [terms[i][leaf_rows:far_first] for i in range(2)]
        own_total = [terms[i][:leaf_rows] for i in range(2)]
        if grad is not None:
            to_sibling = [to_sibling[i] + apply(other[0].T, grad[i]) for i in range(2)]
            own_total = [own_total[i] + apply(mine[0].T, grad[i]) for i in range(2)]
        from_sibling = partner_2(tuple(x.astype(jnp.bfloat16) for x in to_sibling), "seq", 0)
        totals = [own_total[i] + from_sibling[i].astype(jnp.float32) for i in range(2)]
        for slot, piece in enumerate((attended, query_grad, totals[0], totals[1])):
            pieces[slot].append(piece)
    return tuple(jnp.concatenate(p, axis=1).astype(jnp.bfloat16) for p in pieces)


def solution(mesh):
    spec = P(("batch", "seq"), None)
    return jax.shard_map(
        body, mesh=mesh, in_specs=(spec, spec, spec, spec), out_specs=(spec, spec, spec, spec),
        check_vma=False,
    )
```

```python
import functools
import math

import jax
import jax.numpy as jnp
from jax import lax
from jax.experimental import pallas as pl
from jax.sharding import PartitionSpec as P

HEAD_DIM = 128
POOLED = 128
CHUNKS = 4


def partner_2(block, axis, stride):
    count = lax.axis_size(axis)
    route = []
    for low in range(count):
        high = low | 1 << stride
        if high != low and high < count:
            route += [(low, high), (high, low)]
    return lax.ppermute(block, axis, route)


def attention_kernel(bias_ref, q_ref, do_ref, *refs, scale, parts):
    part_refs = refs[:parts]
    o_ref, dq_ref = refs[parts:parts + 2]
    grad_refs = refs[parts + 2:]
    q = q_ref[...]
    do = do_ref[...]
    k = jnp.concatenate([r[0] for r in part_refs], axis=0)
    v = jnp.concatenate([r[1] for r in part_refs], axis=0)
    scores = (
        lax.dot_general(q, k, (((1,), (1,)), ((), ())), preferred_element_type=jnp.float32) * scale
        + bias_ref[...]
    )
    row_max = jnp.max(scores, axis=-1, keepdims=True)
    log_total = row_max + jnp.log(jnp.sum(jnp.exp(scores - row_max), axis=-1, keepdims=True))
    weights = jnp.exp(scores - log_total)
    weights_low = weights.astype(jnp.bfloat16)
    attended = jnp.dot(weights_low, v, preferred_element_type=jnp.float32).astype(jnp.bfloat16)
    o_ref[...] = attended
    row_dot = jnp.sum(
        do.astype(jnp.float32) * attended.astype(jnp.float32), axis=-1, keepdims=True
    )
    weight_grad = lax.dot_general(do, v, (((1,), (1,)), ((), ())), preferred_element_type=jnp.float32)
    score_grad = (weights * (weight_grad - row_dot)).astype(jnp.bfloat16)
    dq_ref[...] = (
        jnp.dot(score_grad, k, preferred_element_type=jnp.float32) * scale
    ).astype(jnp.bfloat16)
    dk = jnp.dot(score_grad.T, q, preferred_element_type=jnp.float32) * scale
    dv = jnp.dot(weights_low.T, do, preferred_element_type=jnp.float32)
    first = 0
    for r in grad_refs:
        rows = r.shape[1]
        r[0] = dk[first:first + rows]
        r[1] = dv[first:first + rows]
        first += rows


def attention(query_rows, out_grad, parts, key_bias, score_scale, head_offset):
    leaf_rows = query_rows.shape[0]
    width = parts[0].shape[2]
    key_count = sum(p.shape[1] for p in parts)
    heads = width // HEAD_DIM
    row_in = pl.BlockSpec((leaf_rows, HEAD_DIM), lambda h: (0, h + head_offset))
    row_out = pl.BlockSpec((leaf_rows, HEAD_DIM), lambda h: (0, h))
    part_specs = [pl.BlockSpec((2, p.shape[1], HEAD_DIM), lambda h: (0, 0, h)) for p in parts]
    flops = 12 * leaf_rows * key_count * width
    io_bytes = 2 * (4 * leaf_rows + 2 * key_count) * width + 8 * key_count * width
    return pl.pallas_call(
        functools.partial(attention_kernel, scale=score_scale, parts=len(parts)),
        grid=(heads,),
        in_specs=[pl.BlockSpec((1, key_count), lambda h: (0, 0)), row_in, row_in] + part_specs,
        out_specs=[row_out, row_out] + part_specs,
        out_shape=[
            jax.ShapeDtypeStruct((leaf_rows, width), jnp.bfloat16),
            jax.ShapeDtypeStruct((leaf_rows, width), jnp.bfloat16),
        ] + [jax.ShapeDtypeStruct(p.shape, jnp.float32) for p in parts],
        cost_estimate=pl.CostEstimate(
            flops=flops, transcendentals=2 * leaf_rows * key_count * heads, bytes_accessed=io_bytes
        ),
    )(key_bias.reshape(1, key_count), query_rows, out_grad, *parts)


def placed_pool(rows_in, upper):
    run = rows_in // (POOLED // 2)
    out_row = lax.broadcasted_iota(jnp.int32, (POOLED, rows_in), 0)
    in_row = lax.broadcasted_iota(jnp.int32, (POOLED, rows_in), 1)
    offset = upper * (POOLED // 2)
    return jnp.where(out_row - offset == in_row // run, 1.0 / run, 0.0).astype(jnp.float32)


def apply(matrix, rows):
    return jnp.einsum(
        "pr,krw->kpw", matrix, rows.astype(jnp.float32), precision=lax.Precision.HIGHEST,
        preferred_element_type=jnp.float32,
    )


def body(query_rows, key_rows, value_rows, out_grad):
    leaf_rows, model_width = query_rows.shape
    seq_count = lax.axis_size("seq")
    levels = seq_count.bit_length() - 1
    position = lax.axis_index("seq")
    pool_ratio = leaf_rows // POOLED
    score_scale = HEAD_DIM ** (-0.5)
    chunk_width = model_width // CHUNKS
    bias_parts = [jnp.zeros((2 * leaf_rows,), jnp.float32)]
    for step_level in range(1, levels):
        bias_parts.append(jnp.full((POOLED,), math.log(pool_ratio * 2**step_level), jnp.float32))
    key_bias = jnp.concatenate(bias_parts, axis=0)
    bits = [position // 2**step_level % 2 for step_level in range(levels)]
    mine = [placed_pool(leaf_rows if s == 0 else POOLED, bits[s]) for s in range(levels)]
    other = [placed_pool(leaf_rows if s == 0 else POOLED, 1 - bits[s]) for s in range(levels)]
    pieces = [[], [], [], []]
    for chunk in range(CHUNKS):
        columns = slice(chunk * chunk_width, (chunk + 1) * chunk_width)
        own = jnp.stack((key_rows[:, columns], value_rows[:, columns]))
        sibling = partner_2(own, "seq", 0)
        summary = apply(mine[0], own) + apply(other[0], sibling)
        far = []
        for step_level in range(1, levels):
            partner = partner_2(summary.astype(jnp.bfloat16), "seq", step_level)
            far.append(partner)
            if step_level + 1 < levels:
                summary = apply(mine[step_level], summary) + apply(other[step_level], partner)
        outs = attention(
            query_rows, out_grad, [own, sibling] + far, key_bias, score_scale,
            chunk * (chunk_width // HEAD_DIM),
        )
        attended, query_grad, terms = outs[0], outs[1], outs[2:]
        grad = None
        for step_level in reversed(range(1, levels)):
            outgoing = terms[1 + step_level]
            if grad is not None:
                outgoing = outgoing + apply(other[step_level].T, grad)
            returned = partner_2(outgoing.astype(jnp.bfloat16), "seq", step_level)
            if grad is None:
                grad = returned.astype(jnp.float32)
            else:
                grad = apply(mine[step_level].T, grad) + returned
        to_sibling = terms[1]
        own_total = terms[0]
        if grad is not None:
            to_sibling = to_sibling + apply(other[0].T, grad)
            own_total = own_total + apply(mine[0].T, grad)
        from_sibling = partner_2(to_sibling.astype(jnp.bfloat16), "seq", 0)
        totals = own_total + from_sibling.astype(jnp.float32)
        for slot, piece in enumerate((attended, query_grad, totals[0], totals[1])):
            pieces[slot].append(piece)
    return tuple(jnp.concatenate(p, axis=1).astype(jnp.bfloat16) for p in pieces)


def solution(mesh):
    spec = P(("batch", "seq"), None)
    return jax.shard_map(
        body, mesh=mesh, in_specs=(spec, spec, spec, spec), out_specs=(spec, spec, spec, spec),
        check_vma=False,
    )
```

```python
import functools
import math

import jax
import jax.numpy as jnp
from jax import lax
from jax.experimental import pallas as pl
from jax.sharding import PartitionSpec as P

HEAD_DIM = 128
POOLED = 128
CHUNKS = 4


def partner_2(block, axis, stride):
    count = lax.axis_size(axis)
    route = []
    for low in range(count):
        high = low | 1 << stride
        if high != low and high < count:
            route += [(low, high), (high, low)]
    return lax.ppermute(block, axis, route)


def attention_kernel(bias_ref, q_ref, do_ref, *refs, scale, parts):
    part_refs = refs[:parts]
    o_ref, dq_ref = refs[parts:parts + 2]
    grad_refs = refs[parts + 2:]
    q = q_ref[...]
    do = do_ref[...]
    k = jnp.concatenate([r[0] for r in part_refs], axis=0)
    v = jnp.concatenate([r[1] for r in part_refs], axis=0)
    scores = (
        lax.dot_general(q, k, (((1,), (1,)), ((), ())), preferred_element_type=jnp.float32) * scale
        + bias_ref[...]
    )
    row_max = jnp.max(scores, axis=-1, keepdims=True)
    log_total = row_max + jnp.log(jnp.sum(jnp.exp(scores - row_max), axis=-1, keepdims=True))
    weights = jnp.exp(scores - log_total)
    weights_low = weights.astype(jnp.bfloat16)
    attended = jnp.dot(weights_low, v, preferred_element_type=jnp.float32).astype(jnp.bfloat16)
    o_ref[...] = attended
    row_dot = jnp.sum(
        do.astype(jnp.float32) * attended.astype(jnp.float32), axis=-1, keepdims=True
    )
    weight_grad = lax.dot_general(do, v, (((1,), (1,)), ((), ())), preferred_element_type=jnp.float32)
    score_grad = (weights * (weight_grad - row_dot)).astype(jnp.bfloat16)
    dq_ref[...] = (
        jnp.dot(score_grad, k, preferred_element_type=jnp.float32) * scale
    ).astype(jnp.bfloat16)
    dk = jnp.dot(score_grad.T, q, preferred_element_type=jnp.float32) * scale
    dv = jnp.dot(weights_low.T, do, preferred_element_type=jnp.float32)
    first = 0
    for r in grad_refs:
        rows = r.shape[1]
        r[0] = dk[first:first + rows]
        r[1] = dv[first:first + rows]
        first += rows


def attention(query_rows, out_grad, parts, key_bias, score_scale, head_offset):
    leaf_rows = query_rows.shape[0]
    width = parts[0].shape[2]
    key_count = sum(p.shape[1] for p in parts)
    heads = width // HEAD_DIM
    row_in = pl.BlockSpec((leaf_rows, HEAD_DIM), lambda h: (0, h + head_offset))
    row_out = pl.BlockSpec((leaf_rows, HEAD_DIM), lambda h: (0, h))
    part_specs = [pl.BlockSpec((2, p.shape[1], HEAD_DIM), lambda h: (0, 0, h)) for p in parts]
    flops = 12 * leaf_rows * key_count * width
    io_bytes = 2 * (4 * leaf_rows + 2 * key_count) * width + 8 * key_count * width
    return pl.pallas_call(
        functools.partial(attention_kernel, scale=score_scale, parts=len(parts)),
        grid=(heads,),
        in_specs=[pl.BlockSpec((1, key_count), lambda h: (0, 0)), row_in, row_in] + part_specs,
        out_specs=[row_out, row_out] + part_specs,
        out_shape=[
            jax.ShapeDtypeStruct((leaf_rows, width), jnp.bfloat16),
            jax.ShapeDtypeStruct((leaf_rows, width), jnp.bfloat16),
        ] + [jax.ShapeDtypeStruct(p.shape, jnp.float32) for p in parts],
        cost_estimate=pl.CostEstimate(
            flops=flops, transcendentals=2 * leaf_rows * key_count * heads, bytes_accessed=io_bytes
        ),
    )(key_bias.reshape(1, key_count), query_rows, out_grad, *parts)


def after(value, earlier):
    if earlier is None:
        return value
    return lax.optimization_barrier((value, earlier))[0]


def placed_pool(rows_in, upper):
    run = rows_in // (POOLED // 2)
    out_row = lax.broadcasted_iota(jnp.int32, (POOLED, rows_in), 0)
    in_row = lax.broadcasted_iota(jnp.int32, (POOLED, rows_in), 1)
    offset = upper * (POOLED // 2)
    return jnp.where(out_row - offset == in_row // run, 1.0 / run, 0.0).astype(jnp.float32)


def apply(matrix, rows):
    return jnp.einsum(
        "pr,krw->kpw", matrix, rows.astype(jnp.float32), precision=lax.Precision.HIGHEST,
        preferred_element_type=jnp.float32,
    )


def body(query_rows, key_rows, value_rows, out_grad):
    leaf_rows, model_width = query_rows.shape
    seq_count = lax.axis_size("seq")
    levels = seq_count.bit_length() - 1
    position = lax.axis_index("seq")
    pool_ratio = leaf_rows // POOLED
    score_scale = HEAD_DIM ** (-0.5)
    chunk_width = model_width // CHUNKS
    bias_parts = [jnp.zeros((2 * leaf_rows,), jnp.float32)]
    for step_level in range(1, levels):
        bias_parts.append(jnp.full((POOLED,), math.log(pool_ratio * 2**step_level), jnp.float32))
    key_bias = jnp.concatenate(bias_parts, axis=0)
    bits = [position // 2**step_level % 2 for step_level in range(levels)]
    mine = [placed_pool(leaf_rows if s == 0 else POOLED, bits[s]) for s in range(levels)]
    other = [placed_pool(leaf_rows if s == 0 else POOLED, 1 - bits[s]) for s in range(levels)]
    pieces = [[], [], [], []]
    last = {}
    for chunk in range(CHUNKS):
        columns = slice(chunk * chunk_width, (chunk + 1) * chunk_width)
        own = jnp.stack((key_rows[:, columns], value_rows[:, columns]))
        sibling = partner_2(own, "seq", 0)
        summary = apply(mine[0], own) + apply(other[0], sibling)
        far = []
        for step_level in range(1, levels):
            send = after(summary.astype(jnp.bfloat16), last.get(("fwd", step_level)))
            partner = partner_2(send, "seq", step_level)
            last[("fwd", step_level)] = partner
            far.append(partner)
            if step_level + 1 < levels:
                summary = apply(mine[step_level], summary) + apply(other[step_level], partner)
        outs = attention(
            query_rows, out_grad, [own, sibling] + far, key_bias, score_scale,
            chunk * (chunk_width // HEAD_DIM),
        )
        attended, query_grad, terms = outs[0], outs[1], outs[2:]
        grad = None
        for step_level in reversed(range(1, levels)):
            outgoing = terms[1 + step_level]
            if grad is not None:
                outgoing = outgoing + apply(other[step_level].T, grad)
            send = after(outgoing.astype(jnp.bfloat16), last.get(("bwd", step_level)))
            returned = partner_2(send, "seq", step_level)
            last[("bwd", step_level)] = returned
            if grad is None:
                grad = returned.astype(jnp.float32)
            else:
                grad = apply(mine[step_level].T, grad) + returned
        to_sibling = terms[1]
        own_total = terms[0]
        if grad is not None:
            to_sibling = to_sibling + apply(other[0].T, grad)
            own_total = own_total + apply(mine[0].T, grad)
        send = after(to_sibling.astype(jnp.bfloat16), last.get(("bwd", 0)))
        from_sibling = partner_2(send, "seq", 0)
        last[("bwd", 0)] = from_sibling
        totals = own_total + from_sibling.astype(jnp.float32)
        for slot, piece in enumerate((attended, query_grad, totals[0], totals[1])):
            pieces[slot].append(piece)
    return tuple(jnp.concatenate(p, axis=1).astype(jnp.bfloat16) for p in pieces)


def solution(mesh):
    spec = P(("batch", "seq"), None)
    return jax.shard_map(
        body, mesh=mesh, in_specs=(spec, spec, spec, spec), out_specs=(spec, spec, spec, spec),
        check_vma=False,
    )
```

```python
import functools
import math

import jax
import jax.numpy as jnp
from jax import lax
from jax.experimental import pallas as pl
from jax.sharding import PartitionSpec as P

HEAD_DIM = 128
POOLED = 128
CHUNKS = 4


def partner_2(block, axis, stride):
    count = lax.axis_size(axis)
    route = []
    for low in range(count):
        high = low | 1 << stride
        if high != low and high < count:
            route += [(low, high), (high, low)]
    return lax.ppermute(block, axis, route)


def attention_kernel(bias_ref, q_ref, do_ref, *refs, scale, parts):
    part_refs = refs[:parts]
    o_ref, dq_ref = refs[parts:parts + 2]
    grad_refs = refs[parts + 2:]
    q = q_ref[...]
    do = do_ref[...]
    k = jnp.concatenate([r[0] for r in part_refs], axis=0)
    v = jnp.concatenate([r[1] for r in part_refs], axis=0)
    scores = (
        lax.dot_general(q, k, (((1,), (1,)), ((), ())), preferred_element_type=jnp.float32) * scale
        + bias_ref[...]
    )
    row_max = jnp.max(scores, axis=-1, keepdims=True)
    log_total = row_max + jnp.log(jnp.sum(jnp.exp(scores - row_max), axis=-1, keepdims=True))
    weights = jnp.exp(scores - log_total)
    weights_low = weights.astype(jnp.bfloat16)
    attended = jnp.dot(weights_low, v, preferred_element_type=jnp.float32).astype(jnp.bfloat16)
    o_ref[...] = attended
    row_dot = jnp.sum(
        do.astype(jnp.float32) * attended.astype(jnp.float32), axis=-1, keepdims=True
    )
    weight_grad = lax.dot_general(do, v, (((1,), (1,)), ((), ())), preferred_element_type=jnp.float32)
    score_grad = (weights * (weight_grad - row_dot)).astype(jnp.bfloat16)
    dq_ref[...] = (
        jnp.dot(score_grad, k, preferred_element_type=jnp.float32) * scale
    ).astype(jnp.bfloat16)
    dk = jnp.dot(score_grad.T, q, preferred_element_type=jnp.float32) * scale
    dv = jnp.dot(weights_low.T, do, preferred_element_type=jnp.float32)
    first = 0
    for r in grad_refs:
        rows = r.shape[1]
        r[0] = dk[first:first + rows]
        r[1] = dv[first:first + rows]
        first += rows


def attention(query_rows, out_grad, parts, key_bias, score_scale, head_offset):
    leaf_rows = query_rows.shape[0]
    width = parts[0].shape[2]
    key_count = sum(p.shape[1] for p in parts)
    heads = width // HEAD_DIM
    row_in = pl.BlockSpec((leaf_rows, HEAD_DIM), lambda h: (0, h + head_offset))
    row_out = pl.BlockSpec((leaf_rows, HEAD_DIM), lambda h: (0, h))
    part_specs = [pl.BlockSpec((2, p.shape[1], HEAD_DIM), lambda h: (0, 0, h)) for p in parts]
    flops = 12 * leaf_rows * key_count * width
    io_bytes = 2 * (4 * leaf_rows + 2 * key_count) * width + 8 * key_count * width
    return pl.pallas_call(
        functools.partial(attention_kernel, scale=score_scale, parts=len(parts)),
        grid=(heads,),
        in_specs=[pl.BlockSpec((1, key_count), lambda h: (0, 0)), row_in, row_in] + part_specs,
        out_specs=[row_out, row_out] + part_specs,
        out_shape=[
            jax.ShapeDtypeStruct((leaf_rows, width), jnp.bfloat16),
            jax.ShapeDtypeStruct((leaf_rows, width), jnp.bfloat16),
        ] + [jax.ShapeDtypeStruct(p.shape, jnp.float32) for p in parts],
        cost_estimate=pl.CostEstimate(
            flops=flops, transcendentals=2 * leaf_rows * key_count * heads, bytes_accessed=io_bytes
        ),
    )(key_bias.reshape(1, key_count), query_rows, out_grad, *parts)


def inner_pairs(count, level):
    mask = (1 << level) | (1 << (level - 1))
    return [(b, b ^ mask) for b in range(count) if (b >> level & 1) != (b >> (level - 1) & 1)]


def outer_pairs(count, level):
    return [(b, b ^ (1 << (level - 1))) for b in range(count) if (b >> level & 1) != (b >> (level - 1) & 1)]


def placed_pool(rows_in, upper):
    run = rows_in // (POOLED // 2)
    out_row = lax.broadcasted_iota(jnp.int32, (POOLED, rows_in), 0)
    in_row = lax.broadcasted_iota(jnp.int32, (POOLED, rows_in), 1)
    offset = upper * (POOLED // 2)
    return jnp.where(out_row - offset == in_row // run, 1.0 / run, 0.0).astype(jnp.float32)


def apply(matrix, rows):
    return jnp.einsum(
        "pr,krw->kpw", matrix, rows.astype(jnp.float32), precision=lax.Precision.HIGHEST,
        preferred_element_type=jnp.float32,
    )


def body(query_rows, key_rows, value_rows, out_grad):
    leaf_rows, model_width = query_rows.shape
    seq_count = lax.axis_size("seq")
    levels = seq_count.bit_length() - 1
    position = lax.axis_index("seq")
    pool_ratio = leaf_rows // POOLED
    score_scale = HEAD_DIM ** (-0.5)
    chunk_width = model_width // CHUNKS
    bias_parts = [jnp.zeros((2 * leaf_rows,), jnp.float32)]
    for step_level in range(1, levels):
        bias_parts.append(jnp.full((POOLED,), math.log(pool_ratio * 2**step_level), jnp.float32))
    key_bias = jnp.concatenate(bias_parts, axis=0)
    bits = [position // 2**step_level % 2 for step_level in range(levels)]
    inner = [None] + [bits[s] != bits[s - 1] for s in range(1, levels)]
    mine = [placed_pool(leaf_rows if s == 0 else POOLED, bits[s]) for s in range(levels)]
    other = [placed_pool(leaf_rows if s == 0 else POOLED, 1 - bits[s]) for s in range(levels)]
    pieces = [[], [], [], []]
    for chunk in range(CHUNKS):
        columns = slice(chunk * chunk_width, (chunk + 1) * chunk_width)
        own = jnp.stack((key_rows[:, columns], value_rows[:, columns]))
        sibling = partner_2(own, "seq", 0)
        summary = apply(mine[0], own) + apply(other[0], sibling)
        far = []
        for step_level in range(1, levels):
            if step_level == 1:
                partner = partner_2(summary.astype(jnp.bfloat16), "seq", step_level)
            else:
                crossed = lax.ppermute(summary.astype(jnp.bfloat16), "seq", inner_pairs(seq_count, step_level))
                passed = lax.ppermute(crossed, "seq", outer_pairs(seq_count, step_level))
                partner = jnp.where(inner[step_level], crossed, passed)
            far.append(partner)
            if step_level + 1 < levels:
                summary = apply(mine[step_level], summary) + apply(other[step_level], partner)
        outs = attention(
            query_rows, out_grad, [own, sibling] + far, key_bias, score_scale,
            chunk * (chunk_width // HEAD_DIM),
        )
        attended, query_grad, terms = outs[0], outs[1], outs[2:]
        grad = None
        for step_level in reversed(range(1, levels)):
            outgoing = terms[1 + step_level]
            if grad is not None:
                outgoing = outgoing + apply(other[step_level].T, grad)
            if step_level == 1:
                returned = partner_2(outgoing.astype(jnp.bfloat16), "seq", step_level)
            else:
                back = [(t, s) for s, t in outer_pairs(seq_count, step_level)]
                gathered = lax.ppermute(outgoing.astype(jnp.bfloat16), "seq", back)
                total = outgoing + gathered.astype(jnp.float32)
                returned = lax.ppermute(total.astype(jnp.bfloat16), "seq", inner_pairs(seq_count, step_level))
            if grad is None:
                grad = returned.astype(jnp.float32)
            else:
                grad = apply(mine[step_level].T, grad) + returned
        to_sibling = terms[1]
        own_total = terms[0]
        if grad is not None:
            to_sibling = to_sibling + apply(other[0].T, grad)
            own_total = own_total + apply(mine[0].T, grad)
        from_sibling = partner_2(to_sibling.astype(jnp.bfloat16), "seq", 0)
        totals = own_total + from_sibling.astype(jnp.float32)
        for slot, piece in enumerate((attended, query_grad, totals[0], totals[1])):
            pieces[slot].append(piece)
    return tuple(jnp.concatenate(p, axis=1).astype(jnp.bfloat16) for p in pieces)


def solution(mesh):
    spec = P(("batch", "seq"), None)
    return jax.shard_map(
        body, mesh=mesh, in_specs=(spec, spec, spec, spec), out_specs=(spec, spec, spec, spec),
        check_vma=False,
    )
```

```python
import functools
import math

import jax
import jax.numpy as jnp
from jax import lax
from jax.experimental import pallas as pl
from jax.sharding import PartitionSpec as P

HEAD_DIM = 128
POOLED = 128
CHUNKS = 4


def partner_2(block, axis, stride):
    count = lax.axis_size(axis)
    route = []
    for low in range(count):
        high = low | 1 << stride
        if high != low and high < count:
            route += [(low, high), (high, low)]
    return lax.ppermute(block, axis, route)


def attention_kernel(bias_ref, q_ref, do_ref, *refs, scale, parts):
    part_refs = refs[:parts]
    o_ref, dq_ref = refs[parts:parts + 2]
    grad_refs = refs[parts + 2:]
    q = q_ref[...]
    do = do_ref[...]
    k = jnp.concatenate([r[0] for r in part_refs], axis=0)
    v = jnp.concatenate([r[1] for r in part_refs], axis=0)
    scores = (
        lax.dot_general(q, k, (((1,), (1,)), ((), ())), preferred_element_type=jnp.float32) * scale
        + bias_ref[...]
    )
    row_max = jnp.max(scores, axis=-1, keepdims=True)
    log_total = row_max + jnp.log(jnp.sum(jnp.exp(scores - row_max), axis=-1, keepdims=True))
    weights = jnp.exp(scores - log_total)
    weights_low = weights.astype(jnp.bfloat16)
    attended = jnp.dot(weights_low, v, preferred_element_type=jnp.float32).astype(jnp.bfloat16)
    o_ref[...] = attended
    row_dot = jnp.sum(
        do.astype(jnp.float32) * attended.astype(jnp.float32), axis=-1, keepdims=True
    )
    weight_grad = lax.dot_general(do, v, (((1,), (1,)), ((), ())), preferred_element_type=jnp.float32)
    score_grad = (weights * (weight_grad - row_dot)).astype(jnp.bfloat16)
    dq_ref[...] = (
        jnp.dot(score_grad, k, preferred_element_type=jnp.float32) * scale
    ).astype(jnp.bfloat16)
    dk = jnp.dot(score_grad.T, q, preferred_element_type=jnp.float32) * scale
    dv = jnp.dot(weights_low.T, do, preferred_element_type=jnp.float32)
    first = 0
    for r in grad_refs:
        rows = r.shape[1]
        r[0] = dk[first:first + rows]
        r[1] = dv[first:first + rows]
        first += rows


def attention(query_rows, out_grad, parts, key_bias, score_scale, head_offset):
    leaf_rows = query_rows.shape[0]
    width = parts[0].shape[2]
    key_count = sum(p.shape[1] for p in parts)
    heads = width // HEAD_DIM
    row_in = pl.BlockSpec((leaf_rows, HEAD_DIM), lambda h: (0, h + head_offset))
    row_out = pl.BlockSpec((leaf_rows, HEAD_DIM), lambda h: (0, h))
    part_specs = [pl.BlockSpec((2, p.shape[1], HEAD_DIM), lambda h: (0, 0, h)) for p in parts]
    flops = 12 * leaf_rows * key_count * width
    io_bytes = 2 * (4 * leaf_rows + 2 * key_count) * width + 8 * key_count * width
    return pl.pallas_call(
        functools.partial(attention_kernel, scale=score_scale, parts=len(parts)),
        grid=(heads,),
        in_specs=[pl.BlockSpec((1, key_count), lambda h: (0, 0)), row_in, row_in] + part_specs,
        out_specs=[row_out, row_out] + part_specs,
        out_shape=[
            jax.ShapeDtypeStruct((leaf_rows, width), jnp.bfloat16),
            jax.ShapeDtypeStruct((leaf_rows, width), jnp.bfloat16),
        ] + [jax.ShapeDtypeStruct(p.shape, jnp.float32) for p in parts],
        cost_estimate=pl.CostEstimate(
            flops=flops, transcendentals=2 * leaf_rows * key_count * heads, bytes_accessed=io_bytes
        ),
    )(key_bias.reshape(1, key_count), query_rows, out_grad, *parts)


def after(value, earlier):
    return lax.optimization_barrier((value, earlier))[0]


def placed_pool(rows_in, upper):
    run = rows_in // (POOLED // 2)
    out_row = lax.broadcasted_iota(jnp.int32, (POOLED, rows_in), 0)
    in_row = lax.broadcasted_iota(jnp.int32, (POOLED, rows_in), 1)
    offset = upper * (POOLED // 2)
    return jnp.where(out_row - offset == in_row // run, 1.0 / run, 0.0).astype(jnp.float32)


def apply(matrix, rows):
    return jnp.einsum(
        "pr,krw->kpw", matrix, rows.astype(jnp.float32), precision=lax.Precision.HIGHEST,
        preferred_element_type=jnp.float32,
    )


def body(query_rows, key_rows, value_rows, out_grad):
    leaf_rows, model_width = query_rows.shape
    seq_count = lax.axis_size("seq")
    levels = seq_count.bit_length() - 1
    position = lax.axis_index("seq")
    pool_ratio = leaf_rows // POOLED
    score_scale = HEAD_DIM ** (-0.5)
    chunk_width = model_width // CHUNKS
    bias_parts = [jnp.zeros((2 * leaf_rows,), jnp.float32)]
    for step_level in range(1, levels):
        bias_parts.append(jnp.full((POOLED,), math.log(pool_ratio * 2**step_level), jnp.float32))
    key_bias = jnp.concatenate(bias_parts, axis=0)
    bits = [position // 2**step_level % 2 for step_level in range(levels)]
    mine = [placed_pool(leaf_rows if s == 0 else POOLED, bits[s]) for s in range(levels)]
    other = [placed_pool(leaf_rows if s == 0 else POOLED, 1 - bits[s]) for s in range(levels)]
    pool_own = placed_pool(leaf_rows, 0)[: POOLED // 2]
    own_pooled = apply(pool_own, jnp.stack((key_rows, value_rows)))
    sibling_pooled = partner_2(own_pooled.astype(jnp.bfloat16), "seq", 0)
    place_mine = placed_pool(POOLED // 2, bits[0])
    place_other = placed_pool(POOLED // 2, 1 - bits[0])
    pieces = [[], [], [], []]
    for chunk in range(CHUNKS):
        columns = slice(chunk * chunk_width, (chunk + 1) * chunk_width)
        own = jnp.stack((key_rows[:, columns], value_rows[:, columns]))
        sibling = partner_2(after(own, sibling_pooled), "seq", 0)
        summary = apply(place_mine, own_pooled[:, :, columns]) + apply(
            place_other, sibling_pooled[:, :, columns]
        )
        far = []
        for step_level in range(1, levels):
            partner = partner_2(summary.astype(jnp.bfloat16), "seq", step_level)
            far.append(partner)
            if step_level + 1 < levels:
                summary = apply(mine[step_level], summary) + apply(other[step_level], partner)
        outs = attention(
            query_rows, out_grad, [own, sibling] + far, key_bias, score_scale,
            chunk * (chunk_width // HEAD_DIM),
        )
        attended, query_grad, terms = outs[0], outs[1], outs[2:]
        grad = None
        for step_level in reversed(range(1, levels)):
            outgoing = terms[1 + step_level]
            if grad is not None:
                outgoing = outgoing + apply(other[step_level].T, grad)
            returned = partner_2(outgoing.astype(jnp.bfloat16), "seq", step_level)
            if grad is None:
                grad = returned.astype(jnp.float32)
            else:
                grad = apply(mine[step_level].T, grad) + returned
        to_sibling = terms[1]
        own_total = terms[0]
        if grad is not None:
            to_sibling = to_sibling + apply(other[0].T, grad)
            own_total = own_total + apply(mine[0].T, grad)
        from_sibling = partner_2(to_sibling.astype(jnp.bfloat16), "seq", 0)
        totals = own_total + from_sibling.astype(jnp.float32)
        for slot, piece in enumerate((attended, query_grad, totals[0], totals[1])):
            pieces[slot].append(piece)
    return tuple(jnp.concatenate(p, axis=1).astype(jnp.bfloat16) for p in pieces)


def solution(mesh):
    spec = P(("batch", "seq"), None)
    return jax.shard_map(
        body, mesh=mesh, in_specs=(spec, spec, spec, spec), out_specs=(spec, spec, spec, spec),
        check_vma=False,
    )
```

```python
import functools
import math

import jax
import jax.numpy as jnp
from jax import lax
from jax.experimental import pallas as pl
from jax.sharding import PartitionSpec as P

HEAD_DIM = 128
POOLED = 128
CHUNKS = 4


def partner_2(block, axis, stride):
    count = lax.axis_size(axis)
    route = []
    for low in range(count):
        high = low | 1 << stride
        if high != low and high < count:
            route += [(low, high), (high, low)]
    return lax.ppermute(block, axis, route)


def attention_kernel(bias_ref, q_ref, do_ref, *refs, scale, parts):
    part_refs = refs[:parts]
    o_ref, dq_ref = refs[parts:parts + 2]
    grad_refs = refs[parts + 2:]
    q = q_ref[...]
    do = do_ref[...]
    k = jnp.concatenate([r[0] for r in part_refs], axis=0)
    v = jnp.concatenate([r[1] for r in part_refs], axis=0)
    scores = (
        lax.dot_general(q, k, (((1,), (1,)), ((), ())), preferred_element_type=jnp.float32) * scale
        + bias_ref[...]
    )
    row_max = jnp.max(scores, axis=-1, keepdims=True)
    log_total = row_max + jnp.log(jnp.sum(jnp.exp(scores - row_max), axis=-1, keepdims=True))
    weights = jnp.exp(scores - log_total)
    weights_low = weights.astype(jnp.bfloat16)
    attended = jnp.dot(weights_low, v, preferred_element_type=jnp.float32).astype(jnp.bfloat16)
    o_ref[...] = attended
    row_dot = jnp.sum(
        do.astype(jnp.float32) * attended.astype(jnp.float32), axis=-1, keepdims=True
    )
    weight_grad = lax.dot_general(do, v, (((1,), (1,)), ((), ())), preferred_element_type=jnp.float32)
    score_grad = (weights * (weight_grad - row_dot)).astype(jnp.bfloat16)
    dq_ref[...] = (
        jnp.dot(score_grad, k, preferred_element_type=jnp.float32) * scale
    ).astype(jnp.bfloat16)
    dk = jnp.dot(score_grad.T, q, preferred_element_type=jnp.float32) * scale
    dv = jnp.dot(weights_low.T, do, preferred_element_type=jnp.float32)
    first = 0
    for r in grad_refs:
        rows = r.shape[1]
        r[0] = dk[first:first + rows]
        r[1] = dv[first:first + rows]
        first += rows


def attention(query_rows, out_grad, parts, key_bias, score_scale, head_offset):
    leaf_rows = query_rows.shape[0]
    width = parts[0].shape[2]
    key_count = sum(p.shape[1] for p in parts)
    heads = width // HEAD_DIM
    row_in = pl.BlockSpec((leaf_rows, HEAD_DIM), lambda h: (0, h + head_offset))
    row_out = pl.BlockSpec((leaf_rows, HEAD_DIM), lambda h: (0, h))
    part_specs = [pl.BlockSpec((2, p.shape[1], HEAD_DIM), lambda h: (0, 0, h)) for p in parts]
    flops = 12 * leaf_rows * key_count * width
    io_bytes = 2 * (4 * leaf_rows + 2 * key_count) * width + 8 * key_count * width
    return pl.pallas_call(
        functools.partial(attention_kernel, scale=score_scale, parts=len(parts)),
        grid=(heads,),
        in_specs=[pl.BlockSpec((1, key_count), lambda h: (0, 0)), row_in, row_in] + part_specs,
        out_specs=[row_out, row_out] + part_specs,
        out_shape=[
            jax.ShapeDtypeStruct((leaf_rows, width), jnp.bfloat16),
            jax.ShapeDtypeStruct((leaf_rows, width), jnp.bfloat16),
        ] + [jax.ShapeDtypeStruct(p.shape, jnp.float32) for p in parts],
        cost_estimate=pl.CostEstimate(
            flops=flops, transcendentals=2 * leaf_rows * key_count * heads, bytes_accessed=io_bytes
        ),
    )(key_bias.reshape(1, key_count), query_rows, out_grad, *parts)


def after(value, earlier):
    return lax.optimization_barrier((value, earlier))[0]


def placed_pool(rows_in, upper):
    run = rows_in // (POOLED // 2)
    out_row = lax.broadcasted_iota(jnp.int32, (POOLED, rows_in), 0)
    in_row = lax.broadcasted_iota(jnp.int32, (POOLED, rows_in), 1)
    offset = upper * (POOLED // 2)
    return jnp.where(out_row - offset == in_row // run, 1.0 / run, 0.0).astype(jnp.float32)


def apply(matrix, rows):
    return jnp.einsum(
        "pr,krw->kpw", matrix, rows.astype(jnp.float32), precision=lax.Precision.HIGHEST,
        preferred_element_type=jnp.float32,
    )


def body(query_rows, key_rows, value_rows, out_grad):
    leaf_rows, model_width = query_rows.shape
    seq_count = lax.axis_size("seq")
    levels = seq_count.bit_length() - 1
    position = lax.axis_index("seq")
    pool_ratio = leaf_rows // POOLED
    score_scale = HEAD_DIM ** (-0.5)
    chunk_width = model_width // CHUNKS
    bias_parts = [jnp.zeros((2 * leaf_rows,), jnp.float32)]
    for step_level in range(1, levels):
        bias_parts.append(jnp.full((POOLED,), math.log(pool_ratio * 2**step_level), jnp.float32))
    key_bias = jnp.concatenate(bias_parts, axis=0)
    bits = [position // 2**step_level % 2 for step_level in range(levels)]
    mine = [placed_pool(leaf_rows if s == 0 else POOLED, bits[s]) for s in range(levels)]
    other = [placed_pool(leaf_rows if s == 0 else POOLED, 1 - bits[s]) for s in range(levels)]
    pool_own = placed_pool(leaf_rows, 0)[: POOLED // 2]
    own_pooled = jnp.einsum(
        "pr,krw->kpw", pool_own.astype(jnp.bfloat16), jnp.stack((key_rows, value_rows)),
        preferred_element_type=jnp.float32,
    )
    sibling_pooled = partner_2(own_pooled.astype(jnp.bfloat16), "seq", 0)
    place_mine = placed_pool(POOLED // 2, bits[0])
    place_other = placed_pool(POOLED // 2, 1 - bits[0])
    pieces = [[], [], [], []]
    late = []
    for chunk in range(CHUNKS):
        columns = slice(chunk * chunk_width, (chunk + 1) * chunk_width)
        own = jnp.stack((key_rows[:, columns], value_rows[:, columns]))
        sibling = partner_2(after(own, sibling_pooled), "seq", 0)
        summary = apply(place_mine, own_pooled[:, :, columns]) + apply(
            place_other, sibling_pooled[:, :, columns]
        )
        far = []
        for step_level in range(1, levels):
            partner = partner_2(summary.astype(jnp.bfloat16), "seq", step_level)
            far.append(partner)
            if step_level + 1 < levels:
                summary = apply(mine[step_level], summary) + apply(other[step_level], partner)
        held = own
        if chunk >= 2:
            held = after(held, late[chunk - 2][1])
        if chunk >= 3:
            held = after(held, late[chunk - 3][0])
        outs = attention(
            query_rows, out_grad, [held, sibling] + far, key_bias, score_scale,
            chunk * (chunk_width // HEAD_DIM),
        )
        attended, query_grad, terms = outs[0], outs[1], outs[2:]
        grad = None
        sends = {}
        for step_level in reversed(range(1, levels)):
            outgoing = terms[1 + step_level]
            if grad is not None:
                outgoing = outgoing + apply(other[step_level].T, grad)
            sends[step_level] = outgoing.astype(jnp.bfloat16)
            returned = partner_2(sends[step_level], "seq", step_level)
            if grad is None:
                grad = returned.astype(jnp.float32)
            else:
                grad = apply(mine[step_level].T, grad) + returned
        to_sibling = terms[1]
        own_total = terms[0]
        if grad is not None:
            to_sibling = to_sibling + apply(other[0].T, grad)
            own_total = own_total + apply(mine[0].T, grad)
        sibling_send = to_sibling.astype(jnp.bfloat16)
        late.append((sibling_send, sends.get(1, sibling_send)))
        from_sibling = partner_2(sibling_send, "seq", 0)
        totals = own_total + from_sibling.astype(jnp.float32)
        for slot, piece in enumerate((attended, query_grad, totals[0], totals[1])):
            pieces[slot].append(piece)
    return tuple(jnp.concatenate(p, axis=1).astype(jnp.bfloat16) for p in pieces)


def solution(mesh):
    spec = P(("batch", "seq"), None)
    return jax.shard_map(
        body, mesh=mesh, in_specs=(spec, spec, spec, spec), out_specs=(spec, spec, spec, spec),
        check_vma=False,
    )
```

```python
import functools
import math

import jax
import jax.numpy as jnp
from jax import lax
from jax.experimental import pallas as pl
from jax.sharding import PartitionSpec as P

HEAD_DIM = 128
POOLED = 128
CHUNKS = 4


def partner_2(block, axis, stride):
    count = lax.axis_size(axis)
    route = []
    for low in range(count):
        high = low | 1 << stride
        if high != low and high < count:
            route += [(low, high), (high, low)]
    return lax.ppermute(block, axis, route)


def attention_kernel(bias_ref, q_ref, do_ref, *refs, scale, parts):
    part_refs = refs[:parts]
    o_ref, dq_ref = refs[parts:parts + 2]
    grad_refs = refs[parts + 2:]
    q = q_ref[...]
    do = do_ref[...]
    k = jnp.concatenate([r[0] for r in part_refs], axis=0)
    v = jnp.concatenate([r[1] for r in part_refs], axis=0)
    scores = (
        lax.dot_general(q, k, (((1,), (1,)), ((), ())), preferred_element_type=jnp.float32) * scale
        + bias_ref[...]
    )
    row_max = jnp.max(scores, axis=-1, keepdims=True)
    log_total = row_max + jnp.log(jnp.sum(jnp.exp(scores - row_max), axis=-1, keepdims=True))
    weights = jnp.exp(scores - log_total)
    weights_low = weights.astype(jnp.bfloat16)
    attended = jnp.dot(weights_low, v, preferred_element_type=jnp.float32).astype(jnp.bfloat16)
    o_ref[...] = attended
    row_dot = jnp.sum(
        do.astype(jnp.float32) * attended.astype(jnp.float32), axis=-1, keepdims=True
    )
    weight_grad = lax.dot_general(do, v, (((1,), (1,)), ((), ())), preferred_element_type=jnp.float32)
    score_grad = (weights * (weight_grad - row_dot)).astype(jnp.bfloat16)
    dq_ref[...] = (
        jnp.dot(score_grad, k, preferred_element_type=jnp.float32) * scale
    ).astype(jnp.bfloat16)
    dk = jnp.dot(score_grad.T, q, preferred_element_type=jnp.float32) * scale
    dv = jnp.dot(weights_low.T, do, preferred_element_type=jnp.float32)
    first = 0
    for r in grad_refs:
        rows = r.shape[1]
        r[0] = dk[first:first + rows]
        r[1] = dv[first:first + rows]
        first += rows


def attention(query_rows, out_grad, parts, key_bias, score_scale, head_offset):
    leaf_rows = query_rows.shape[0]
    width = parts[0].shape[2]
    key_count = sum(p.shape[1] for p in parts)
    heads = width // HEAD_DIM
    row_in = pl.BlockSpec((leaf_rows, HEAD_DIM), lambda h: (0, h + head_offset))
    row_out = pl.BlockSpec((leaf_rows, HEAD_DIM), lambda h: (0, h))
    part_specs = [pl.BlockSpec((2, p.shape[1], HEAD_DIM), lambda h: (0, 0, h)) for p in parts]
    flops = 12 * leaf_rows * key_count * width
    io_bytes = 2 * (4 * leaf_rows + 2 * key_count) * width + 8 * key_count * width
    return pl.pallas_call(
        functools.partial(attention_kernel, scale=score_scale, parts=len(parts)),
        grid=(heads,),
        in_specs=[pl.BlockSpec((1, key_count), lambda h: (0, 0)), row_in, row_in] + part_specs,
        out_specs=[row_out, row_out] + part_specs,
        out_shape=[
            jax.ShapeDtypeStruct((leaf_rows, width), jnp.bfloat16),
            jax.ShapeDtypeStruct((leaf_rows, width), jnp.bfloat16),
        ] + [jax.ShapeDtypeStruct(p.shape, jnp.float32) for p in parts],
        cost_estimate=pl.CostEstimate(
            flops=flops, transcendentals=2 * leaf_rows * key_count * heads, bytes_accessed=io_bytes
        ),
    )(key_bias.reshape(1, key_count), query_rows, out_grad, *parts)


def after(value, earlier):
    return lax.optimization_barrier((value, earlier))[0]


def inner_pairs(count, level):
    mask = (1 << level) | (1 << (level - 1))
    return [(b, b ^ mask) for b in range(count) if (b >> level & 1) != (b >> (level - 1) & 1)]


def outer_pairs(count, level):
    return [(b, b ^ (1 << (level - 1))) for b in range(count) if (b >> level & 1) != (b >> (level - 1) & 1)]


def placed_pool(rows_in, upper):
    run = rows_in // (POOLED // 2)
    out_row = lax.broadcasted_iota(jnp.int32, (POOLED, rows_in), 0)
    in_row = lax.broadcasted_iota(jnp.int32, (POOLED, rows_in), 1)
    offset = upper * (POOLED // 2)
    return jnp.where(out_row - offset == in_row // run, 1.0 / run, 0.0).astype(jnp.float32)


def apply(matrix, rows):
    return jnp.einsum(
        "pr,krw->kpw", matrix, rows.astype(jnp.float32), precision=lax.Precision.HIGHEST,
        preferred_element_type=jnp.float32,
    )


def body(query_rows, key_rows, value_rows, out_grad):
    leaf_rows, model_width = query_rows.shape
    seq_count = lax.axis_size("seq")
    levels = seq_count.bit_length() - 1
    position = lax.axis_index("seq")
    pool_ratio = leaf_rows // POOLED
    score_scale = HEAD_DIM ** (-0.5)
    chunk_width = model_width // CHUNKS
    bias_parts = [jnp.zeros((2 * leaf_rows,), jnp.float32)]
    for step_level in range(1, levels):
        bias_parts.append(jnp.full((POOLED,), math.log(pool_ratio * 2**step_level), jnp.float32))
    key_bias = jnp.concatenate(bias_parts, axis=0)
    bits = [position // 2**step_level % 2 for step_level in range(levels)]
    inner = [None] + [bits[s] != bits[s - 1] for s in range(1, levels)]
    mine = [placed_pool(leaf_rows if s == 0 else POOLED, bits[s]) for s in range(levels)]
    other = [placed_pool(leaf_rows if s == 0 else POOLED, 1 - bits[s]) for s in range(levels)]
    pool_own = placed_pool(leaf_rows, 0)[: POOLED // 2]
    own_pooled = jnp.einsum(
        "pr,krw->kpw", pool_own.astype(jnp.bfloat16), jnp.stack((key_rows, value_rows)),
        preferred_element_type=jnp.float32,
    )
    sibling_pooled = partner_2(own_pooled.astype(jnp.bfloat16), "seq", 0)
    place_mine = placed_pool(POOLED // 2, bits[0])
    place_other = placed_pool(POOLED // 2, 1 - bits[0])
    pieces = [[], [], [], []]
    late = []
    for chunk in range(CHUNKS):
        columns = slice(chunk * chunk_width, (chunk + 1) * chunk_width)
        own = jnp.stack((key_rows[:, columns], value_rows[:, columns]))
        sibling = partner_2(after(own, sibling_pooled), "seq", 0)
        summary = apply(place_mine, own_pooled[:, :, columns]) + apply(
            place_other, sibling_pooled[:, :, columns]
        )
        far = []
        for step_level in range(1, levels):
            if step_level == 1:
                partner = partner_2(summary.astype(jnp.bfloat16), "seq", step_level)
            else:
                crossed = lax.ppermute(summary.astype(jnp.bfloat16), "seq", inner_pairs(seq_count, step_level))
                passed = lax.ppermute(crossed, "seq", outer_pairs(seq_count, step_level))
                partner = jnp.where(inner[step_level], crossed, passed)
            far.append(partner)
            if step_level + 1 < levels:
                summary = apply(mine[step_level], summary) + apply(other[step_level], partner)
        held = own
        if chunk >= 2:
            held = after(held, late[chunk - 2][1])
        if chunk >= 3:
            held = after(held, late[chunk - 3][0])
        outs = attention(
            query_rows, out_grad, [held, sibling] + far, key_bias, score_scale,
            chunk * (chunk_width // HEAD_DIM),
        )
        attended, query_grad, terms = outs[0], outs[1], outs[2:]
        grad = None
        sends = {}
        for step_level in reversed(range(1, levels)):
            outgoing = terms[1 + step_level]
            if grad is not None:
                outgoing = outgoing + apply(other[step_level].T, grad)
            sends[step_level] = outgoing.astype(jnp.bfloat16)
            if step_level == 1:
                returned = partner_2(sends[step_level], "seq", step_level)
            else:
                back = [(t, s) for s, t in outer_pairs(seq_count, step_level)]
                gathered = lax.ppermute(sends[step_level], "seq", back)
                total = outgoing + gathered.astype(jnp.float32)
                returned = lax.ppermute(total.astype(jnp.bfloat16), "seq", inner_pairs(seq_count, step_level))
            if grad is None:
                grad = returned.astype(jnp.float32)
            else:
                grad = apply(mine[step_level].T, grad) + returned
        to_sibling = terms[1]
        own_total = terms[0]
        if grad is not None:
            to_sibling = to_sibling + apply(other[0].T, grad)
            own_total = own_total + apply(mine[0].T, grad)
        sibling_send = to_sibling.astype(jnp.bfloat16)
        late.append((sibling_send, sends.get(1, sibling_send)))
        from_sibling = partner_2(sibling_send, "seq", 0)
        totals = own_total + from_sibling.astype(jnp.float32)
        for slot, piece in enumerate((attended, query_grad, totals[0], totals[1])):
            pieces[slot].append(piece)
    return tuple(jnp.concatenate(p, axis=1).astype(jnp.bfloat16) for p in pieces)


def solution(mesh):
    spec = P(("batch", "seq"), None)
    return jax.shard_map(
        body, mesh=mesh, in_specs=(spec, spec, spec, spec), out_specs=(spec, spec, spec, spec),
        check_vma=False,
    )
```

```python
import functools
import math

import jax
import jax.numpy as jnp
from jax import lax
from jax.experimental import pallas as pl
from jax.sharding import PartitionSpec as P

HEAD_DIM = 128
POOLED = 128
CHUNKS = 4


def partner_2(block, axis, stride):
    count = lax.axis_size(axis)
    route = []
    for low in range(count):
        high = low | 1 << stride
        if high != low and high < count:
            route += [(low, high), (high, low)]
    return lax.ppermute(block, axis, route)


def attention_kernel(bias_ref, q_ref, do_ref, *refs, scale, parts):
    part_refs = refs[:parts]
    o_ref, dq_ref = refs[parts:parts + 2]
    grad_refs = refs[parts + 2:]
    q = q_ref[...]
    do = do_ref[...]
    k = jnp.concatenate([r[0] for r in part_refs], axis=0)
    v = jnp.concatenate([r[1] for r in part_refs], axis=0)
    scores = (
        lax.dot_general(q, k, (((1,), (1,)), ((), ())), preferred_element_type=jnp.float32) * scale
        + bias_ref[...]
    )
    row_max = jnp.max(scores, axis=-1, keepdims=True)
    shifted = jnp.exp(scores - row_max)
    weights = shifted * (1.0 / jnp.sum(shifted, axis=-1, keepdims=True))
    weights_low = weights.astype(jnp.bfloat16)
    attended = jnp.dot(weights_low, v, preferred_element_type=jnp.float32).astype(jnp.bfloat16)
    o_ref[...] = attended
    row_dot = jnp.sum(
        do.astype(jnp.float32) * attended.astype(jnp.float32), axis=-1, keepdims=True
    )
    weight_grad = lax.dot_general(do, v, (((1,), (1,)), ((), ())), preferred_element_type=jnp.float32)
    score_grad = (weights * (weight_grad - row_dot)).astype(jnp.bfloat16)
    dq_ref[...] = (
        jnp.dot(score_grad, k, preferred_element_type=jnp.float32) * scale
    ).astype(jnp.bfloat16)
    by_query = (((0,), (0,)), ((), ()))
    dk = lax.dot_general(score_grad, q, by_query, preferred_element_type=jnp.float32) * scale
    dv = lax.dot_general(weights_low, do, by_query, preferred_element_type=jnp.float32)
    first = 0
    for r in grad_refs:
        rows = r.shape[1]
        r[0] = dk[first:first + rows]
        r[1] = dv[first:first + rows]
        first += rows


def attention(query_rows, out_grad, parts, key_bias, score_scale, head_offset):
    leaf_rows = query_rows.shape[0]
    width = parts[0].shape[2]
    key_count = sum(p.shape[1] for p in parts)
    heads = width // HEAD_DIM
    row_in = pl.BlockSpec((leaf_rows, HEAD_DIM), lambda h: (0, h + head_offset))
    row_out = pl.BlockSpec((leaf_rows, HEAD_DIM), lambda h: (0, h))
    part_specs = [pl.BlockSpec((2, p.shape[1], HEAD_DIM), lambda h: (0, 0, h)) for p in parts]
    flops = 12 * leaf_rows * key_count * width
    io_bytes = 2 * (4 * leaf_rows + 2 * key_count) * width + 8 * key_count * width
    return pl.pallas_call(
        functools.partial(attention_kernel, scale=score_scale, parts=len(parts)),
        grid=(heads,),
        in_specs=[pl.BlockSpec((1, key_count), lambda h: (0, 0)), row_in, row_in] + part_specs,
        out_specs=[row_out, row_out] + part_specs,
        out_shape=[
            jax.ShapeDtypeStruct((leaf_rows, width), jnp.bfloat16),
            jax.ShapeDtypeStruct((leaf_rows, width), jnp.bfloat16),
        ] + [jax.ShapeDtypeStruct(p.shape, jnp.float32) for p in parts],
        cost_estimate=pl.CostEstimate(
            flops=flops, transcendentals=2 * leaf_rows * key_count * heads, bytes_accessed=io_bytes
        ),
    )(key_bias.reshape(1, key_count), query_rows, out_grad, *parts)


def after(value, earlier):
    return lax.optimization_barrier((value, earlier))[0]


def inner_pairs(count, level):
    mask = (1 << level) | (1 << (level - 1))
    return [(b, b ^ mask) for b in range(count) if (b >> level & 1) != (b >> (level - 1) & 1)]


def outer_pairs(count, level):
    return [(b, b ^ (1 << (level - 1))) for b in range(count) if (b >> level & 1) != (b >> (level - 1) & 1)]


def placed_pool(rows_in, upper):
    run = rows_in // (POOLED // 2)
    out_row = lax.broadcasted_iota(jnp.int32, (POOLED, rows_in), 0)
    in_row = lax.broadcasted_iota(jnp.int32, (POOLED, rows_in), 1)
    offset = upper * (POOLED // 2)
    return jnp.where(out_row - offset == in_row // run, 1.0 / run, 0.0).astype(jnp.float32)


def apply(matrix, rows):
    return jnp.einsum(
        "pr,krw->kpw", matrix, rows.astype(jnp.float32), precision=lax.Precision.HIGHEST,
        preferred_element_type=jnp.float32,
    )


def body(query_rows, key_rows, value_rows, out_grad):
    leaf_rows, model_width = query_rows.shape
    seq_count = lax.axis_size("seq")
    levels = seq_count.bit_length() - 1
    position = lax.axis_index("seq")
    pool_ratio = leaf_rows // POOLED
    score_scale = HEAD_DIM ** (-0.5)
    chunk_width = model_width // CHUNKS
    bias_parts = [jnp.zeros((2 * leaf_rows,), jnp.float32)]
    for step_level in range(1, levels):
        bias_parts.append(jnp.full((POOLED,), math.log(pool_ratio * 2**step_level), jnp.float32))
    key_bias = jnp.concatenate(bias_parts, axis=0)
    bits = [position // 2**step_level % 2 for step_level in range(levels)]
    inner = [None] + [bits[s] != bits[s - 1] for s in range(1, levels)]
    mine = [placed_pool(leaf_rows if s == 0 else POOLED, bits[s]) for s in range(levels)]
    other = [placed_pool(leaf_rows if s == 0 else POOLED, 1 - bits[s]) for s in range(levels)]
    pool_own = placed_pool(leaf_rows, 0)[: POOLED // 2]
    own_pooled = jnp.einsum(
        "pr,krw->kpw", pool_own.astype(jnp.bfloat16), jnp.stack((key_rows, value_rows)),
        preferred_element_type=jnp.float32,
    )
    sibling_pooled = partner_2(own_pooled.astype(jnp.bfloat16), "seq", 0)
    place_mine = placed_pool(POOLED // 2, bits[0])
    place_other = placed_pool(POOLED // 2, 1 - bits[0])
    pieces = [[], [], [], []]
    late = []
    for chunk in range(CHUNKS):
        columns = slice(chunk * chunk_width, (chunk + 1) * chunk_width)
        own = jnp.stack((key_rows[:, columns], value_rows[:, columns]))
        sibling = partner_2(after(own, sibling_pooled), "seq", 0)
        summary = apply(place_mine, own_pooled[:, :, columns]) + apply(
            place_other, sibling_pooled[:, :, columns]
        )
        far = []
        for step_level in range(1, levels):
            if step_level == 1:
                partner = partner_2(summary.astype(jnp.bfloat16), "seq", step_level)
            else:
                crossed = lax.ppermute(summary.astype(jnp.bfloat16), "seq", inner_pairs(seq_count, step_level))
                passed = lax.ppermute(crossed, "seq", outer_pairs(seq_count, step_level))
                partner = jnp.where(inner[step_level], crossed, passed)
            far.append(partner)
            if step_level + 1 < levels:
                summary = apply(mine[step_level], summary) + apply(other[step_level], partner)
        held = own
        if chunk >= 2:
            held = after(held, late[chunk - 2][1])
        if chunk >= 3:
            held = after(held, late[chunk - 3][0])
        outs = attention(
            query_rows, out_grad, [held, sibling] + far, key_bias, score_scale,
            chunk * (chunk_width // HEAD_DIM),
        )
        attended, query_grad, terms = outs[0], outs[1], outs[2:]
        grad = None
        sends = {}
        for step_level in reversed(range(1, levels)):
            outgoing = terms[1 + step_level]
            if grad is not None:
                outgoing = outgoing + apply(other[step_level].T, grad)
            sends[step_level] = outgoing.astype(jnp.bfloat16)
            if step_level == 1:
                returned = partner_2(sends[step_level], "seq", step_level)
            else:
                back = [(t, s) for s, t in outer_pairs(seq_count, step_level)]
                gathered = lax.ppermute(sends[step_level], "seq", back)
                total = outgoing + gathered.astype(jnp.float32)
                returned = lax.ppermute(total.astype(jnp.bfloat16), "seq", inner_pairs(seq_count, step_level))
            if grad is None:
                grad = returned.astype(jnp.float32)
            else:
                grad = apply(mine[step_level].T, grad) + returned
        to_sibling = terms[1]
        own_total = terms[0]
        if grad is not None:
            to_sibling = to_sibling + apply(other[0].T, grad)
            own_total = own_total + apply(mine[0].T, grad)
        sibling_send = to_sibling.astype(jnp.bfloat16)
        late.append((sibling_send, sends.get(1, sibling_send)))
        from_sibling = partner_2(sibling_send, "seq", 0)
        totals = own_total + from_sibling.astype(jnp.float32)
        for slot, piece in enumerate((attended, query_grad, totals[0], totals[1])):
            pieces[slot].append(piece)
    return tuple(jnp.concatenate(p, axis=1).astype(jnp.bfloat16) for p in pieces)


def solution(mesh):
    spec = P(("batch", "seq"), None)
    return jax.shard_map(
        body, mesh=mesh, in_specs=(spec, spec, spec, spec), out_specs=(spec, spec, spec, spec),
        check_vma=False,
    )
```

```python
import functools
import math

import jax
import jax.numpy as jnp
from jax import lax
from jax.experimental import pallas as pl
from jax.sharding import PartitionSpec as P

HEAD_DIM = 128
POOLED = 128
CHUNKS = 2


def partner_2(block, axis, stride):
    count = lax.axis_size(axis)
    route = []
    for low in range(count):
        high = low | 1 << stride
        if high != low and high < count:
            route += [(low, high), (high, low)]
    return lax.ppermute(block, axis, route)


def attention_kernel(bias_ref, q_ref, do_ref, *refs, scale, parts):
    part_refs = refs[:parts]
    o_ref, dq_ref = refs[parts:parts + 2]
    grad_refs = refs[parts + 2:]
    q = q_ref[...]
    do = do_ref[...]
    k = jnp.concatenate([r[0] for r in part_refs], axis=0)
    v = jnp.concatenate([r[1] for r in part_refs], axis=0)
    scores = (
        lax.dot_general(q, k, (((1,), (1,)), ((), ())), preferred_element_type=jnp.float32) * scale
        + bias_ref[...]
    )
    row_max = jnp.max(scores, axis=-1, keepdims=True)
    shifted = jnp.exp(scores - row_max)
    weights = shifted * (1.0 / jnp.sum(shifted, axis=-1, keepdims=True))
    weights_low = weights.astype(jnp.bfloat16)
    attended = jnp.dot(weights_low, v, preferred_element_type=jnp.float32).astype(jnp.bfloat16)
    o_ref[...] = attended
    row_dot = jnp.sum(
        do.astype(jnp.float32) * attended.astype(jnp.float32), axis=-1, keepdims=True
    )
    weight_grad = lax.dot_general(do, v, (((1,), (1,)), ((), ())), preferred_element_type=jnp.float32)
    score_grad = (weights * (weight_grad - row_dot)).astype(jnp.bfloat16)
    dq_ref[...] = (
        jnp.dot(score_grad, k, preferred_element_type=jnp.float32) * scale
    ).astype(jnp.bfloat16)
    by_query = (((0,), (0,)), ((), ()))
    dk = lax.dot_general(score_grad, q, by_query, preferred_element_type=jnp.float32) * scale
    dv = lax.dot_general(weights_low, do, by_query, preferred_element_type=jnp.float32)
    first = 0
    for r in grad_refs:
        rows = r.shape[1]
        r[0] = dk[first:first + rows]
        r[1] = dv[first:first + rows]
        first += rows


def attention(query_rows, out_grad, parts, key_bias, score_scale, head_offset):
    leaf_rows = query_rows.shape[0]
    width = parts[0].shape[2]
    key_count = sum(p.shape[1] for p in parts)
    heads = width // HEAD_DIM
    row_in = pl.BlockSpec((leaf_rows, HEAD_DIM), lambda h: (0, h + head_offset))
    row_out = pl.BlockSpec((leaf_rows, HEAD_DIM), lambda h: (0, h))
    part_specs = [pl.BlockSpec((2, p.shape[1], HEAD_DIM), lambda h: (0, 0, h)) for p in parts]
    flops = 12 * leaf_rows * key_count * width
    io_bytes = 2 * (4 * leaf_rows + 2 * key_count) * width + 8 * key_count * width
    return pl.pallas_call(
        functools.partial(attention_kernel, scale=score_scale, parts=len(parts)),
        grid=(heads,),
        in_specs=[pl.BlockSpec((1, key_count), lambda h: (0, 0)), row_in, row_in] + part_specs,
        out_specs=[row_out, row_out] + part_specs,
        out_shape=[
            jax.ShapeDtypeStruct((leaf_rows, width), jnp.bfloat16),
            jax.ShapeDtypeStruct((leaf_rows, width), jnp.bfloat16),
        ] + [jax.ShapeDtypeStruct(p.shape, jnp.float32) for p in parts],
        cost_estimate=pl.CostEstimate(
            flops=flops, transcendentals=2 * leaf_rows * key_count * heads, bytes_accessed=io_bytes
        ),
    )(key_bias.reshape(1, key_count), query_rows, out_grad, *parts)


def after(value, earlier):
    return lax.optimization_barrier((value, earlier))[0]


def inner_pairs(count, level):
    mask = (1 << level) | (1 << (level - 1))
    return [(b, b ^ mask) for b in range(count) if (b >> level & 1) != (b >> (level - 1) & 1)]


def outer_pairs(count, level):
    return [(b, b ^ (1 << (level - 1))) for b in range(count) if (b >> level & 1) != (b >> (level - 1) & 1)]


def placed_pool(rows_in, upper):
    run = rows_in // (POOLED // 2)
    out_row = lax.broadcasted_iota(jnp.int32, (POOLED, rows_in), 0)
    in_row = lax.broadcasted_iota(jnp.int32, (POOLED, rows_in), 1)
    offset = upper * (POOLED // 2)
    return jnp.where(out_row - offset == in_row // run, 1.0 / run, 0.0).astype(jnp.float32)


def apply(matrix, rows):
    return jnp.einsum(
        "pr,krw->kpw", matrix, rows.astype(jnp.float32), precision=lax.Precision.HIGHEST,
        preferred_element_type=jnp.float32,
    )


def body(query_rows, key_rows, value_rows, out_grad):
    leaf_rows, model_width = query_rows.shape
    seq_count = lax.axis_size("seq")
    levels = seq_count.bit_length() - 1
    position = lax.axis_index("seq")
    pool_ratio = leaf_rows // POOLED
    score_scale = HEAD_DIM ** (-0.5)
    chunk_width = model_width // CHUNKS
    bias_parts = [jnp.zeros((2 * leaf_rows,), jnp.float32)]
    for step_level in range(1, levels):
        bias_parts.append(jnp.full((POOLED,), math.log(pool_ratio * 2**step_level), jnp.float32))
    key_bias = jnp.concatenate(bias_parts, axis=0)
    bits = [position // 2**step_level % 2 for step_level in range(levels)]
    inner = [None] + [bits[s] != bits[s - 1] for s in range(1, levels)]
    mine = [placed_pool(leaf_rows if s == 0 else POOLED, bits[s]) for s in range(levels)]
    other = [placed_pool(leaf_rows if s == 0 else POOLED, 1 - bits[s]) for s in range(levels)]
    pool_own = placed_pool(leaf_rows, 0)[: POOLED // 2]
    own_pooled = jnp.einsum(
        "pr,krw->kpw", pool_own.astype(jnp.bfloat16), jnp.stack((key_rows, value_rows)),
        preferred_element_type=jnp.float32,
    )
    sibling_pooled = partner_2(own_pooled.astype(jnp.bfloat16), "seq", 0)
    place_mine = placed_pool(POOLED // 2, bits[0])
    place_other = placed_pool(POOLED // 2, 1 - bits[0])
    pieces = [[], [], [], []]
    late = []
    for chunk in range(CHUNKS):
        columns = slice(chunk * chunk_width, (chunk + 1) * chunk_width)
        own = jnp.stack((key_rows[:, columns], value_rows[:, columns]))
        sibling = partner_2(after(own, sibling_pooled), "seq", 0)
        summary = apply(place_mine, own_pooled[:, :, columns]) + apply(
            place_other, sibling_pooled[:, :, columns]
        )
        far = []
        for step_level in range(1, levels):
            if step_level == 1:
                partner = partner_2(summary.astype(jnp.bfloat16), "seq", step_level)
            else:
                crossed = lax.ppermute(summary.astype(jnp.bfloat16), "seq", inner_pairs(seq_count, step_level))
                passed = lax.ppermute(crossed, "seq", outer_pairs(seq_count, step_level))
                partner = jnp.where(inner[step_level], crossed, passed)
            far.append(partner)
            if step_level + 1 < levels:
                summary = apply(mine[step_level], summary) + apply(other[step_level], partner)
        held = own
        if chunk >= 2:
            held = after(held, late[chunk - 2][1])
        if chunk >= 3:
            held = after(held, late[chunk - 3][0])
        outs = attention(
            query_rows, out_grad, [held, sibling] + far, key_bias, score_scale,
            chunk * (chunk_width // HEAD_DIM),
        )
        attended, query_grad, terms = outs[0], outs[1], outs[2:]
        grad = None
        sends = {}
        for step_level in reversed(range(1, levels)):
            outgoing = terms[1 + step_level]
            if grad is not None:
                outgoing = outgoing + apply(other[step_level].T, grad)
            sends[step_level] = outgoing.astype(jnp.bfloat16)
            if step_level == 1:
                returned = partner_2(sends[step_level], "seq", step_level)
            else:
                back = [(t, s) for s, t in outer_pairs(seq_count, step_level)]
                gathered = lax.ppermute(sends[step_level], "seq", back)
                total = outgoing + gathered.astype(jnp.float32)
                returned = lax.ppermute(total.astype(jnp.bfloat16), "seq", inner_pairs(seq_count, step_level))
            if grad is None:
                grad = returned.astype(jnp.float32)
            else:
                grad = apply(mine[step_level].T, grad) + returned
        to_sibling = terms[1]
        own_total = terms[0]
        if grad is not None:
            to_sibling = to_sibling + apply(other[0].T, grad)
            own_total = own_total + apply(mine[0].T, grad)
        sibling_send = to_sibling.astype(jnp.bfloat16)
        late.append((sibling_send, sends.get(1, sibling_send)))
        from_sibling = partner_2(sibling_send, "seq", 0)
        totals = own_total + from_sibling.astype(jnp.float32)
        for slot, piece in enumerate((attended, query_grad, totals[0], totals[1])):
            pieces[slot].append(piece)
    return tuple(jnp.concatenate(p, axis=1).astype(jnp.bfloat16) for p in pieces)


def solution(mesh):
    spec = P(("batch", "seq"), None)
    return jax.shard_map(
        body, mesh=mesh, in_specs=(spec, spec, spec, spec), out_specs=(spec, spec, spec, spec),
        check_vma=False,
    )
```

```python
import functools
import math

import jax
import jax.numpy as jnp
from jax import lax
from jax.experimental import pallas as pl
from jax.sharding import PartitionSpec as P

HEAD_DIM = 128
POOLED = 128
CHUNKS_MIDDLE = 2


def partner_2(block, axis, stride):
    count = lax.axis_size(axis)
    route = []
    for low in range(count):
        high = low | 1 << stride
        if high != low and high < count:
            route += [(low, high), (high, low)]
    return lax.ppermute(block, axis, route)


def attention_kernel(bias_ref, q_ref, do_ref, *refs, scale, parts):
    part_refs = refs[:parts]
    o_ref, dq_ref = refs[parts:parts + 2]
    grad_refs = refs[parts + 2:]
    q = q_ref[...]
    do = do_ref[...]
    k = jnp.concatenate([r[0] for r in part_refs], axis=0)
    v = jnp.concatenate([r[1] for r in part_refs], axis=0)
    scores = (
        lax.dot_general(q, k, (((1,), (1,)), ((), ())), preferred_element_type=jnp.float32) * scale
        + bias_ref[...]
    )
    row_max = jnp.max(scores, axis=-1, keepdims=True)
    shifted = jnp.exp(scores - row_max)
    weights = shifted * (1.0 / jnp.sum(shifted, axis=-1, keepdims=True))
    weights_low = weights.astype(jnp.bfloat16)
    attended = jnp.dot(weights_low, v, preferred_element_type=jnp.float32).astype(jnp.bfloat16)
    o_ref[...] = attended
    row_dot = jnp.sum(
        do.astype(jnp.float32) * attended.astype(jnp.float32), axis=-1, keepdims=True
    )
    weight_grad = lax.dot_general(do, v, (((1,), (1,)), ((), ())), preferred_element_type=jnp.float32)
    score_grad = (weights * (weight_grad - row_dot)).astype(jnp.bfloat16)
    dq_ref[...] = (
        jnp.dot(score_grad, k, preferred_element_type=jnp.float32) * scale
    ).astype(jnp.bfloat16)
    by_query = (((0,), (0,)), ((), ()))
    dk = lax.dot_general(score_grad, q, by_query, preferred_element_type=jnp.float32) * scale
    dv = lax.dot_general(weights_low, do, by_query, preferred_element_type=jnp.float32)
    first = 0
    for r in grad_refs:
        rows = r.shape[1]
        r[0] = dk[first:first + rows]
        r[1] = dv[first:first + rows]
        first += rows


def attention(query_rows, out_grad, parts, key_bias, score_scale, head_offset):
    leaf_rows = query_rows.shape[0]
    width = parts[0].shape[2]
    key_count = sum(p.shape[1] for p in parts)
    heads = width // HEAD_DIM
    row_in = pl.BlockSpec((leaf_rows, HEAD_DIM), lambda h: (0, h + head_offset))
    row_out = pl.BlockSpec((leaf_rows, HEAD_DIM), lambda h: (0, h))
    part_specs = [pl.BlockSpec((2, p.shape[1], HEAD_DIM), lambda h: (0, 0, h)) for p in parts]
    flops = 12 * leaf_rows * key_count * width
    io_bytes = 2 * (4 * leaf_rows + 2 * key_count) * width + 8 * key_count * width
    return pl.pallas_call(
        functools.partial(attention_kernel, scale=score_scale, parts=len(parts)),
        grid=(heads,),
        in_specs=[pl.BlockSpec((1, key_count), lambda h: (0, 0)), row_in, row_in] + part_specs,
        out_specs=[row_out, row_out] + part_specs,
        out_shape=[
            jax.ShapeDtypeStruct((leaf_rows, width), jnp.bfloat16),
            jax.ShapeDtypeStruct((leaf_rows, width), jnp.bfloat16),
        ] + [jax.ShapeDtypeStruct(p.shape, jnp.float32) for p in parts],
        cost_estimate=pl.CostEstimate(
            flops=flops, transcendentals=2 * leaf_rows * key_count * heads, bytes_accessed=io_bytes
        ),
    )(key_bias.reshape(1, key_count), query_rows, out_grad, *parts)


def after(value, earlier):
    return lax.optimization_barrier((value, earlier))[0]


def inner_pairs(count, level):
    mask = (1 << level) | (1 << (level - 1))
    return [(b, b ^ mask) for b in range(count) if (b >> level & 1) != (b >> (level - 1) & 1)]


def outer_pairs(count, level):
    return [(b, b ^ (1 << (level - 1))) for b in range(count) if (b >> level & 1) != (b >> (level - 1) & 1)]


def placed_pool(rows_in, upper):
    run = rows_in // (POOLED // 2)
    out_row = lax.broadcasted_iota(jnp.int32, (POOLED, rows_in), 0)
    in_row = lax.broadcasted_iota(jnp.int32, (POOLED, rows_in), 1)
    offset = upper * (POOLED // 2)
    return jnp.where(out_row - offset == in_row // run, 1.0 / run, 0.0).astype(jnp.float32)


def apply(matrix, rows):
    return jnp.einsum(
        "pr,krw->kpw", matrix, rows.astype(jnp.float32), precision=lax.Precision.HIGHEST,
        preferred_element_type=jnp.float32,
    )


def body(query_rows, key_rows, value_rows, out_grad):
    leaf_rows, model_width = query_rows.shape
    seq_count = lax.axis_size("seq")
    levels = seq_count.bit_length() - 1
    position = lax.axis_index("seq")
    pool_ratio = leaf_rows // POOLED
    score_scale = HEAD_DIM ** (-0.5)
    head_count = model_width // HEAD_DIM
    edge = max(1, head_count * 3 // 16)
    middle = (head_count - 2 * edge) // CHUNKS_MIDDLE
    chunk_heads = [edge] + [middle] * (CHUNKS_MIDDLE - 1) + [head_count - 2 * edge - middle * (CHUNKS_MIDDLE - 1), edge]
    chunk_first = [sum(chunk_heads[:i]) for i in range(len(chunk_heads))]
    bias_parts = [jnp.zeros((2 * leaf_rows,), jnp.float32)]
    for step_level in range(1, levels):
        bias_parts.append(jnp.full((POOLED,), math.log(pool_ratio * 2**step_level), jnp.float32))
    key_bias = jnp.concatenate(bias_parts, axis=0)
    bits = [position // 2**step_level % 2 for step_level in range(levels)]
    inner = [None] + [bits[s] != bits[s - 1] for s in range(1, levels)]
    mine = [placed_pool(leaf_rows if s == 0 else POOLED, bits[s]) for s in range(levels)]
    other = [placed_pool(leaf_rows if s == 0 else POOLED, 1 - bits[s]) for s in range(levels)]
    pool_own = placed_pool(leaf_rows, 0)[: POOLED // 2]
    own_pooled = jnp.einsum(
        "pr,krw->kpw", pool_own.astype(jnp.bfloat16), jnp.stack((key_rows, value_rows)),
        preferred_element_type=jnp.float32,
    )
    sibling_pooled = partner_2(own_pooled.astype(jnp.bfloat16), "seq", 0)
    place_mine = placed_pool(POOLED // 2, bits[0])
    place_other = placed_pool(POOLED // 2, 1 - bits[0])
    pieces = [[], [], [], []]
    late = []
    for chunk in range(len(chunk_heads)):
        columns = slice(chunk_first[chunk] * HEAD_DIM, (chunk_first[chunk] + chunk_heads[chunk]) * HEAD_DIM)
        own = jnp.stack((key_rows[:, columns], value_rows[:, columns]))
        sibling = partner_2(after(own, sibling_pooled), "seq", 0)
        summary = apply(place_mine, own_pooled[:, :, columns]) + apply(
            place_other, sibling_pooled[:, :, columns]
        )
        far = []
        for step_level in range(1, levels):
            if step_level == 1:
                partner = partner_2(summary.astype(jnp.bfloat16), "seq", step_level)
            else:
                crossed = lax.ppermute(summary.astype(jnp.bfloat16), "seq", inner_pairs(seq_count, step_level))
                passed = lax.ppermute(crossed, "seq", outer_pairs(seq_count, step_level))
                partner = jnp.where(inner[step_level], crossed, passed)
            far.append(partner)
            if step_level + 1 < levels:
                summary = apply(mine[step_level], summary) + apply(other[step_level], partner)
        held = own
        if chunk >= 2:
            held = after(held, late[chunk - 2][1])
        if chunk >= 3:
            held = after(held, late[chunk - 3][0])
        outs = attention(
            query_rows, out_grad, [held, sibling] + far, key_bias, score_scale,
            chunk_first[chunk],
        )
        attended, query_grad, terms = outs[0], outs[1], outs[2:]
        grad = None
        sends = {}
        for step_level in reversed(range(1, levels)):
            outgoing = terms[1 + step_level]
            if grad is not None:
                outgoing = outgoing + apply(other[step_level].T, grad)
            sends[step_level] = outgoing.astype(jnp.bfloat16)
            if step_level == 1:
                returned = partner_2(sends[step_level], "seq", step_level)
            else:
                back = [(t, s) for s, t in outer_pairs(seq_count, step_level)]
                gathered = lax.ppermute(sends[step_level], "seq", back)
                total = outgoing + gathered.astype(jnp.float32)
                returned = lax.ppermute(total.astype(jnp.bfloat16), "seq", inner_pairs(seq_count, step_level))
            if grad is None:
                grad = returned.astype(jnp.float32)
            else:
                grad = apply(mine[step_level].T, grad) + returned
        to_sibling = terms[1]
        own_total = terms[0]
        if grad is not None:
            to_sibling = to_sibling + apply(other[0].T, grad)
            own_total = own_total + apply(mine[0].T, grad)
        sibling_send = to_sibling.astype(jnp.bfloat16)
        late.append((sibling_send, sends.get(1, sibling_send)))
        from_sibling = partner_2(sibling_send, "seq", 0)
        totals = own_total + from_sibling.astype(jnp.float32)
        for slot, piece in enumerate((attended, query_grad, totals[0], totals[1])):
            pieces[slot].append(piece)
    return tuple(jnp.concatenate(p, axis=1).astype(jnp.bfloat16) for p in pieces)


def solution(mesh):
    spec = P(("batch", "seq"), None)
    return jax.shard_map(
        body, mesh=mesh, in_specs=(spec, spec, spec, spec), out_specs=(spec, spec, spec, spec),
        check_vma=False,
    )
```

```python
import functools
import math

import jax
import jax.numpy as jnp
from jax import lax
from jax.experimental import pallas as pl
from jax.sharding import PartitionSpec as P

HEAD_DIM = 128
POOLED = 128
CHUNKS = 4


def partner_2(block, axis, stride):
    count = lax.axis_size(axis)
    route = []
    for low in range(count):
        high = low | 1 << stride
        if high != low and high < count:
            route += [(low, high), (high, low)]
    return lax.ppermute(block, axis, route)


def attention_kernel(bias_ref, q_ref, do_ref, *refs, scale, parts):
    part_refs = refs[:parts]
    o_ref, dq_ref = refs[parts:parts + 2]
    grad_refs = refs[parts + 2:]
    q = q_ref[...]
    do = do_ref[...]
    k = jnp.concatenate([r[0] for r in part_refs], axis=0)
    v = jnp.concatenate([r[1] for r in part_refs], axis=0)
    scores = (
        lax.dot_general(q, k, (((1,), (1,)), ((), ())), preferred_element_type=jnp.float32) * scale
        + bias_ref[...]
    )
    row_max = jnp.max(scores, axis=-1, keepdims=True)
    shifted = jnp.exp(scores - row_max)
    weights = shifted * (1.0 / jnp.sum(shifted, axis=-1, keepdims=True))
    weights_low = weights.astype(jnp.bfloat16)
    attended = jnp.dot(weights_low, v, preferred_element_type=jnp.float32).astype(jnp.bfloat16)
    o_ref[...] = attended
    row_dot = jnp.sum(
        do.astype(jnp.float32) * attended.astype(jnp.float32), axis=-1, keepdims=True
    )
    weight_grad = lax.dot_general(do, v, (((1,), (1,)), ((), ())), preferred_element_type=jnp.float32)
    score_grad = (weights * (weight_grad - row_dot)).astype(jnp.bfloat16)
    dq_ref[...] = (
        jnp.dot(score_grad, k, preferred_element_type=jnp.float32) * scale
    ).astype(jnp.bfloat16)
    by_query = (((0,), (0,)), ((), ()))
    dk = lax.dot_general(score_grad, q, by_query, preferred_element_type=jnp.float32) * scale
    dv = lax.dot_general(weights_low, do, by_query, preferred_element_type=jnp.float32)
    first = 0
    for r in grad_refs:
        rows = r.shape[1]
        r[0] = dk[first:first + rows]
        r[1] = dv[first:first + rows]
        first += rows


def attention(query_rows, out_grad, parts, key_bias, score_scale, head_offset):
    leaf_rows = query_rows.shape[0]
    width = parts[0].shape[2]
    key_count = sum(p.shape[1] for p in parts)
    heads = width // HEAD_DIM
    row_in = pl.BlockSpec((leaf_rows, HEAD_DIM), lambda h: (0, h + head_offset))
    row_out = pl.BlockSpec((leaf_rows, HEAD_DIM), lambda h: (0, h))
    part_specs = [pl.BlockSpec((2, p.shape[1], HEAD_DIM), lambda h: (0, 0, h)) for p in parts]
    flops = 12 * leaf_rows * key_count * width
    io_bytes = 2 * (4 * leaf_rows + 2 * key_count) * width + 8 * key_count * width
    return pl.pallas_call(
        functools.partial(attention_kernel, scale=score_scale, parts=len(parts)),
        grid=(heads,),
        in_specs=[pl.BlockSpec((1, key_count), lambda h: (0, 0)), row_in, row_in] + part_specs,
        out_specs=[row_out, row_out] + part_specs,
        out_shape=[
            jax.ShapeDtypeStruct((leaf_rows, width), jnp.bfloat16),
            jax.ShapeDtypeStruct((leaf_rows, width), jnp.bfloat16),
        ] + [jax.ShapeDtypeStruct(p.shape, jnp.float32) for p in parts],
        cost_estimate=pl.CostEstimate(
            flops=flops, transcendentals=2 * leaf_rows * key_count * heads, bytes_accessed=io_bytes
        ),
    )(key_bias.reshape(1, key_count), query_rows, out_grad, *parts)


def after(value, earlier):
    return lax.optimization_barrier((value, earlier))[0]


def inner_pairs(count, level):
    mask = (1 << level) | (1 << (level - 1))
    return [(b, b ^ mask) for b in range(count) if (b >> level & 1) != (b >> (level - 1) & 1)]


def outer_pairs(count, level):
    return [(b, b ^ (1 << (level - 1))) for b in range(count) if (b >> level & 1) != (b >> (level - 1) & 1)]


def placed_pool(rows_in, upper):
    run = rows_in // (POOLED // 2)
    out_row = lax.broadcasted_iota(jnp.int32, (POOLED, rows_in), 0)
    in_row = lax.broadcasted_iota(jnp.int32, (POOLED, rows_in), 1)
    offset = upper * (POOLED // 2)
    return jnp.where(out_row - offset == in_row // run, 1.0 / run, 0.0).astype(jnp.float32)


def apply(matrix, rows):
    return jnp.einsum(
        "pr,krw->kpw", matrix, rows.astype(jnp.float32), precision=lax.Precision.HIGHEST,
        preferred_element_type=jnp.float32,
    )


def body(query_rows, key_rows, value_rows, out_grad):
    leaf_rows, model_width = query_rows.shape
    seq_count = lax.axis_size("seq")
    levels = seq_count.bit_length() - 1
    position = lax.axis_index("seq")
    pool_ratio = leaf_rows // POOLED
    score_scale = HEAD_DIM ** (-0.5)
    chunk_width = model_width // CHUNKS
    bias_parts = [jnp.zeros((2 * leaf_rows,), jnp.float32)]
    for step_level in range(1, levels):
        bias_parts.append(jnp.full((POOLED,), math.log(pool_ratio * 2**step_level), jnp.float32))
    key_bias = jnp.concatenate(bias_parts, axis=0)
    bits = [position // 2**step_level % 2 for step_level in range(levels)]
    inner = [None] + [bits[s] != bits[s - 1] for s in range(1, levels)]
    mine = [placed_pool(leaf_rows if s == 0 else POOLED, bits[s]) for s in range(levels)]
    other = [placed_pool(leaf_rows if s == 0 else POOLED, 1 - bits[s]) for s in range(levels)]
    pool_own = placed_pool(leaf_rows, 0)[: POOLED // 2]
    own_pooled = jnp.einsum(
        "pr,krw->kpw", pool_own.astype(jnp.bfloat16), jnp.stack((key_rows, value_rows)),
        preferred_element_type=jnp.float32,
    )
    sibling_pooled = partner_2(own_pooled.astype(jnp.bfloat16), "seq", 0)
    pick_row = lax.broadcasted_iota(jnp.int32, (POOLED // 2, POOLED), 0)
    pick_col = lax.broadcasted_iota(jnp.int32, (POOLED // 2, POOLED), 1)
    pick_other = jnp.where(
        pick_col == pick_row + (1 - bits[0]) * (POOLED // 2), 1.0, 0.0
    ).astype(jnp.float32)
    spread_own = pool_own.T
    place_mine = placed_pool(POOLED // 2, bits[0])
    place_other = placed_pool(POOLED // 2, 1 - bits[0])
    pieces = [[], [], [], []]
    late = []
    for chunk in range(CHUNKS):
        columns = slice(chunk * chunk_width, (chunk + 1) * chunk_width)
        own = jnp.stack((key_rows[:, columns], value_rows[:, columns]))
        sibling = partner_2(after(own, sibling_pooled), "seq", 0)
        summary = apply(place_mine, own_pooled[:, :, columns]) + apply(
            place_other, sibling_pooled[:, :, columns]
        )
        far = []
        for step_level in range(1, levels):
            if step_level == 1:
                partner = partner_2(summary.astype(jnp.bfloat16), "seq", step_level)
            else:
                crossed = lax.ppermute(summary.astype(jnp.bfloat16), "seq", inner_pairs(seq_count, step_level))
                passed = lax.ppermute(crossed, "seq", outer_pairs(seq_count, step_level))
                partner = jnp.where(inner[step_level], crossed, passed)
            far.append(partner)
            if step_level + 1 < levels:
                summary = apply(mine[step_level], summary) + apply(other[step_level], partner)
        held = own
        if chunk >= 2:
            held = after(held, late[chunk - 2][1])
        if chunk >= 3:
            held = after(held, late[chunk - 3][0])
        outs = attention(
            query_rows, out_grad, [held, sibling] + far, key_bias, score_scale,
            chunk * (chunk_width // HEAD_DIM),
        )
        attended, query_grad, terms = outs[0], outs[1], outs[2:]
        grad = None
        sends = {}
        for step_level in reversed(range(1, levels)):
            outgoing = terms[1 + step_level]
            if grad is not None:
                outgoing = outgoing + apply(other[step_level].T, grad)
            sends[step_level] = outgoing.astype(jnp.bfloat16)
            if step_level == 1:
                returned = partner_2(sends[step_level], "seq", step_level)
            else:
                back = [(t, s) for s, t in outer_pairs(seq_count, step_level)]
                gathered = lax.ppermute(sends[step_level], "seq", back)
                total = outgoing + gathered.astype(jnp.float32)
                returned = lax.ppermute(total.astype(jnp.bfloat16), "seq", inner_pairs(seq_count, step_level))
            if grad is None:
                grad = returned.astype(jnp.float32)
            else:
                grad = apply(mine[step_level].T, grad) + returned
        own_total = terms[0]
        sibling_send = terms[1].astype(jnp.bfloat16)
        late.append((sibling_send, sends.get(1, sibling_send)))
        from_sibling = partner_2(sibling_send, "seq", 0)
        if grad is not None:
            own_total = own_total + apply(mine[0].T, grad)
            pooled_back = partner_2(apply(pick_other, grad).astype(jnp.bfloat16), "seq", 0)
            own_total = own_total + apply(spread_own, pooled_back)
        totals = own_total + from_sibling.astype(jnp.float32)
        for slot, piece in enumerate((attended, query_grad, totals[0], totals[1])):
            pieces[slot].append(piece)
    return tuple(jnp.concatenate(p, axis=1).astype(jnp.bfloat16) for p in pieces)


def solution(mesh):
    spec = P(("batch", "seq"), None)
    return jax.shard_map(
        body, mesh=mesh, in_specs=(spec, spec, spec, spec), out_specs=(spec, spec, spec, spec),
        check_vma=False,
    )
```

```python
import functools
import math

import jax
import jax.numpy as jnp
from jax import lax
from jax.experimental import pallas as pl
from jax.sharding import PartitionSpec as P

HEAD_DIM = 128
POOLED = 128
CHUNKS = 4


def partner_2(block, axis, stride):
    count = lax.axis_size(axis)
    route = []
    for low in range(count):
        high = low | 1 << stride
        if high != low and high < count:
            route += [(low, high), (high, low)]
    return lax.ppermute(block, axis, route)


def attention_kernel(bias_ref, q_ref, do_ref, *refs, scale, parts):
    part_refs = refs[:parts]
    o_ref, dq_ref = refs[parts:parts + 2]
    grad_refs = refs[parts + 2:]
    q = q_ref[...]
    do = do_ref[...]
    k = jnp.concatenate([r[0] for r in part_refs], axis=0)
    v = jnp.concatenate([r[1] for r in part_refs], axis=0)
    scores = (
        lax.dot_general(q, k, (((1,), (1,)), ((), ())), preferred_element_type=jnp.float32) * scale
        + bias_ref[...]
    )
    row_max = jnp.max(scores, axis=-1, keepdims=True)
    shifted = jnp.exp(scores - row_max)
    weights = shifted * (1.0 / jnp.sum(shifted, axis=-1, keepdims=True))
    weights_low = weights.astype(jnp.bfloat16)
    attended = jnp.dot(weights_low, v, preferred_element_type=jnp.float32).astype(jnp.bfloat16)
    o_ref[...] = attended
    row_dot = jnp.sum(
        do.astype(jnp.float32) * attended.astype(jnp.float32), axis=-1, keepdims=True
    )
    weight_grad = lax.dot_general(do, v, (((1,), (1,)), ((), ())), preferred_element_type=jnp.float32)
    score_grad = (weights * (weight_grad - row_dot)).astype(jnp.bfloat16)
    dq_ref[...] = (
        jnp.dot(score_grad, k, preferred_element_type=jnp.float32) * scale
    ).astype(jnp.bfloat16)
    by_query = (((0,), (0,)), ((), ()))
    dk = lax.dot_general(score_grad, q, by_query, preferred_element_type=jnp.float32) * scale
    dv = lax.dot_general(weights_low, do, by_query, preferred_element_type=jnp.float32)
    first = 0
    for r in grad_refs:
        rows = r.shape[1]
        r[0] = dk[first:first + rows]
        r[1] = dv[first:first + rows]
        first += rows


def attention(query_rows, out_grad, parts, key_bias, score_scale, head_offset):
    leaf_rows = query_rows.shape[0]
    width = parts[0].shape[2]
    key_count = sum(p.shape[1] for p in parts)
    heads = width // HEAD_DIM
    row_in = pl.BlockSpec((leaf_rows, HEAD_DIM), lambda h: (0, h + head_offset))
    row_out = pl.BlockSpec((leaf_rows, HEAD_DIM), lambda h: (0, h))
    part_specs = [pl.BlockSpec((2, p.shape[1], HEAD_DIM), lambda h: (0, 0, h)) for p in parts]
    flops = 12 * leaf_rows * key_count * width
    io_bytes = 2 * (4 * leaf_rows + 2 * key_count) * width + 8 * key_count * width
    return pl.pallas_call(
        functools.partial(attention_kernel, scale=score_scale, parts=len(parts)),
        grid=(heads,),
        in_specs=[pl.BlockSpec((1, key_count), lambda h: (0, 0)), row_in, row_in] + part_specs,
        out_specs=[row_out, row_out] + part_specs,
        out_shape=[
            jax.ShapeDtypeStruct((leaf_rows, width), jnp.bfloat16),
            jax.ShapeDtypeStruct((leaf_rows, width), jnp.bfloat16),
        ] + [jax.ShapeDtypeStruct(p.shape, jnp.float32) for p in parts],
        cost_estimate=pl.CostEstimate(
            flops=flops, transcendentals=2 * leaf_rows * key_count * heads, bytes_accessed=io_bytes
        ),
    )(key_bias.reshape(1, key_count), query_rows, out_grad, *parts)


def after(value, earlier):
    return lax.optimization_barrier((value, earlier))[0]


def inner_pairs(count, level):
    mask = (1 << level) | (1 << (level - 1))
    return [(b, b ^ mask) for b in range(count) if (b >> level & 1) != (b >> (level - 1) & 1)]


def outer_pairs(count, level):
    return [(b, b ^ (1 << (level - 1))) for b in range(count) if (b >> level & 1) != (b >> (level - 1) & 1)]


def placed_pool(rows_in, upper):
    run = rows_in // (POOLED // 2)
    out_row = lax.broadcasted_iota(jnp.int32, (POOLED, rows_in), 0)
    in_row = lax.broadcasted_iota(jnp.int32, (POOLED, rows_in), 1)
    offset = upper * (POOLED // 2)
    return jnp.where(out_row - offset == in_row // run, 1.0 / run, 0.0).astype(jnp.float32)


def apply(matrix, rows):
    return jnp.einsum(
        "pr,krw->kpw", matrix, rows.astype(jnp.float32), precision=lax.Precision.HIGHEST,
        preferred_element_type=jnp.float32,
    )


def body(query_rows, key_rows, value_rows, out_grad):
    leaf_rows, model_width = query_rows.shape
    seq_count = lax.axis_size("seq")
    levels = seq_count.bit_length() - 1
    position = lax.axis_index("seq")
    pool_ratio = leaf_rows // POOLED
    score_scale = HEAD_DIM ** (-0.5)
    chunk_width = model_width // CHUNKS
    bias_parts = [jnp.zeros((2 * leaf_rows,), jnp.float32)]
    for step_level in range(1, levels):
        bias_parts.append(jnp.full((POOLED,), math.log(pool_ratio * 2**step_level), jnp.float32))
    key_bias = jnp.concatenate(bias_parts, axis=0)
    bits = [position // 2**step_level % 2 for step_level in range(levels)]
    inner = [None] + [bits[s] != bits[s - 1] for s in range(1, levels)]
    mine = [placed_pool(leaf_rows if s == 0 else POOLED, bits[s]) for s in range(levels)]
    other = [placed_pool(leaf_rows if s == 0 else POOLED, 1 - bits[s]) for s in range(levels)]
    pool_own = placed_pool(leaf_rows, 0)[: POOLED // 2]
    own_pooled = jnp.einsum(
        "pr,krw->kpw", pool_own.astype(jnp.bfloat16), jnp.stack((key_rows, value_rows)),
        preferred_element_type=jnp.float32,
    )
    sibling_pooled = partner_2(own_pooled.astype(jnp.bfloat16), "seq", 0)
    pick_row = lax.broadcasted_iota(jnp.int32, (POOLED // 2, POOLED), 0)
    pick_col = lax.broadcasted_iota(jnp.int32, (POOLED // 2, POOLED), 1)
    pick_other = jnp.where(
        pick_col == pick_row + (1 - bits[0]) * (POOLED // 2), 1.0, 0.0
    ).astype(jnp.float32)
    spread_own = pool_own.T
    place_mine = placed_pool(POOLED // 2, bits[0])
    place_other = placed_pool(POOLED // 2, 1 - bits[0])
    pieces = [[], [], [], []]
    late = []
    for chunk in range(CHUNKS):
        columns = slice(chunk * chunk_width, (chunk + 1) * chunk_width)
        own = jnp.stack((key_rows[:, columns], value_rows[:, columns]))
        sibling = partner_2(after(own, sibling_pooled), "seq", 0)
        summary = apply(place_mine, own_pooled[:, :, columns]) + apply(
            place_other, sibling_pooled[:, :, columns]
        )
        far = []
        for step_level in range(1, levels):
            if step_level == 1:
                partner = partner_2(summary.astype(jnp.bfloat16), "seq", step_level)
            else:
                crossed = lax.ppermute(summary.astype(jnp.bfloat16), "seq", inner_pairs(seq_count, step_level))
                passed = lax.ppermute(crossed, "seq", outer_pairs(seq_count, step_level))
                partner = jnp.where(inner[step_level], crossed, passed)
            far.append(partner)
            if step_level + 1 < levels:
                summary = apply(mine[step_level], summary) + apply(other[step_level], partner)
        held = own
        if chunk >= 2:
            held = after(held, late[chunk - 2][1])
        if chunk >= 3:
            held = after(held, late[chunk - 3][0])
        outs = attention(
            query_rows, out_grad, [held, sibling] + far, key_bias, score_scale,
            chunk * (chunk_width // HEAD_DIM),
        )
        attended, query_grad, terms = outs[0], outs[1], outs[2:]
        grad = None
        sends = {}
        for step_level in reversed(range(1, levels)):
            outgoing = terms[1 + step_level]
            if grad is not None:
                outgoing = outgoing + apply(other[step_level].T, grad)
            sends[step_level] = outgoing.astype(jnp.bfloat16)
            if step_level == 1:
                returned = partner_2(sends[step_level], "seq", step_level)
            else:
                back = [(t, s) for s, t in outer_pairs(seq_count, step_level)]
                gathered = lax.ppermute(sends[step_level], "seq", back)
                total = outgoing + gathered.astype(jnp.float32)
                returned = lax.ppermute(total.astype(jnp.bfloat16), "seq", inner_pairs(seq_count, step_level))
            if grad is None:
                grad = returned.astype(jnp.float32)
            else:
                grad = apply(mine[step_level].T, grad) + returned
        to_sibling = terms[1]
        own_total = terms[0]
        split = chunk == CHUNKS - 1 and grad is not None
        if grad is not None:
            if not split:
                to_sibling = to_sibling + apply(other[0].T, grad)
            own_total = own_total + apply(mine[0].T, grad)
        sibling_send = to_sibling.astype(jnp.bfloat16)
        late.append((sibling_send, sends.get(1, sibling_send)))
        from_sibling = partner_2(sibling_send, "seq", 0)
        if split:
            pooled_back = partner_2(apply(pick_other, grad).astype(jnp.bfloat16), "seq", 0)
            own_total = own_total + apply(spread_own, pooled_back)
        totals = own_total + from_sibling.astype(jnp.float32)
        for slot, piece in enumerate((attended, query_grad, totals[0], totals[1])):
            pieces[slot].append(piece)
    return tuple(jnp.concatenate(p, axis=1).astype(jnp.bfloat16) for p in pieces)


def solution(mesh):
    spec = P(("batch", "seq"), None)
    return jax.shard_map(
        body, mesh=mesh, in_specs=(spec, spec, spec, spec), out_specs=(spec, spec, spec, spec),
        check_vma=False,
    )
```

```python
import functools
import math

import jax
import jax.numpy as jnp
from jax import lax
from jax.experimental import pallas as pl
from jax.sharding import PartitionSpec as P

HEAD_DIM = 128
POOLED = 128
CHUNKS = 4


def partner_2(block, axis, stride):
    count = lax.axis_size(axis)
    route = []
    for low in range(count):
        high = low | 1 << stride
        if high != low and high < count:
            route += [(low, high), (high, low)]
    return lax.ppermute(block, axis, route)


def attention_kernel(bias_ref, q_ref, do_ref, *refs, scale, parts):
    part_refs = refs[:parts]
    o_ref, dq_ref = refs[parts:parts + 2]
    grad_refs = refs[parts + 2:]
    q = q_ref[...]
    do = do_ref[...]
    k = jnp.concatenate([r[0] for r in part_refs], axis=0)
    v = jnp.concatenate([r[1] for r in part_refs], axis=0)
    scores = (
        lax.dot_general(q, k, (((1,), (1,)), ((), ())), preferred_element_type=jnp.float32) * scale
        + bias_ref[...]
    )
    row_max = jnp.max(scores, axis=-1, keepdims=True)
    shifted = jnp.exp(scores - row_max)
    weights = shifted * (1.0 / jnp.sum(shifted, axis=-1, keepdims=True))
    weights_low = weights.astype(jnp.bfloat16)
    attended = jnp.dot(weights_low, v, preferred_element_type=jnp.float32).astype(jnp.bfloat16)
    o_ref[...] = attended
    row_dot = jnp.sum(
        do.astype(jnp.float32) * attended.astype(jnp.float32), axis=-1, keepdims=True
    )
    weight_grad = lax.dot_general(do, v, (((1,), (1,)), ((), ())), preferred_element_type=jnp.float32)
    score_grad = (weights * (weight_grad - row_dot)).astype(jnp.bfloat16)
    dq_ref[...] = (
        jnp.dot(score_grad, k, preferred_element_type=jnp.float32) * scale
    ).astype(jnp.bfloat16)
    by_query = (((0,), (0,)), ((), ()))
    dk = lax.dot_general(score_grad, q, by_query, preferred_element_type=jnp.float32) * scale
    dv = lax.dot_general(weights_low, do, by_query, preferred_element_type=jnp.float32)
    first = 0
    for r in grad_refs:
        rows = r.shape[1]
        r[0] = dk[first:first + rows]
        r[1] = dv[first:first + rows]
        first += rows


def attention(query_rows, out_grad, parts, key_bias, score_scale, head_offset):
    leaf_rows = query_rows.shape[0]
    width = parts[0].shape[2]
    key_count = sum(p.shape[1] for p in parts)
    heads = width // HEAD_DIM
    row_in = pl.BlockSpec((leaf_rows, HEAD_DIM), lambda h: (0, h + head_offset))
    row_out = pl.BlockSpec((leaf_rows, HEAD_DIM), lambda h: (0, h))
    part_specs = [pl.BlockSpec((2, p.shape[1], HEAD_DIM), lambda h: (0, 0, h)) for p in parts]
    flops = 12 * leaf_rows * key_count * width
    io_bytes = 2 * (4 * leaf_rows + 2 * key_count) * width + 8 * key_count * width
    return pl.pallas_call(
        functools.partial(attention_kernel, scale=score_scale, parts=len(parts)),
        grid=(heads,),
        in_specs=[pl.BlockSpec((1, key_count), lambda h: (0, 0)), row_in, row_in] + part_specs,
        out_specs=[row_out, row_out] + part_specs,
        out_shape=[
            jax.ShapeDtypeStruct((leaf_rows, width), jnp.bfloat16),
            jax.ShapeDtypeStruct((leaf_rows, width), jnp.bfloat16),
        ] + [jax.ShapeDtypeStruct(p.shape, jnp.float32) for p in parts],
        cost_estimate=pl.CostEstimate(
            flops=flops, transcendentals=2 * leaf_rows * key_count * heads, bytes_accessed=io_bytes
        ),
    )(key_bias.reshape(1, key_count), query_rows, out_grad, *parts)


def after(value, earlier):
    return lax.optimization_barrier((value, earlier))[0]


def inner_pairs(count, level):
    mask = (1 << level) | (1 << (level - 1))
    return [(b, b ^ mask) for b in range(count) if (b >> level & 1) != (b >> (level - 1) & 1)]


def outer_pairs(count, level):
    return [(b, b ^ (1 << (level - 1))) for b in range(count) if (b >> level & 1) != (b >> (level - 1) & 1)]


def placed_pool(rows_in, upper):
    run = rows_in // (POOLED // 2)
    out_row = lax.broadcasted_iota(jnp.int32, (POOLED, rows_in), 0)
    in_row = lax.broadcasted_iota(jnp.int32, (POOLED, rows_in), 1)
    offset = upper * (POOLED // 2)
    return jnp.where(out_row - offset == in_row // run, 1.0 / run, 0.0).astype(jnp.float32)


def apply(matrix, rows):
    return jnp.einsum(
        "pr,krw->kpw", matrix, rows.astype(jnp.float32), precision=lax.Precision.HIGHEST,
        preferred_element_type=jnp.float32,
    )


def body(query_rows, key_rows, value_rows, out_grad):
    leaf_rows, model_width = query_rows.shape
    seq_count = lax.axis_size("seq")
    levels = seq_count.bit_length() - 1
    position = lax.axis_index("seq")
    pool_ratio = leaf_rows // POOLED
    score_scale = HEAD_DIM ** (-0.5)
    chunk_width = model_width // CHUNKS
    bias_parts = [jnp.zeros((2 * leaf_rows,), jnp.float32)]
    for step_level in range(1, levels):
        bias_parts.append(jnp.full((POOLED,), math.log(pool_ratio * 2**step_level), jnp.float32))
    key_bias = jnp.concatenate(bias_parts, axis=0)
    bits = [position // 2**step_level % 2 for step_level in range(levels)]
    inner = [None] + [bits[s] != bits[s - 1] for s in range(1, levels)]
    mine = [placed_pool(leaf_rows if s == 0 else POOLED, bits[s]) for s in range(levels)]
    other = [placed_pool(leaf_rows if s == 0 else POOLED, 1 - bits[s]) for s in range(levels)]
    pool_own = placed_pool(leaf_rows, 0)[: POOLED // 2]
    own_pooled = jnp.einsum(
        "pr,krw->kpw", pool_own.astype(jnp.bfloat16), jnp.stack((key_rows, value_rows)),
        preferred_element_type=jnp.float32,
    )
    sibling_pooled = partner_2(own_pooled.astype(jnp.bfloat16), "seq", 0)
    pick_row = lax.broadcasted_iota(jnp.int32, (POOLED // 2, POOLED), 0)
    pick_col = lax.broadcasted_iota(jnp.int32, (POOLED // 2, POOLED), 1)
    pick_other = jnp.where(
        pick_col == pick_row + (1 - bits[0]) * (POOLED // 2), 1.0, 0.0
    ).astype(jnp.float32)
    spread_own = pool_own.T
    place_mine = placed_pool(POOLED // 2, bits[0])
    place_other = placed_pool(POOLED // 2, 1 - bits[0])
    pieces = [[], [], [], []]
    late = []
    for chunk in range(CHUNKS):
        columns = slice(chunk * chunk_width, (chunk + 1) * chunk_width)
        own = jnp.stack((key_rows[:, columns], value_rows[:, columns]))
        sibling = partner_2(after(own, sibling_pooled), "seq", 0)
        summary = apply(place_mine, own_pooled[:, :, columns]) + apply(
            place_other, sibling_pooled[:, :, columns]
        )
        far = []
        for step_level in range(1, levels):
            if step_level == 1:
                partner = partner_2(summary.astype(jnp.bfloat16), "seq", step_level)
            else:
                crossed = lax.ppermute(summary.astype(jnp.bfloat16), "seq", inner_pairs(seq_count, step_level))
                passed = lax.ppermute(crossed, "seq", outer_pairs(seq_count, step_level))
                partner = jnp.where(inner[step_level], crossed, passed)
            far.append(partner)
            if step_level + 1 < levels:
                summary = apply(mine[step_level], summary) + apply(other[step_level], partner)
        held = own
        if chunk >= 2:
            held = after(held, late[chunk - 2][1])
        if chunk >= 3:
            held = after(held, late[chunk - 3][0])
        outs = attention(
            query_rows, out_grad, [held, sibling] + far, key_bias, score_scale,
            chunk * (chunk_width // HEAD_DIM),
        )
        attended, query_grad, terms = outs[0], outs[1], outs[2:]
        grad = None
        sends = {}
        for step_level in reversed(range(1, levels)):
            outgoing = terms[1 + step_level]
            if grad is not None:
                outgoing = outgoing + apply(other[step_level].T, grad)
            sends[step_level] = outgoing.astype(jnp.bfloat16)
            if step_level == 1:
                returned = partner_2(sends[step_level], "seq", step_level)
            else:
                back = [(t, s) for s, t in outer_pairs(seq_count, step_level)]
                gathered = lax.ppermute(sends[step_level], "seq", back)
                total = outgoing + gathered.astype(jnp.float32)
                returned = lax.ppermute(total.astype(jnp.bfloat16), "seq", inner_pairs(seq_count, step_level))
            if grad is None:
                grad = returned.astype(jnp.float32)
            else:
                grad = apply(mine[step_level].T, grad) + returned
        to_sibling = terms[1]
        own_total = terms[0]
        split = chunk >= CHUNKS - 2 and grad is not None
        if grad is not None:
            if not split:
                to_sibling = to_sibling + apply(other[0].T, grad)
            own_total = own_total + apply(mine[0].T, grad)
        sibling_send = to_sibling.astype(jnp.bfloat16)
        late.append((sibling_send, sends.get(1, sibling_send)))
        from_sibling = partner_2(sibling_send, "seq", 0)
        if split:
            pooled_back = partner_2(apply(pick_other, grad).astype(jnp.bfloat16), "seq", 0)
            own_total = own_total + apply(spread_own, pooled_back)
        totals = own_total + from_sibling.astype(jnp.float32)
        for slot, piece in enumerate((attended, query_grad, totals[0], totals[1])):
            pieces[slot].append(piece)
    return tuple(jnp.concatenate(p, axis=1).astype(jnp.bfloat16) for p in pieces)


def solution(mesh):
    spec = P(("batch", "seq"), None)
    return jax.shard_map(
        body, mesh=mesh, in_specs=(spec, spec, spec, spec), out_specs=(spec, spec, spec, spec),
        check_vma=False,
    )
```

```python
import functools
import math

import jax
import jax.numpy as jnp
from jax import lax
from jax.experimental import pallas as pl
from jax.sharding import PartitionSpec as P

HEAD_DIM = 128
POOLED = 128
CHUNKS = 4


def partner_2(block, axis, stride):
    count = lax.axis_size(axis)
    route = []
    for low in range(count):
        high = low | 1 << stride
        if high != low and high < count:
            route += [(low, high), (high, low)]
    return lax.ppermute(block, axis, route)


def attention_kernel(bias_ref, q_ref, do_ref, *refs, scale, parts):
    part_refs = refs[:parts]
    o_ref, dq_ref = refs[parts:parts + 2]
    grad_refs = refs[parts + 2:]
    q = q_ref[...]
    do = do_ref[...]
    k = jnp.concatenate([r[0] for r in part_refs], axis=0)
    v = jnp.concatenate([r[1] for r in part_refs], axis=0)
    scores = (
        lax.dot_general(q, k, (((1,), (1,)), ((), ())), preferred_element_type=jnp.float32) * scale
        + bias_ref[...]
    )
    row_max = jnp.max(scores, axis=-1, keepdims=True)
    shifted = jnp.exp(scores - row_max)
    weights = shifted * (1.0 / jnp.sum(shifted, axis=-1, keepdims=True))
    weights_low = weights.astype(jnp.bfloat16)
    attended = jnp.dot(weights_low, v, preferred_element_type=jnp.float32).astype(jnp.bfloat16)
    o_ref[...] = attended
    row_dot = jnp.sum(
        do.astype(jnp.float32) * attended.astype(jnp.float32), axis=-1, keepdims=True
    )
    weight_grad = lax.dot_general(do, v, (((1,), (1,)), ((), ())), preferred_element_type=jnp.float32)
    score_grad = (weights * (weight_grad - row_dot)).astype(jnp.bfloat16)
    dq_ref[...] = (
        jnp.dot(score_grad, k, preferred_element_type=jnp.float32) * scale
    ).astype(jnp.bfloat16)
    by_query = (((0,), (0,)), ((), ()))
    dk = lax.dot_general(score_grad, q, by_query, preferred_element_type=jnp.float32) * scale
    dv = lax.dot_general(weights_low, do, by_query, preferred_element_type=jnp.float32)
    first = 0
    for r in grad_refs:
        rows = r.shape[1]
        r[0] = dk[first:first + rows]
        r[1] = dv[first:first + rows]
        first += rows


def attention(query_rows, out_grad, parts, key_bias, score_scale, head_offset):
    leaf_rows = query_rows.shape[0]
    width = parts[0].shape[2]
    key_count = sum(p.shape[1] for p in parts)
    heads = width // HEAD_DIM
    row_in = pl.BlockSpec((leaf_rows, HEAD_DIM), lambda h: (0, h + head_offset))
    row_out = pl.BlockSpec((leaf_rows, HEAD_DIM), lambda h: (0, h))
    part_specs = [pl.BlockSpec((2, p.shape[1], HEAD_DIM), lambda h: (0, 0, h)) for p in parts]
    flops = 12 * leaf_rows * key_count * width
    io_bytes = 2 * (4 * leaf_rows + 2 * key_count) * width + 8 * key_count * width
    return pl.pallas_call(
        functools.partial(attention_kernel, scale=score_scale, parts=len(parts)),
        grid=(heads,),
        in_specs=[pl.BlockSpec((1, key_count), lambda h: (0, 0)), row_in, row_in] + part_specs,
        out_specs=[row_out, row_out] + part_specs,
        out_shape=[
            jax.ShapeDtypeStruct((leaf_rows, width), jnp.bfloat16),
            jax.ShapeDtypeStruct((leaf_rows, width), jnp.bfloat16),
        ] + [jax.ShapeDtypeStruct(p.shape, jnp.float32) for p in parts],
        cost_estimate=pl.CostEstimate(
            flops=flops, transcendentals=2 * leaf_rows * key_count * heads, bytes_accessed=io_bytes
        ),
    )(key_bias.reshape(1, key_count), query_rows, out_grad, *parts)


def after(value, earlier):
    return lax.optimization_barrier((value, earlier))[0]


def inner_pairs(count, level):
    mask = (1 << level) | (1 << (level - 1))
    return [(b, b ^ mask) for b in range(count) if (b >> level & 1) != (b >> (level - 1) & 1)]


def outer_pairs(count, level):
    return [(b, b ^ (1 << (level - 1))) for b in range(count) if (b >> level & 1) != (b >> (level - 1) & 1)]


def placed_pool(rows_in, upper):
    run = rows_in // (POOLED // 2)
    out_row = lax.broadcasted_iota(jnp.int32, (POOLED, rows_in), 0)
    in_row = lax.broadcasted_iota(jnp.int32, (POOLED, rows_in), 1)
    offset = upper * (POOLED // 2)
    return jnp.where(out_row - offset == in_row // run, 1.0 / run, 0.0).astype(jnp.float32)


def apply(matrix, rows):
    return jnp.einsum(
        "pr,krw->kpw", matrix, rows.astype(jnp.float32), precision=lax.Precision.HIGHEST,
        preferred_element_type=jnp.float32,
    )


def body(query_rows, key_rows, value_rows, out_grad):
    leaf_rows, model_width = query_rows.shape
    seq_count = lax.axis_size("seq")
    levels = seq_count.bit_length() - 1
    position = lax.axis_index("seq")
    pool_ratio = leaf_rows // POOLED
    score_scale = HEAD_DIM ** (-0.5)
    chunk_width = model_width // CHUNKS
    bias_parts = [jnp.zeros((2 * leaf_rows,), jnp.float32)]
    for step_level in range(1, levels):
        bias_parts.append(jnp.full((POOLED,), math.log(pool_ratio * 2**step_level), jnp.float32))
    key_bias = jnp.concatenate(bias_parts, axis=0)
    bits = [position // 2**step_level % 2 for step_level in range(levels)]
    inner = [None] + [bits[s] != bits[s - 1] for s in range(1, levels)]
    mine = [placed_pool(leaf_rows if s == 0 else POOLED, bits[s]) for s in range(levels)]
    other = [placed_pool(leaf_rows if s == 0 else POOLED, 1 - bits[s]) for s in range(levels)]
    pool_own = placed_pool(leaf_rows, 0)[: POOLED // 2]
    own_pooled = jnp.stack([
        jnp.dot(pool_own.astype(jnp.bfloat16), rows, preferred_element_type=jnp.float32)
        for rows in (key_rows, value_rows)
    ])
    sibling_pooled = partner_2(own_pooled.astype(jnp.bfloat16), "seq", 0)
    pick_row = lax.broadcasted_iota(jnp.int32, (POOLED // 2, POOLED), 0)
    pick_col = lax.broadcasted_iota(jnp.int32, (POOLED // 2, POOLED), 1)
    pick_other = jnp.where(
        pick_col == pick_row + (1 - bits[0]) * (POOLED // 2), 1.0, 0.0
    ).astype(jnp.float32)
    spread_own = pool_own.T
    place_mine = placed_pool(POOLED // 2, bits[0])
    place_other = placed_pool(POOLED // 2, 1 - bits[0])
    pieces = [[], [], [], []]
    late = []
    for chunk in range(CHUNKS):
        columns = slice(chunk * chunk_width, (chunk + 1) * chunk_width)
        own = jnp.stack((key_rows[:, columns], value_rows[:, columns]))
        sibling = partner_2(after(own, sibling_pooled), "seq", 0)
        summary = apply(place_mine, own_pooled[:, :, columns]) + apply(
            place_other, sibling_pooled[:, :, columns]
        )
        far = []
        for step_level in range(1, levels):
            if step_level == 1:
                partner = partner_2(summary.astype(jnp.bfloat16), "seq", step_level)
            else:
                crossed = lax.ppermute(summary.astype(jnp.bfloat16), "seq", inner_pairs(seq_count, step_level))
                passed = lax.ppermute(crossed, "seq", outer_pairs(seq_count, step_level))
                partner = jnp.where(inner[step_level], crossed, passed)
            far.append(partner)
            if step_level + 1 < levels:
                summary = apply(mine[step_level], summary) + apply(other[step_level], partner)
        held = own
        if chunk >= 2:
            held = after(held, late[chunk - 2][1])
        if chunk >= 3:
            held = after(held, late[chunk - 3][0])
        outs = attention(
            query_rows, out_grad, [held, sibling] + far, key_bias, score_scale,
            chunk * (chunk_width // HEAD_DIM),
        )
        attended, query_grad, terms = outs[0], outs[1], outs[2:]
        grad = None
        sends = {}
        for step_level in reversed(range(1, levels)):
            outgoing = terms[1 + step_level]
            if grad is not None:
                outgoing = outgoing + apply(other[step_level].T, grad)
            sends[step_level] = outgoing.astype(jnp.bfloat16)
            if step_level == 1:
                returned = partner_2(sends[step_level], "seq", step_level)
            else:
                back = [(t, s) for s, t in outer_pairs(seq_count, step_level)]
                gathered = lax.ppermute(sends[step_level], "seq", back)
                total = outgoing + gathered.astype(jnp.float32)
                returned = lax.ppermute(total.astype(jnp.bfloat16), "seq", inner_pairs(seq_count, step_level))
            if grad is None:
                grad = returned.astype(jnp.float32)
            else:
                grad = apply(mine[step_level].T, grad) + returned
        to_sibling = terms[1]
        own_total = terms[0]
        split = chunk == CHUNKS - 1 and grad is not None
        if grad is not None:
            if not split:
                to_sibling = to_sibling + apply(other[0].T, grad)
            own_total = own_total + apply(mine[0].T, grad)
        sibling_send = to_sibling.astype(jnp.bfloat16)
        late.append((sibling_send, sends.get(1, sibling_send)))
        from_sibling = partner_2(sibling_send, "seq", 0)
        if split:
            pooled_back = partner_2(apply(pick_other, grad).astype(jnp.bfloat16), "seq", 0)
            own_total = own_total + apply(spread_own, pooled_back)
        totals = own_total + from_sibling.astype(jnp.float32)
        for slot, piece in enumerate((attended, query_grad, totals[0], totals[1])):
            pieces[slot].append(piece)
    return tuple(jnp.concatenate(p, axis=1).astype(jnp.bfloat16) for p in pieces)


def solution(mesh):
    spec = P(("batch", "seq"), None)
    return jax.shard_map(
        body, mesh=mesh, in_specs=(spec, spec, spec, spec), out_specs=(spec, spec, spec, spec),
        check_vma=False,
    )
```

```python
import functools
import math

import jax
import jax.numpy as jnp
from jax import lax
from jax.experimental import pallas as pl
from jax.sharding import PartitionSpec as P

HEAD_DIM = 128
POOLED = 128
CHUNKS = 4


def partner_2(block, axis, stride):
    count = lax.axis_size(axis)
    route = []
    for low in range(count):
        high = low | 1 << stride
        if high != low and high < count:
            route += [(low, high), (high, low)]
    return lax.ppermute(block, axis, route)


def attention_kernel(bias_ref, q_ref, do_ref, *refs, scale, parts):
    part_refs = refs[:parts]
    o_ref, dq_ref = refs[parts:parts + 2]
    grad_refs = refs[parts + 2:]
    q = q_ref[...]
    do = do_ref[...]
    k = jnp.concatenate([r[0] for r in part_refs], axis=0)
    v = jnp.concatenate([r[1] for r in part_refs], axis=0)
    scores = (
        lax.dot_general(q, k, (((1,), (1,)), ((), ())), preferred_element_type=jnp.float32) * scale
        + bias_ref[...]
    )
    row_max = jnp.max(scores, axis=-1, keepdims=True)
    shifted = jnp.exp(scores - row_max)
    weights = shifted * (1.0 / jnp.sum(shifted, axis=-1, keepdims=True))
    weights_low = weights.astype(jnp.bfloat16)
    attended = jnp.dot(weights_low, v, preferred_element_type=jnp.float32).astype(jnp.bfloat16)
    o_ref[...] = attended
    row_dot = jnp.sum(
        do.astype(jnp.float32) * attended.astype(jnp.float32), axis=-1, keepdims=True
    )
    weight_grad = lax.dot_general(do, v, (((1,), (1,)), ((), ())), preferred_element_type=jnp.float32)
    score_grad = (weights * (weight_grad - row_dot)).astype(jnp.bfloat16)
    dq_ref[...] = (
        jnp.dot(score_grad, k, preferred_element_type=jnp.float32) * scale
    ).astype(jnp.bfloat16)
    by_query = (((0,), (0,)), ((), ()))
    dk = lax.dot_general(score_grad, q, by_query, preferred_element_type=jnp.float32) * scale
    dv = lax.dot_general(weights_low, do, by_query, preferred_element_type=jnp.float32)
    first = 0
    for r in grad_refs:
        rows = r.shape[1]
        r[0] = dk[first:first + rows]
        r[1] = dv[first:first + rows]
        first += rows


def attention(query_rows, out_grad, parts, key_bias, score_scale, head_offset):
    leaf_rows = query_rows.shape[0]
    width = parts[0].shape[2]
    key_count = sum(p.shape[1] for p in parts)
    heads = width // HEAD_DIM
    row_in = pl.BlockSpec((leaf_rows, HEAD_DIM), lambda h: (0, h + head_offset))
    row_out = pl.BlockSpec((leaf_rows, HEAD_DIM), lambda h: (0, h))
    part_specs = [pl.BlockSpec((2, p.shape[1], HEAD_DIM), lambda h: (0, 0, h)) for p in parts]
    flops = 12 * leaf_rows * key_count * width
    io_bytes = 2 * (4 * leaf_rows + 2 * key_count) * width + 8 * key_count * width
    return pl.pallas_call(
        functools.partial(attention_kernel, scale=score_scale, parts=len(parts)),
        grid=(heads,),
        in_specs=[pl.BlockSpec((1, key_count), lambda h: (0, 0)), row_in, row_in] + part_specs,
        out_specs=[row_out, row_out] + part_specs,
        out_shape=[
            jax.ShapeDtypeStruct((leaf_rows, width), jnp.bfloat16),
            jax.ShapeDtypeStruct((leaf_rows, width), jnp.bfloat16),
        ] + [jax.ShapeDtypeStruct(p.shape, jnp.float32) for p in parts],
        cost_estimate=pl.CostEstimate(
            flops=flops, transcendentals=2 * leaf_rows * key_count * heads, bytes_accessed=io_bytes
        ),
    )(key_bias.reshape(1, key_count), query_rows, out_grad, *parts)


def after(value, earlier):
    return lax.optimization_barrier((value, earlier))[0]


def inner_pairs(count, level):
    mask = (1 << level) | (1 << (level - 1))
    return [(b, b ^ mask) for b in range(count) if (b >> level & 1) != (b >> (level - 1) & 1)]


def outer_pairs(count, level):
    return [(b, b ^ (1 << (level - 1))) for b in range(count) if (b >> level & 1) != (b >> (level - 1) & 1)]


def placed_pool(rows_in, upper):
    run = rows_in // (POOLED // 2)
    out_row = lax.broadcasted_iota(jnp.int32, (POOLED, rows_in), 0)
    in_row = lax.broadcasted_iota(jnp.int32, (POOLED, rows_in), 1)
    offset = upper * (POOLED // 2)
    return jnp.where(out_row - offset == in_row // run, 1.0 / run, 0.0).astype(jnp.float32)


def apply(matrix, rows):
    return jnp.einsum(
        "pr,krw->kpw", matrix, rows.astype(jnp.float32), precision=lax.Precision.HIGHEST,
        preferred_element_type=jnp.float32,
    )


def body(query_rows, key_rows, value_rows, out_grad):
    leaf_rows, model_width = query_rows.shape
    seq_count = lax.axis_size("seq")
    levels = seq_count.bit_length() - 1
    position = lax.axis_index("seq")
    pool_ratio = leaf_rows // POOLED
    score_scale = HEAD_DIM ** (-0.5)
    chunk_width = model_width // CHUNKS
    bias_parts = [jnp.zeros((2 * leaf_rows,), jnp.float32)]
    for step_level in range(1, levels):
        bias_parts.append(jnp.full((POOLED,), math.log(pool_ratio * 2**step_level), jnp.float32))
    key_bias = jnp.concatenate(bias_parts, axis=0)
    bits = [position // 2**step_level % 2 for step_level in range(levels)]
    inner = [None] + [bits[s] != bits[s - 1] for s in range(1, levels)]
    mine = [placed_pool(leaf_rows if s == 0 else POOLED, bits[s]) for s in range(levels)]
    other = [placed_pool(leaf_rows if s == 0 else POOLED, 1 - bits[s]) for s in range(levels)]
    pool_own = placed_pool(leaf_rows, 0)[: POOLED // 2]
    own_pooled = jnp.stack([
        jnp.dot(pool_own.astype(jnp.bfloat16), rows, preferred_element_type=jnp.float32)
        for rows in (key_rows, value_rows)
    ])
    sibling_pooled = partner_2(own_pooled.astype(jnp.bfloat16), "seq", 0)
    pick_row = lax.broadcasted_iota(jnp.int32, (POOLED // 2, POOLED), 0)
    pick_col = lax.broadcasted_iota(jnp.int32, (POOLED // 2, POOLED), 1)
    pick_other = jnp.where(
        pick_col == pick_row + (1 - bits[0]) * (POOLED // 2), 1.0, 0.0
    ).astype(jnp.float32)
    spread_own = pool_own.T
    place_mine = placed_pool(POOLED // 2, bits[0])
    place_other = placed_pool(POOLED // 2, 1 - bits[0])
    pieces = [[], []]
    grads_out = [jnp.zeros((leaf_rows, model_width), jnp.bfloat16) for _ in range(2)]
    late = []
    for chunk in range(CHUNKS):
        columns = slice(chunk * chunk_width, (chunk + 1) * chunk_width)
        own = jnp.stack((key_rows[:, columns], value_rows[:, columns]))
        sibling = partner_2(after(own, sibling_pooled), "seq", 0)
        summary = apply(place_mine, own_pooled[:, :, columns]) + apply(
            place_other, sibling_pooled[:, :, columns]
        )
        far = []
        for step_level in range(1, levels):
            if step_level == 1:
                partner = partner_2(summary.astype(jnp.bfloat16), "seq", step_level)
            else:
                crossed = lax.ppermute(summary.astype(jnp.bfloat16), "seq", inner_pairs(seq_count, step_level))
                passed = lax.ppermute(crossed, "seq", outer_pairs(seq_count, step_level))
                partner = jnp.where(inner[step_level], crossed, passed)
            far.append(partner)
            if step_level + 1 < levels:
                summary = apply(mine[step_level], summary) + apply(other[step_level], partner)
        held = own
        if chunk >= 2:
            held = after(held, late[chunk - 2][1])
        if chunk >= 3:
            held = after(held, late[chunk - 3][0])
        outs = attention(
            query_rows, out_grad, [held, sibling] + far, key_bias, score_scale,
            chunk * (chunk_width // HEAD_DIM),
        )
        attended, query_grad, terms = outs[0], outs[1], outs[2:]
        grad = None
        sends = {}
        for step_level in reversed(range(1, levels)):
            outgoing = terms[1 + step_level]
            if grad is not None:
                outgoing = outgoing + apply(other[step_level].T, grad)
            sends[step_level] = outgoing.astype(jnp.bfloat16)
            if step_level == 1:
                returned = partner_2(sends[step_level], "seq", step_level)
            else:
                back = [(t, s) for s, t in outer_pairs(seq_count, step_level)]
                gathered = lax.ppermute(sends[step_level], "seq", back)
                total = outgoing + gathered.astype(jnp.float32)
                returned = lax.ppermute(total.astype(jnp.bfloat16), "seq", inner_pairs(seq_count, step_level))
            if grad is None:
                grad = returned.astype(jnp.float32)
            else:
                grad = apply(mine[step_level].T, grad) + returned
        to_sibling = terms[1]
        own_total = terms[0]
        split = chunk == CHUNKS - 1 and grad is not None
        if grad is not None:
            if not split:
                to_sibling = to_sibling + apply(other[0].T, grad)
            own_total = own_total + apply(mine[0].T, grad)
        sibling_send = to_sibling.astype(jnp.bfloat16)
        late.append((sibling_send, sends.get(1, sibling_send)))
        from_sibling = partner_2(sibling_send, "seq", 0)
        if split:
            pooled_back = partner_2(apply(pick_other, grad).astype(jnp.bfloat16), "seq", 0)
            own_total = own_total + apply(spread_own, pooled_back)
        totals = own_total + from_sibling.astype(jnp.float32)
        for slot, piece in enumerate((attended, query_grad)):
            pieces[slot].append(piece)
        for slot in range(2):
            grads_out[slot] = lax.dynamic_update_slice(
                grads_out[slot], totals[slot].astype(jnp.bfloat16), (0, columns.start)
            )
    return tuple(jnp.concatenate(p, axis=1) for p in pieces[:2]) + tuple(grads_out)


def solution(mesh):
    spec = P(("batch", "seq"), None)
    return jax.shard_map(
        body, mesh=mesh, in_specs=(spec, spec, spec, spec), out_specs=(spec, spec, spec, spec),
        check_vma=False,
    )
```

```python
import functools
import math

import jax
import jax.numpy as jnp
from jax import lax
from jax.experimental import pallas as pl
from jax.sharding import PartitionSpec as P

HEAD_DIM = 128
POOLED = 128
CHUNKS = 4


def partner_2(block, axis, stride):
    count = lax.axis_size(axis)
    route = []
    for low in range(count):
        high = low | 1 << stride
        if high != low and high < count:
            route += [(low, high), (high, low)]
    return lax.ppermute(block, axis, route)


def attention_kernel(bias_ref, q_ref, do_ref, *refs, scale, parts):
    part_refs = refs[:parts]
    o_ref, dq_ref = refs[parts:parts + 2]
    grad_refs = refs[parts + 2:]
    for head in range(q_ref.shape[1] // HEAD_DIM):
        cols = slice(head * HEAD_DIM, (head + 1) * HEAD_DIM)
        head_block(bias_ref, q_ref, do_ref, part_refs, o_ref, dq_ref, grad_refs, cols, scale)


def head_block(bias_ref, q_ref, do_ref, part_refs, o_ref, dq_ref, grad_refs, cols, scale):
    q = q_ref[:, cols]
    do = do_ref[:, cols]
    k = jnp.concatenate([r[0, :, cols] for r in part_refs], axis=0)
    v = jnp.concatenate([r[1, :, cols] for r in part_refs], axis=0)
    scores = (
        lax.dot_general(q, k, (((1,), (1,)), ((), ())), preferred_element_type=jnp.float32) * scale
        + bias_ref[...]
    )
    row_max = jnp.max(scores, axis=-1, keepdims=True)
    shifted = jnp.exp(scores - row_max)
    weights = shifted * (1.0 / jnp.sum(shifted, axis=-1, keepdims=True))
    weights_low = weights.astype(jnp.bfloat16)
    attended = jnp.dot(weights_low, v, preferred_element_type=jnp.float32).astype(jnp.bfloat16)
    o_ref[:, cols] = attended
    row_dot = jnp.sum(
        do.astype(jnp.float32) * attended.astype(jnp.float32), axis=-1, keepdims=True
    )
    weight_grad = lax.dot_general(do, v, (((1,), (1,)), ((), ())), preferred_element_type=jnp.float32)
    score_grad = (weights * (weight_grad - row_dot)).astype(jnp.bfloat16)
    dq_ref[:, cols] = (
        jnp.dot(score_grad, k, preferred_element_type=jnp.float32) * scale
    ).astype(jnp.bfloat16)
    by_query = (((0,), (0,)), ((), ()))
    dk = lax.dot_general(score_grad, q, by_query, preferred_element_type=jnp.float32) * scale
    dv = lax.dot_general(weights_low, do, by_query, preferred_element_type=jnp.float32)
    first = 0
    for r in grad_refs:
        rows = r.shape[1]
        r[0, :, cols] = dk[first:first + rows]
        r[1, :, cols] = dv[first:first + rows]
        first += rows


def attention(query_rows, out_grad, parts, key_bias, score_scale, head_offset):
    leaf_rows = query_rows.shape[0]
    width = parts[0].shape[2]
    key_count = sum(p.shape[1] for p in parts)
    heads = width // HEAD_DIM
    step = HEAD_DIM * (2 if heads % 2 == 0 and head_offset % 2 == 0 else 1)
    row_in = pl.BlockSpec((leaf_rows, step), lambda h: (0, h + head_offset * HEAD_DIM // step))
    row_out = pl.BlockSpec((leaf_rows, step), lambda h: (0, h))
    part_specs = [pl.BlockSpec((2, p.shape[1], step), lambda h: (0, 0, h)) for p in parts]
    flops = 12 * leaf_rows * key_count * width
    io_bytes = 2 * (4 * leaf_rows + 2 * key_count) * width + 8 * key_count * width
    return pl.pallas_call(
        functools.partial(attention_kernel, scale=score_scale, parts=len(parts)),
        grid=(width // step,),
        in_specs=[pl.BlockSpec((1, key_count), lambda h: (0, 0)), row_in, row_in] + part_specs,
        out_specs=[row_out, row_out] + part_specs,
        out_shape=[
            jax.ShapeDtypeStruct((leaf_rows, width), jnp.bfloat16),
            jax.ShapeDtypeStruct((leaf_rows, width), jnp.bfloat16),
        ] + [jax.ShapeDtypeStruct(p.shape, jnp.float32) for p in parts],
        cost_estimate=pl.CostEstimate(
            flops=flops, transcendentals=2 * leaf_rows * key_count * heads, bytes_accessed=io_bytes
        ),
    )(key_bias.reshape(1, key_count), query_rows, out_grad, *parts)


def after(value, earlier):
    return lax.optimization_barrier((value, earlier))[0]


def inner_pairs(count, level):
    mask = (1 << level) | (1 << (level - 1))
    return [(b, b ^ mask) for b in range(count) if (b >> level & 1) != (b >> (level - 1) & 1)]


def outer_pairs(count, level):
    return [(b, b ^ (1 << (level - 1))) for b in range(count) if (b >> level & 1) != (b >> (level - 1) & 1)]


def placed_pool(rows_in, upper):
    run = rows_in // (POOLED // 2)
    out_row = lax.broadcasted_iota(jnp.int32, (POOLED, rows_in), 0)
    in_row = lax.broadcasted_iota(jnp.int32, (POOLED, rows_in), 1)
    offset = upper * (POOLED // 2)
    return jnp.where(out_row - offset == in_row // run, 1.0 / run, 0.0).astype(jnp.float32)


def apply(matrix, rows):
    return jnp.einsum(
        "pr,krw->kpw", matrix, rows.astype(jnp.float32), precision=lax.Precision.HIGHEST,
        preferred_element_type=jnp.float32,
    )


def body(query_rows, key_rows, value_rows, out_grad):
    leaf_rows, model_width = query_rows.shape
    seq_count = lax.axis_size("seq")
    levels = seq_count.bit_length() - 1
    position = lax.axis_index("seq")
    pool_ratio = leaf_rows // POOLED
    score_scale = HEAD_DIM ** (-0.5)
    chunk_width = model_width // CHUNKS
    bias_parts = [jnp.zeros((2 * leaf_rows,), jnp.float32)]
    for step_level in range(1, levels):
        bias_parts.append(jnp.full((POOLED,), math.log(pool_ratio * 2**step_level), jnp.float32))
    key_bias = jnp.concatenate(bias_parts, axis=0)
    bits = [position // 2**step_level % 2 for step_level in range(levels)]
    inner = [None] + [bits[s] != bits[s - 1] for s in range(1, levels)]
    mine = [placed_pool(leaf_rows if s == 0 else POOLED, bits[s]) for s in range(levels)]
    other = [placed_pool(leaf_rows if s == 0 else POOLED, 1 - bits[s]) for s in range(levels)]
    pool_own = placed_pool(leaf_rows, 0)[: POOLED // 2]
    own_pooled = jnp.stack([
        jnp.dot(pool_own.astype(jnp.bfloat16), rows, preferred_element_type=jnp.float32)
        for rows in (key_rows, value_rows)
    ])
    sibling_pooled = partner_2(own_pooled.astype(jnp.bfloat16), "seq", 0)
    pick_row = lax.broadcasted_iota(jnp.int32, (POOLED // 2, POOLED), 0)
    pick_col = lax.broadcasted_iota(jnp.int32, (POOLED // 2, POOLED), 1)
    pick_other = jnp.where(
        pick_col == pick_row + (1 - bits[0]) * (POOLED // 2), 1.0, 0.0
    ).astype(jnp.float32)
    spread_own = pool_own.T
    place_mine = placed_pool(POOLED // 2, bits[0])
    place_other = placed_pool(POOLED // 2, 1 - bits[0])
    pieces = [[], []]
    grads_out = [jnp.zeros((leaf_rows, model_width), jnp.bfloat16) for _ in range(2)]
    late = []
    for chunk in range(CHUNKS):
        columns = slice(chunk * chunk_width, (chunk + 1) * chunk_width)
        own = jnp.stack((key_rows[:, columns], value_rows[:, columns]))
        sibling = partner_2(after(own, sibling_pooled), "seq", 0)
        summary = apply(place_mine, own_pooled[:, :, columns]) + apply(
            place_other, sibling_pooled[:, :, columns]
        )
        far = []
        for step_level in range(1, levels):
            if step_level == 1:
                partner = partner_2(summary.astype(jnp.bfloat16), "seq", step_level)
            else:
                crossed = lax.ppermute(summary.astype(jnp.bfloat16), "seq", inner_pairs(seq_count, step_level))
                passed = lax.ppermute(crossed, "seq", outer_pairs(seq_count, step_level))
                partner = jnp.where(inner[step_level], crossed, passed)
            far.append(partner)
            if step_level + 1 < levels:
                summary = apply(mine[step_level], summary) + apply(other[step_level], partner)
        held = own
        if chunk >= 2:
            held = after(held, late[chunk - 2][1])
        if chunk >= 3:
            held = after(held, late[chunk - 3][0])
        outs = attention(
            query_rows, out_grad, [held, sibling] + far, key_bias, score_scale,
            chunk * (chunk_width // HEAD_DIM),
        )
        attended, query_grad, terms = outs[0], outs[1], outs[2:]
        grad = None
        sends = {}
        for step_level in reversed(range(1, levels)):
            outgoing = terms[1 + step_level]
            if grad is not None:
                outgoing = outgoing + apply(other[step_level].T, grad)
            sends[step_level] = outgoing.astype(jnp.bfloat16)
            if step_level == 1:
                returned = partner_2(sends[step_level], "seq", step_level)
            else:
                back = [(t, s) for s, t in outer_pairs(seq_count, step_level)]
                gathered = lax.ppermute(sends[step_level], "seq", back)
                total = outgoing + gathered.astype(jnp.float32)
                returned = lax.ppermute(total.astype(jnp.bfloat16), "seq", inner_pairs(seq_count, step_level))
            if grad is None:
                grad = returned.astype(jnp.float32)
            else:
                grad = apply(mine[step_level].T, grad) + returned
        to_sibling = terms[1]
        own_total = terms[0]
        split = chunk == CHUNKS - 1 and grad is not None
        if grad is not None:
            if not split:
                to_sibling = to_sibling + apply(other[0].T, grad)
            own_total = own_total + apply(mine[0].T, grad)
        sibling_send = to_sibling.astype(jnp.bfloat16)
        late.append((sibling_send, sends.get(1, sibling_send)))
        from_sibling = partner_2(sibling_send, "seq", 0)
        if split:
            pooled_back = partner_2(apply(pick_other, grad).astype(jnp.bfloat16), "seq", 0)
            own_total = own_total + apply(spread_own, pooled_back)
        totals = own_total + from_sibling.astype(jnp.float32)
        for slot, piece in enumerate((attended, query_grad)):
            pieces[slot].append(piece)
        for slot in range(2):
            grads_out[slot] = lax.dynamic_update_slice(
                grads_out[slot], totals[slot].astype(jnp.bfloat16), (0, columns.start)
            )
    return tuple(jnp.concatenate(p, axis=1) for p in pieces[:2]) + tuple(grads_out)


def solution(mesh):
    spec = P(("batch", "seq"), None)
    return jax.shard_map(
        body, mesh=mesh, in_specs=(spec, spec, spec, spec), out_specs=(spec, spec, spec, spec),
        check_vma=False,
    )
```

```python
import functools
import math

import jax
import jax.numpy as jnp
from jax import lax
from jax.experimental import pallas as pl
from jax.sharding import PartitionSpec as P

HEAD_DIM = 128
POOLED = 128
CHUNKS = 4


def partner_2(block, axis, stride):
    count = lax.axis_size(axis)
    route = []
    for low in range(count):
        high = low | 1 << stride
        if high != low and high < count:
            route += [(low, high), (high, low)]
    return lax.ppermute(block, axis, route)


def attention_kernel(bias_ref, q_ref, do_ref, *refs, scale, parts):
    part_refs = refs[:parts]
    o_ref, dq_ref = refs[parts:parts + 2]
    grad_refs = refs[parts + 2:]
    q = q_ref[...]
    do = do_ref[...]
    k = jnp.concatenate([r[0] for r in part_refs], axis=0)
    v = jnp.concatenate([r[1] for r in part_refs], axis=0)
    scores = (
        lax.dot_general(q, k, (((1,), (1,)), ((), ())), preferred_element_type=jnp.float32) * scale
        + bias_ref[...]
    )
    row_max = jnp.max(scores, axis=-1, keepdims=True)
    shifted = jnp.exp(scores - row_max)
    weights = shifted * (1.0 / jnp.sum(shifted, axis=-1, keepdims=True))
    weights_low = weights.astype(jnp.bfloat16)
    attended = jnp.dot(weights_low, v, preferred_element_type=jnp.float32).astype(jnp.bfloat16)
    o_ref[...] = attended
    row_dot = jnp.sum(
        do.astype(jnp.float32) * attended.astype(jnp.float32), axis=-1, keepdims=True
    )
    weight_grad = lax.dot_general(do, v, (((1,), (1,)), ((), ())), preferred_element_type=jnp.float32)
    score_grad = (weights * (weight_grad - row_dot)).astype(jnp.bfloat16)
    dq_ref[...] = (
        jnp.dot(score_grad, k, preferred_element_type=jnp.float32) * scale
    ).astype(jnp.bfloat16)
    by_query = (((0,), (0,)), ((), ()))
    dk = lax.dot_general(score_grad, q, by_query, preferred_element_type=jnp.float32) * scale
    dv = lax.dot_general(weights_low, do, by_query, preferred_element_type=jnp.float32)
    first = 0
    for r in grad_refs:
        rows = r.shape[1]
        r[0] = dk[first:first + rows]
        r[1] = dv[first:first + rows]
        first += rows


def attention(query_rows, out_grad, parts, key_bias, score_scale, head_offset):
    leaf_rows = query_rows.shape[0]
    width = parts[0].shape[2]
    key_count = sum(p.shape[1] for p in parts)
    heads = width // HEAD_DIM
    row_in = pl.BlockSpec((leaf_rows, HEAD_DIM), lambda h: (0, h + head_offset))
    row_out = pl.BlockSpec((leaf_rows, HEAD_DIM), lambda h: (0, h))
    part_specs = [pl.BlockSpec((2, p.shape[1], HEAD_DIM), lambda h: (0, 0, h)) for p in parts]
    flops = 12 * leaf_rows * key_count * width
    io_bytes = 2 * (4 * leaf_rows + 2 * key_count) * width + 8 * key_count * width
    return pl.pallas_call(
        functools.partial(attention_kernel, scale=score_scale, parts=len(parts)),
        grid=(heads,),
        in_specs=[pl.BlockSpec((1, key_count), lambda h: (0, 0)), row_in, row_in] + part_specs,
        out_specs=[row_out, row_out] + part_specs,
        out_shape=[
            jax.ShapeDtypeStruct((leaf_rows, width), jnp.bfloat16),
            jax.ShapeDtypeStruct((leaf_rows, width), jnp.bfloat16),
        ] + [jax.ShapeDtypeStruct(p.shape, jnp.float32) for p in parts],
        cost_estimate=pl.CostEstimate(
            flops=flops, transcendentals=2 * leaf_rows * key_count * heads, bytes_accessed=io_bytes
        ),
    )(key_bias.reshape(1, key_count), query_rows, out_grad, *parts)


def after(value, earlier):
    return lax.optimization_barrier((value, earlier))[0]


def inner_pairs(count, level):
    mask = (1 << level) | (1 << (level - 1))
    return [(b, b ^ mask) for b in range(count) if (b >> level & 1) != (b >> (level - 1) & 1)]


def outer_pairs(count, level):
    return [(b, b ^ (1 << (level - 1))) for b in range(count) if (b >> level & 1) != (b >> (level - 1) & 1)]


def placed_pool(rows_in, upper):
    run = rows_in // (POOLED // 2)
    out_row = lax.broadcasted_iota(jnp.int32, (POOLED, rows_in), 0)
    in_row = lax.broadcasted_iota(jnp.int32, (POOLED, rows_in), 1)
    offset = upper * (POOLED // 2)
    return jnp.where(out_row - offset == in_row // run, 1.0 / run, 0.0).astype(jnp.float32)


def apply(matrix, rows):
    return jnp.einsum(
        "pr,krw->kpw", matrix, rows.astype(jnp.float32), precision=lax.Precision.HIGHEST,
        preferred_element_type=jnp.float32,
    )


def body(query_rows, key_rows, value_rows, out_grad):
    leaf_rows, model_width = query_rows.shape
    seq_count = lax.axis_size("seq")
    levels = seq_count.bit_length() - 1
    position = lax.axis_index("seq")
    pool_ratio = leaf_rows // POOLED
    score_scale = HEAD_DIM ** (-0.5)
    chunk_width = model_width // CHUNKS
    bias_parts = [jnp.zeros((2 * leaf_rows,), jnp.float32)]
    for step_level in range(1, levels):
        bias_parts.append(jnp.full((POOLED,), math.log(pool_ratio * 2**step_level), jnp.float32))
    key_bias = jnp.concatenate(bias_parts, axis=0)
    bits = [position // 2**step_level % 2 for step_level in range(levels)]
    inner = [None] + [bits[s] != bits[s - 1] for s in range(1, levels)]
    mine = [placed_pool(leaf_rows if s == 0 else POOLED, bits[s]) for s in range(levels)]
    other = [placed_pool(leaf_rows if s == 0 else POOLED, 1 - bits[s]) for s in range(levels)]
    pool_own = placed_pool(leaf_rows, 0)[: POOLED // 2]
    own_pooled = jnp.stack([
        jnp.dot(pool_own.astype(jnp.bfloat16), rows, preferred_element_type=jnp.float32)
        for rows in (key_rows, value_rows)
    ])
    sibling_pooled = partner_2(own_pooled.astype(jnp.bfloat16), "seq", 0)
    pick_row = lax.broadcasted_iota(jnp.int32, (POOLED // 2, POOLED), 0)
    pick_col = lax.broadcasted_iota(jnp.int32, (POOLED // 2, POOLED), 1)
    pick_other = jnp.where(
        pick_col == pick_row + (1 - bits[0]) * (POOLED // 2), 1.0, 0.0
    ).astype(jnp.float32)
    spread_own = pool_own.T
    place_mine = placed_pool(POOLED // 2, bits[0])
    place_other = placed_pool(POOLED // 2, 1 - bits[0])
    pieces = [[], []]
    grads_out = [jnp.zeros((leaf_rows, model_width), jnp.bfloat16) for _ in range(2)]
    late = []
    for chunk in range(CHUNKS):
        columns = slice(chunk * chunk_width, (chunk + 1) * chunk_width)
        own = jnp.stack((key_rows[:, columns], value_rows[:, columns]))
        sibling = partner_2(after(own, sibling_pooled), "seq", 0)
        summary = apply(place_mine, own_pooled[:, :, columns]) + apply(
            place_other, sibling_pooled[:, :, columns]
        )
        far = []
        for step_level in range(1, levels):
            if step_level == 1:
                partner = partner_2(summary.astype(jnp.bfloat16), "seq", step_level)
            else:
                crossed = lax.ppermute(summary.astype(jnp.bfloat16), "seq", inner_pairs(seq_count, step_level))
                passed = lax.ppermute(crossed, "seq", outer_pairs(seq_count, step_level))
                partner = jnp.where(inner[step_level], crossed, passed)
            far.append(partner)
            if step_level + 1 < levels:
                summary = apply(mine[step_level], summary) + apply(other[step_level], partner)
        held = own
        if chunk >= 2:
            held = after(held, late[chunk - 2][1])
        outs = attention(
            query_rows, out_grad, [held, sibling] + far, key_bias, score_scale,
            chunk * (chunk_width // HEAD_DIM),
        )
        attended, query_grad, terms = outs[0], outs[1], outs[2:]
        grad = None
        sends = {}
        for step_level in reversed(range(1, levels)):
            outgoing = terms[1 + step_level]
            if grad is not None:
                outgoing = outgoing + apply(other[step_level].T, grad)
            sends[step_level] = outgoing.astype(jnp.bfloat16)
            if step_level == 1:
                returned = partner_2(sends[step_level], "seq", step_level)
            else:
                back = [(t, s) for s, t in outer_pairs(seq_count, step_level)]
                gathered = lax.ppermute(sends[step_level], "seq", back)
                total = outgoing + gathered.astype(jnp.float32)
                returned = lax.ppermute(total.astype(jnp.bfloat16), "seq", inner_pairs(seq_count, step_level))
            if grad is None:
                grad = returned.astype(jnp.float32)
            else:
                grad = apply(mine[step_level].T, grad) + returned
        to_sibling = terms[1]
        own_total = terms[0]
        split = chunk == CHUNKS - 1 and grad is not None
        if grad is not None:
            if not split:
                to_sibling = to_sibling + apply(other[0].T, grad)
            own_total = own_total + apply(mine[0].T, grad)
        sibling_send = to_sibling.astype(jnp.bfloat16)
        late.append((sibling_send, sends.get(1, sibling_send)))
        from_sibling = partner_2(sibling_send, "seq", 0)
        if split:
            pooled_back = partner_2(apply(pick_other, grad).astype(jnp.bfloat16), "seq", 0)
            own_total = own_total + apply(spread_own, pooled_back)
        totals = own_total + from_sibling.astype(jnp.float32)
        for slot, piece in enumerate((attended, query_grad)):
            pieces[slot].append(piece)
        for slot in range(2):
            grads_out[slot] = lax.dynamic_update_slice(
                grads_out[slot], totals[slot].astype(jnp.bfloat16), (0, columns.start)
            )
    return tuple(jnp.concatenate(p, axis=1) for p in pieces[:2]) + tuple(grads_out)


def solution(mesh):
    spec = P(("batch", "seq"), None)
    return jax.shard_map(
        body, mesh=mesh, in_specs=(spec, spec, spec, spec), out_specs=(spec, spec, spec, spec),
        check_vma=False,
    )
```

```python
import functools
import math

import jax
import jax.numpy as jnp
from jax import lax
from jax.experimental import pallas as pl
from jax.sharding import PartitionSpec as P

HEAD_DIM = 128
POOLED = 128
CHUNKS = 4


def partner_2(block, axis, stride):
    count = lax.axis_size(axis)
    route = []
    for low in range(count):
        high = low | 1 << stride
        if high != low and high < count:
            route += [(low, high), (high, low)]
    return lax.ppermute(block, axis, route)


def attention_kernel(bias_ref, q_ref, do_ref, *refs, scale, parts):
    part_refs = refs[:parts]
    o_ref, dq_ref = refs[parts:parts + 2]
    grad_refs = refs[parts + 2:]
    q = q_ref[...]
    do = do_ref[...]
    k = jnp.concatenate([r[0] for r in part_refs], axis=0)
    v = jnp.concatenate([r[1] for r in part_refs], axis=0)
    scores = (
        lax.dot_general(q, k, (((1,), (1,)), ((), ())), preferred_element_type=jnp.float32) * scale
        + bias_ref[...]
    )
    row_max = jnp.max(scores, axis=-1, keepdims=True)
    shifted = jnp.exp(scores - row_max)
    weights = shifted * (1.0 / jnp.sum(shifted, axis=-1, keepdims=True))
    weights_low = weights.astype(jnp.bfloat16)
    attended = jnp.dot(weights_low, v, preferred_element_type=jnp.float32).astype(jnp.bfloat16)
    o_ref[...] = attended
    row_dot = jnp.sum(
        do.astype(jnp.float32) * attended.astype(jnp.float32), axis=-1, keepdims=True
    )
    weight_grad = lax.dot_general(do, v, (((1,), (1,)), ((), ())), preferred_element_type=jnp.float32)
    score_grad = (weights * (weight_grad - row_dot)).astype(jnp.bfloat16)
    dq_ref[...] = (
        jnp.dot(score_grad, k, preferred_element_type=jnp.float32) * scale
    ).astype(jnp.bfloat16)
    by_query = (((0,), (0,)), ((), ()))
    dk = lax.dot_general(score_grad, q, by_query, preferred_element_type=jnp.float32) * scale
    dv = lax.dot_general(weights_low, do, by_query, preferred_element_type=jnp.float32)
    first = 0
    for r in grad_refs:
        rows = r.shape[1]
        r[0] = dk[first:first + rows]
        r[1] = dv[first:first + rows]
        first += rows


def attention(query_rows, out_grad, parts, key_bias, score_scale, head_offset):
    leaf_rows = query_rows.shape[0]
    width = parts[0].shape[2]
    key_count = sum(p.shape[1] for p in parts)
    heads = width // HEAD_DIM
    row_in = pl.BlockSpec((leaf_rows, HEAD_DIM), lambda h: (0, h + head_offset))
    row_out = pl.BlockSpec((leaf_rows, HEAD_DIM), lambda h: (0, h))
    part_specs = [pl.BlockSpec((2, p.shape[1], HEAD_DIM), lambda h: (0, 0, h)) for p in parts]
    flops = 12 * leaf_rows * key_count * width
    io_bytes = 2 * (4 * leaf_rows + 2 * key_count) * width + 8 * key_count * width
    return pl.pallas_call(
        functools.partial(attention_kernel, scale=score_scale, parts=len(parts)),
        grid=(heads,),
        in_specs=[pl.BlockSpec((1, key_count), lambda h: (0, 0)), row_in, row_in] + part_specs,
        out_specs=[row_out, row_out] + part_specs,
        out_shape=[
            jax.ShapeDtypeStruct((leaf_rows, width), jnp.bfloat16),
            jax.ShapeDtypeStruct((leaf_rows, width), jnp.bfloat16),
        ] + [jax.ShapeDtypeStruct(p.shape, jnp.float32) for p in parts],
        cost_estimate=pl.CostEstimate(
            flops=flops, transcendentals=2 * leaf_rows * key_count * heads, bytes_accessed=io_bytes
        ),
    )(key_bias.reshape(1, key_count), query_rows, out_grad, *parts)


def after(value, earlier):
    return lax.optimization_barrier((value, earlier))[0]


def inner_pairs(count, level):
    mask = (1 << level) | (1 << (level - 1))
    return [(b, b ^ mask) for b in range(count) if (b >> level & 1) != (b >> (level - 1) & 1)]


def outer_pairs(count, level):
    return [(b, b ^ (1 << (level - 1))) for b in range(count) if (b >> level & 1) != (b >> (level - 1) & 1)]


def placed_pool(rows_in, upper):
    run = rows_in // (POOLED // 2)
    out_row = lax.broadcasted_iota(jnp.int32, (POOLED, rows_in), 0)
    in_row = lax.broadcasted_iota(jnp.int32, (POOLED, rows_in), 1)
    offset = upper * (POOLED // 2)
    return jnp.where(out_row - offset == in_row // run, 1.0 / run, 0.0).astype(jnp.float32)


def apply(matrix, rows):
    return jnp.einsum(
        "pr,krw->kpw", matrix, rows.astype(jnp.float32), precision=lax.Precision.HIGH,
        preferred_element_type=jnp.float32,
    )


def body(query_rows, key_rows, value_rows, out_grad):
    leaf_rows, model_width = query_rows.shape
    seq_count = lax.axis_size("seq")
    levels = seq_count.bit_length() - 1
    position = lax.axis_index("seq")
    pool_ratio = leaf_rows // POOLED
    score_scale = HEAD_DIM ** (-0.5)
    chunk_width = model_width // CHUNKS
    bias_parts = [jnp.zeros((2 * leaf_rows,), jnp.float32)]
    for step_level in range(1, levels):
        bias_parts.append(jnp.full((POOLED,), math.log(pool_ratio * 2**step_level), jnp.float32))
    key_bias = jnp.concatenate(bias_parts, axis=0)
    bits = [position // 2**step_level % 2 for step_level in range(levels)]
    inner = [None] + [bits[s] != bits[s - 1] for s in range(1, levels)]
    mine = [placed_pool(leaf_rows if s == 0 else POOLED, bits[s]) for s in range(levels)]
    other = [placed_pool(leaf_rows if s == 0 else POOLED, 1 - bits[s]) for s in range(levels)]
    pool_own = placed_pool(leaf_rows, 0)[: POOLED // 2]
    own_pooled = jnp.stack([
        jnp.dot(pool_own.astype(jnp.bfloat16), rows, preferred_element_type=jnp.float32)
        for rows in (key_rows, value_rows)
    ])
    sibling_pooled = partner_2(own_pooled.astype(jnp.bfloat16), "seq", 0)
    pick_row = lax.broadcasted_iota(jnp.int32, (POOLED // 2, POOLED), 0)
    pick_col = lax.broadcasted_iota(jnp.int32, (POOLED // 2, POOLED), 1)
    pick_other = jnp.where(
        pick_col == pick_row + (1 - bits[0]) * (POOLED // 2), 1.0, 0.0
    ).astype(jnp.float32)
    spread_own = pool_own.T
    place_mine = placed_pool(POOLED // 2, bits[0])
    place_other = placed_pool(POOLED // 2, 1 - bits[0])
    pieces = [[], []]
    grads_out = [jnp.zeros((leaf_rows, model_width), jnp.bfloat16) for _ in range(2)]
    late = []
    for chunk in range(CHUNKS):
        columns = slice(chunk * chunk_width, (chunk + 1) * chunk_width)
        own = jnp.stack((key_rows[:, columns], value_rows[:, columns]))
        sibling = partner_2(after(own, sibling_pooled), "seq", 0)
        summary = apply(place_mine, own_pooled[:, :, columns]) + apply(
            place_other, sibling_pooled[:, :, columns]
        )
        far = []
        for step_level in range(1, levels):
            if step_level == 1:
                partner = partner_2(summary.astype(jnp.bfloat16), "seq", step_level)
            else:
                crossed = lax.ppermute(summary.astype(jnp.bfloat16), "seq", inner_pairs(seq_count, step_level))
                passed = lax.ppermute(crossed, "seq", outer_pairs(seq_count, step_level))
                partner = jnp.where(inner[step_level], crossed, passed)
            far.append(partner)
            if step_level + 1 < levels:
                summary = apply(mine[step_level], summary) + apply(other[step_level], partner)
        held = own
        if chunk >= 2:
            held = after(held, late[chunk - 2][1])
        if chunk >= 3:
            held = after(held, late[chunk - 3][0])
        outs = attention(
            query_rows, out_grad, [held, sibling] + far, key_bias, score_scale,
            chunk * (chunk_width // HEAD_DIM),
        )
        attended, query_grad, terms = outs[0], outs[1], outs[2:]
        grad = None
        sends = {}
        for step_level in reversed(range(1, levels)):
            outgoing = terms[1 + step_level]
            if grad is not None:
                outgoing = outgoing + apply(other[step_level].T, grad)
            sends[step_level] = outgoing.astype(jnp.bfloat16)
            if step_level == 1:
                returned = partner_2(sends[step_level], "seq", step_level)
            else:
                back = [(t, s) for s, t in outer_pairs(seq_count, step_level)]
                gathered = lax.ppermute(sends[step_level], "seq", back)
                total = outgoing + gathered.astype(jnp.float32)
                returned = lax.ppermute(total.astype(jnp.bfloat16), "seq", inner_pairs(seq_count, step_level))
            if grad is None:
                grad = returned.astype(jnp.float32)
            else:
                grad = apply(mine[step_level].T, grad) + returned
        to_sibling = terms[1]
        own_total = terms[0]
        split = chunk == CHUNKS - 1 and grad is not None
        if grad is not None:
            if not split:
                to_sibling = to_sibling + apply(other[0].T, grad)
            own_total = own_total + apply(mine[0].T, grad)
        sibling_send = to_sibling.astype(jnp.bfloat16)
        late.append((sibling_send, sends.get(1, sibling_send)))
        from_sibling = partner_2(sibling_send, "seq", 0)
        if split:
            pooled_back = partner_2(apply(pick_other, grad).astype(jnp.bfloat16), "seq", 0)
            own_total = own_total + apply(spread_own, pooled_back)
        totals = own_total + from_sibling.astype(jnp.float32)
        for slot, piece in enumerate((attended, query_grad)):
            pieces[slot].append(piece)
        for slot in range(2):
            grads_out[slot] = lax.dynamic_update_slice(
                grads_out[slot], totals[slot].astype(jnp.bfloat16), (0, columns.start)
            )
    return tuple(jnp.concatenate(p, axis=1) for p in pieces[:2]) + tuple(grads_out)


def solution(mesh):
    spec = P(("batch", "seq"), None)
    return jax.shard_map(
        body, mesh=mesh, in_specs=(spec, spec, spec, spec), out_specs=(spec, spec, spec, spec),
        check_vma=False,
    )
```

```python
import functools
import math

import jax
import jax.numpy as jnp
from jax import lax
from jax.experimental import pallas as pl
from jax.sharding import PartitionSpec as P

HEAD_DIM = 128
POOLED = 128
CHUNKS = 4


def partner_2(block, axis, stride):
    count = lax.axis_size(axis)
    route = []
    for low in range(count):
        high = low | 1 << stride
        if high != low and high < count:
            route += [(low, high), (high, low)]
    return lax.ppermute(block, axis, route)


def attention_kernel(bias_ref, q_ref, do_ref, *refs, scale, parts):
    part_refs = refs[:parts]
    o_ref, dq_ref = refs[parts:parts + 2]
    grad_refs = refs[parts + 2:]
    q = q_ref[...]
    do = do_ref[...]
    k = jnp.concatenate([r[0] for r in part_refs], axis=0)
    v = jnp.concatenate([r[1] for r in part_refs], axis=0)
    scores = (
        lax.dot_general(q, k, (((1,), (1,)), ((), ())), preferred_element_type=jnp.float32) * scale
        + bias_ref[...]
    )
    row_max = jnp.max(scores, axis=-1, keepdims=True)
    shifted = jnp.exp(scores - row_max)
    weights = shifted * (1.0 / jnp.sum(shifted, axis=-1, keepdims=True))
    weights_low = weights.astype(jnp.bfloat16)
    attended = jnp.dot(weights_low, v, preferred_element_type=jnp.float32).astype(jnp.bfloat16)
    o_ref[...] = attended
    row_dot = jnp.sum(
        do.astype(jnp.float32) * attended.astype(jnp.float32), axis=-1, keepdims=True
    )
    weight_grad = lax.dot_general(do, v, (((1,), (1,)), ((), ())), preferred_element_type=jnp.float32)
    score_grad = (weights * (weight_grad - row_dot)).astype(jnp.bfloat16)
    dq_ref[...] = (
        jnp.dot(score_grad, k, preferred_element_type=jnp.float32) * scale
    ).astype(jnp.bfloat16)
    by_query = (((0,), (0,)), ((), ()))
    dk = lax.dot_general(score_grad, q, by_query, preferred_element_type=jnp.float32) * scale
    dv = lax.dot_general(weights_low, do, by_query, preferred_element_type=jnp.float32)
    first = 0
    for r in grad_refs:
        rows = r.shape[1]
        r[0] = dk[first:first + rows]
        r[1] = dv[first:first + rows]
        first += rows


def attention(query_rows, out_grad, parts, key_bias, score_scale, head_offset):
    leaf_rows = query_rows.shape[0]
    width = parts[0].shape[2]
    key_count = sum(p.shape[1] for p in parts)
    heads = width // HEAD_DIM
    row_in = pl.BlockSpec((leaf_rows, HEAD_DIM), lambda h: (0, h + head_offset))
    row_out = pl.BlockSpec((leaf_rows, HEAD_DIM), lambda h: (0, h))
    part_specs = [pl.BlockSpec((2, p.shape[1], HEAD_DIM), lambda h: (0, 0, h)) for p in parts]
    flops = 12 * leaf_rows * key_count * width
    io_bytes = 2 * (4 * leaf_rows + 2 * key_count) * width + 8 * key_count * width
    return pl.pallas_call(
        functools.partial(attention_kernel, scale=score_scale, parts=len(parts)),
        grid=(heads,),
        in_specs=[pl.BlockSpec((1, key_count), lambda h: (0, 0)), row_in, row_in] + part_specs,
        out_specs=[row_out, row_out] + part_specs,
        out_shape=[
            jax.ShapeDtypeStruct((leaf_rows, width), jnp.bfloat16),
            jax.ShapeDtypeStruct((leaf_rows, width), jnp.bfloat16),
        ] + [jax.ShapeDtypeStruct(p.shape, jnp.float32) for p in parts],
        cost_estimate=pl.CostEstimate(
            flops=flops, transcendentals=2 * leaf_rows * key_count * heads, bytes_accessed=io_bytes
        ),
    )(key_bias.reshape(1, key_count), query_rows, out_grad, *parts)


def after(value, earlier):
    return lax.optimization_barrier((value, earlier))[0]


def inner_pairs(count, level):
    mask = (1 << level) | (1 << (level - 1))
    return [(b, b ^ mask) for b in range(count) if (b >> level & 1) != (b >> (level - 1) & 1)]


def outer_pairs(count, level):
    return [(b, b ^ (1 << (level - 1))) for b in range(count) if (b >> level & 1) != (b >> (level - 1) & 1)]


def placed_pool(rows_in, upper):
    run = rows_in // (POOLED // 2)
    out_row = lax.broadcasted_iota(jnp.int32, (POOLED, rows_in), 0)
    in_row = lax.broadcasted_iota(jnp.int32, (POOLED, rows_in), 1)
    offset = upper * (POOLED // 2)
    return jnp.where(out_row - offset == in_row // run, 1.0 / run, 0.0).astype(jnp.float32)


def apply(matrix, rows):
    return jnp.einsum(
        "pr,krw->kpw", matrix, rows.astype(jnp.float32), precision=lax.Precision.HIGH,
        preferred_element_type=jnp.float32,
    )


def body(query_rows, key_rows, value_rows, out_grad):
    leaf_rows, model_width = query_rows.shape
    seq_count = lax.axis_size("seq")
    levels = seq_count.bit_length() - 1
    position = lax.axis_index("seq")
    pool_ratio = leaf_rows // POOLED
    score_scale = HEAD_DIM ** (-0.5)
    chunk_width = model_width // CHUNKS
    bias_parts = [jnp.zeros((2 * leaf_rows,), jnp.float32)]
    for step_level in range(1, levels):
        bias_parts.append(jnp.full((POOLED,), math.log(pool_ratio * 2**step_level), jnp.float32))
    key_bias = jnp.concatenate(bias_parts, axis=0)
    bits = [position // 2**step_level % 2 for step_level in range(levels)]
    inner = [None] + [bits[s] != bits[s - 1] for s in range(1, levels)]
    mine = [placed_pool(leaf_rows if s == 0 else POOLED, bits[s]) for s in range(levels)]
    other = [placed_pool(leaf_rows if s == 0 else POOLED, 1 - bits[s]) for s in range(levels)]
    pool_own = placed_pool(leaf_rows, 0)[: POOLED // 2]
    own_pooled = jnp.stack([
        jnp.dot(pool_own.astype(jnp.bfloat16), rows, preferred_element_type=jnp.float32)
        for rows in (key_rows, value_rows)
    ])
    sibling_pooled = partner_2(own_pooled.astype(jnp.bfloat16), "seq", 0)
    pick_row = lax.broadcasted_iota(jnp.int32, (POOLED // 2, POOLED), 0)
    pick_col = lax.broadcasted_iota(jnp.int32, (POOLED // 2, POOLED), 1)
    pick_other = jnp.where(
        pick_col == pick_row + (1 - bits[0]) * (POOLED // 2), 1.0, 0.0
    ).astype(jnp.float32)
    spread_own = pool_own.T
    place_mine = placed_pool(POOLED // 2, bits[0])
    place_other = placed_pool(POOLED // 2, 1 - bits[0])
    rows_out = [jnp.zeros((leaf_rows, model_width), jnp.bfloat16) for _ in range(2)]
    grads_out = [jnp.zeros((leaf_rows, model_width), jnp.bfloat16) for _ in range(2)]
    late = []
    for chunk in range(CHUNKS):
        columns = slice(chunk * chunk_width, (chunk + 1) * chunk_width)
        own = jnp.stack((key_rows[:, columns], value_rows[:, columns]))
        sibling = partner_2(after(own, sibling_pooled), "seq", 0)
        summary = apply(place_mine, own_pooled[:, :, columns]) + apply(
            place_other, sibling_pooled[:, :, columns]
        )
        far = []
        for step_level in range(1, levels):
            if step_level == 1:
                partner = partner_2(summary.astype(jnp.bfloat16), "seq", step_level)
            else:
                crossed = lax.ppermute(summary.astype(jnp.bfloat16), "seq", inner_pairs(seq_count, step_level))
                passed = lax.ppermute(crossed, "seq", outer_pairs(seq_count, step_level))
                partner = jnp.where(inner[step_level], crossed, passed)
            far.append(partner)
            if step_level + 1 < levels:
                summary = apply(mine[step_level], summary) + apply(other[step_level], partner)
        held = own
        if chunk >= 2:
            held = after(held, late[chunk - 2][1])
        if chunk >= 3:
            held = after(held, late[chunk - 3][0])
        outs = attention(
            query_rows, out_grad, [held, sibling] + far, key_bias, score_scale,
            chunk * (chunk_width // HEAD_DIM),
        )
        attended, query_grad, terms = outs[0], outs[1], outs[2:]
        grad = None
        sends = {}
        for step_level in reversed(range(1, levels)):
            outgoing = terms[1 + step_level]
            if grad is not None:
                outgoing = outgoing + apply(other[step_level].T, grad)
            sends[step_level] = outgoing.astype(jnp.bfloat16)
            if step_level == 1:
                returned = partner_2(sends[step_level], "seq", step_level)
            else:
                back = [(t, s) for s, t in outer_pairs(seq_count, step_level)]
                gathered = lax.ppermute(sends[step_level], "seq", back)
                total = outgoing + gathered.astype(jnp.float32)
                returned = lax.ppermute(total.astype(jnp.bfloat16), "seq", inner_pairs(seq_count, step_level))
            if grad is None:
                grad = returned.astype(jnp.float32)
            else:
                grad = apply(mine[step_level].T, grad) + returned
        to_sibling = terms[1]
        own_total = terms[0]
        split = chunk == CHUNKS - 1 and grad is not None
        if grad is not None:
            if not split:
                to_sibling = to_sibling + apply(other[0].T, grad)
            own_total = own_total + apply(mine[0].T, grad)
        sibling_send = to_sibling.astype(jnp.bfloat16)
        late.append((sibling_send, sends.get(1, sibling_send)))
        from_sibling = partner_2(sibling_send, "seq", 0)
        if split:
            pooled_back = partner_2(apply(pick_other, grad).astype(jnp.bfloat16), "seq", 0)
            own_total = own_total + apply(spread_own, pooled_back)
        totals = own_total + from_sibling.astype(jnp.float32)
        for slot, piece in enumerate((attended, query_grad)):
            rows_out[slot] = lax.dynamic_update_slice(rows_out[slot], piece, (0, columns.start))
        for slot in range(2):
            grads_out[slot] = lax.dynamic_update_slice(
                grads_out[slot], totals[slot].astype(jnp.bfloat16), (0, columns.start)
            )
    return tuple(rows_out) + tuple(grads_out)


def solution(mesh):
    spec = P(("batch", "seq"), None)
    return jax.shard_map(
        body, mesh=mesh, in_specs=(spec, spec, spec, spec), out_specs=(spec, spec, spec, spec),
        check_vma=False,
    )
```

```python
import functools
import math

import jax
import jax.numpy as jnp
from jax import lax
from jax.experimental import pallas as pl
from jax.sharding import PartitionSpec as P

HEAD_DIM = 128
POOLED = 128
CHUNKS = 4


def partner_2(block, axis, stride):
    count = lax.axis_size(axis)
    route = []
    for low in range(count):
        high = low | 1 << stride
        if high != low and high < count:
            route += [(low, high), (high, low)]
    return lax.ppermute(block, axis, route)


def attention_kernel(bias_ref, q_ref, do_ref, *refs, scale, parts):
    part_refs = refs[:parts]
    o_ref, dq_ref = refs[parts:parts + 2]
    grad_refs = refs[parts + 2:]
    q = q_ref[...]
    do = do_ref[...]
    k = jnp.concatenate([r[0] for r in part_refs], axis=0)
    v = jnp.concatenate([r[1] for r in part_refs], axis=0)
    scores = (
        lax.dot_general(q, k, (((1,), (1,)), ((), ())), preferred_element_type=jnp.float32) * scale
        + bias_ref[...]
    )
    row_max = jnp.max(scores, axis=-1, keepdims=True)
    shifted = jnp.exp(scores - row_max)
    weights = shifted * (1.0 / jnp.sum(shifted, axis=-1, keepdims=True))
    weights_low = weights.astype(jnp.bfloat16)
    attended = jnp.dot(weights_low, v, preferred_element_type=jnp.float32).astype(jnp.bfloat16)
    o_ref[...] = attended
    row_dot = jnp.sum(
        do.astype(jnp.float32) * attended.astype(jnp.float32), axis=-1, keepdims=True
    )
    weight_grad = lax.dot_general(do, v, (((1,), (1,)), ((), ())), preferred_element_type=jnp.float32)
    score_grad = (weights * (weight_grad - row_dot)).astype(jnp.bfloat16)
    dq_ref[...] = (
        jnp.dot(score_grad, k, preferred_element_type=jnp.float32) * scale
    ).astype(jnp.bfloat16)
    by_query = (((0,), (0,)), ((), ()))
    dk = lax.dot_general(score_grad, q, by_query, preferred_element_type=jnp.float32) * scale
    dv = lax.dot_general(weights_low, do, by_query, preferred_element_type=jnp.float32)
    first = 0
    for r in grad_refs:
        rows = r.shape[1]
        r[0] = dk[first:first + rows]
        r[1] = dv[first:first + rows]
        first += rows


def attention(query_rows, out_grad, parts, key_bias, score_scale, head_offset):
    leaf_rows = query_rows.shape[0]
    width = parts[0].shape[2]
    key_count = sum(p.shape[1] for p in parts)
    heads = width // HEAD_DIM
    row_in = pl.BlockSpec((leaf_rows, HEAD_DIM), lambda h: (0, h + head_offset))
    row_out = pl.BlockSpec((leaf_rows, HEAD_DIM), lambda h: (0, h))
    part_specs = [pl.BlockSpec((2, p.shape[1], HEAD_DIM), lambda h: (0, 0, h)) for p in parts]
    flops = 12 * leaf_rows * key_count * width
    io_bytes = 2 * (4 * leaf_rows + 2 * key_count) * width + 8 * key_count * width
    return pl.pallas_call(
        functools.partial(attention_kernel, scale=score_scale, parts=len(parts)),
        grid=(heads,),
        in_specs=[pl.BlockSpec((1, key_count), lambda h: (0, 0)), row_in, row_in] + part_specs,
        out_specs=[row_out, row_out] + part_specs,
        out_shape=[
            jax.ShapeDtypeStruct((leaf_rows, width), jnp.bfloat16),
            jax.ShapeDtypeStruct((leaf_rows, width), jnp.bfloat16),
        ] + [jax.ShapeDtypeStruct(p.shape, jnp.float32) for p in parts],
        cost_estimate=pl.CostEstimate(
            flops=flops, transcendentals=2 * leaf_rows * key_count * heads, bytes_accessed=io_bytes
        ),
    )(key_bias.reshape(1, key_count), query_rows, out_grad, *parts)


def after(value, earlier):
    return lax.optimization_barrier((value, earlier))[0]


def inner_pairs(count, level):
    mask = (1 << level) | (1 << (level - 1))
    return [(b, b ^ mask) for b in range(count) if (b >> level & 1) != (b >> (level - 1) & 1)]


def outer_pairs(count, level):
    return [(b, b ^ (1 << (level - 1))) for b in range(count) if (b >> level & 1) != (b >> (level - 1) & 1)]


def placed_pool(rows_in, upper):
    run = rows_in // (POOLED // 2)
    out_row = lax.broadcasted_iota(jnp.int32, (POOLED, rows_in), 0)
    in_row = lax.broadcasted_iota(jnp.int32, (POOLED, rows_in), 1)
    offset = upper * (POOLED // 2)
    return jnp.where(out_row - offset == in_row // run, 1.0 / run, 0.0).astype(jnp.float32)


def apply(matrix, rows):
    return jnp.einsum(
        "pr,krw->kpw", matrix, rows.astype(jnp.float32), precision=lax.Precision.DEFAULT,
        preferred_element_type=jnp.float32,
    )


def body(query_rows, key_rows, value_rows, out_grad):
    leaf_rows, model_width = query_rows.shape
    seq_count = lax.axis_size("seq")
    levels = seq_count.bit_length() - 1
    position = lax.axis_index("seq")
    pool_ratio = leaf_rows // POOLED
    score_scale = HEAD_DIM ** (-0.5)
    chunk_width = model_width // CHUNKS
    bias_parts = [jnp.zeros((2 * leaf_rows,), jnp.float32)]
    for step_level in range(1, levels):
        bias_parts.append(jnp.full((POOLED,), math.log(pool_ratio * 2**step_level), jnp.float32))
    key_bias = jnp.concatenate(bias_parts, axis=0)
    bits = [position // 2**step_level % 2 for step_level in range(levels)]
    inner = [None] + [bits[s] != bits[s - 1] for s in range(1, levels)]
    mine = [placed_pool(leaf_rows if s == 0 else POOLED, bits[s]) for s in range(levels)]
    other = [placed_pool(leaf_rows if s == 0 else POOLED, 1 - bits[s]) for s in range(levels)]
    pool_own = placed_pool(leaf_rows, 0)[: POOLED // 2]
    own_pooled = jnp.stack([
        jnp.dot(pool_own.astype(jnp.bfloat16), rows, preferred_element_type=jnp.float32)
        for rows in (key_rows, value_rows)
    ])
    sibling_pooled = partner_2(own_pooled.astype(jnp.bfloat16), "seq", 0)
    pick_row = lax.broadcasted_iota(jnp.int32, (POOLED // 2, POOLED), 0)
    pick_col = lax.broadcasted_iota(jnp.int32, (POOLED // 2, POOLED), 1)
    pick_other = jnp.where(
        pick_col == pick_row + (1 - bits[0]) * (POOLED // 2), 1.0, 0.0
    ).astype(jnp.float32)
    spread_own = pool_own.T
    place_mine = placed_pool(POOLED // 2, bits[0])
    place_other = placed_pool(POOLED // 2, 1 - bits[0])
    pieces = [[], []]
    grads_out = [jnp.zeros((leaf_rows, model_width), jnp.bfloat16) for _ in range(2)]
    late = []
    for chunk in range(CHUNKS):
        columns = slice(chunk * chunk_width, (chunk + 1) * chunk_width)
        own = jnp.stack((key_rows[:, columns], value_rows[:, columns]))
        sibling = partner_2(after(own, sibling_pooled), "seq", 0)
        summary = apply(place_mine, own_pooled[:, :, columns]) + apply(
            place_other, sibling_pooled[:, :, columns]
        )
        far = []
        for step_level in range(1, levels):
            if step_level == 1:
                partner = partner_2(summary.astype(jnp.bfloat16), "seq", step_level)
            else:
                crossed = lax.ppermute(summary.astype(jnp.bfloat16), "seq", inner_pairs(seq_count, step_level))
                passed = lax.ppermute(crossed, "seq", outer_pairs(seq_count, step_level))
                partner = jnp.where(inner[step_level], crossed, passed)
            far.append(partner)
            if step_level + 1 < levels:
                summary = apply(mine[step_level], summary) + apply(other[step_level], partner)
        held = own
        if chunk >= 2:
            held = after(held, late[chunk - 2][1])
        if chunk >= 3:
            held = after(held, late[chunk - 3][0])
        outs = attention(
            query_rows, out_grad, [held, sibling] + far, key_bias, score_scale,
            chunk * (chunk_width // HEAD_DIM),
        )
        attended, query_grad, terms = outs[0], outs[1], outs[2:]
        grad = None
        sends = {}
        for step_level in reversed(range(1, levels)):
            outgoing = terms[1 + step_level]
            if grad is not None:
                outgoing = outgoing + apply(other[step_level].T, grad)
            sends[step_level] = outgoing.astype(jnp.bfloat16)
            if step_level == 1:
                returned = partner_2(sends[step_level], "seq", step_level)
            else:
                back = [(t, s) for s, t in outer_pairs(seq_count, step_level)]
                gathered = lax.ppermute(sends[step_level], "seq", back)
                total = outgoing + gathered.astype(jnp.float32)
                returned = lax.ppermute(total.astype(jnp.bfloat16), "seq", inner_pairs(seq_count, step_level))
            if grad is None:
                grad = returned.astype(jnp.float32)
            else:
                grad = apply(mine[step_level].T, grad) + returned
        to_sibling = terms[1]
        own_total = terms[0]
        split = chunk == CHUNKS - 1 and grad is not None
        if grad is not None:
            if not split:
                to_sibling = to_sibling + apply(other[0].T, grad)
            own_total = own_total + apply(mine[0].T, grad)
        sibling_send = to_sibling.astype(jnp.bfloat16)
        late.append((sibling_send, sends.get(1, sibling_send)))
        from_sibling = partner_2(sibling_send, "seq", 0)
        if split:
            pooled_back = partner_2(apply(pick_other, grad).astype(jnp.bfloat16), "seq", 0)
            own_total = own_total + apply(spread_own, pooled_back)
        totals = own_total + from_sibling.astype(jnp.float32)
        for slot, piece in enumerate((attended, query_grad)):
            pieces[slot].append(piece)
        for slot in range(2):
            grads_out[slot] = lax.dynamic_update_slice(
                grads_out[slot], totals[slot].astype(jnp.bfloat16), (0, columns.start)
            )
    return tuple(jnp.concatenate(p, axis=1) for p in pieces[:2]) + tuple(grads_out)


def solution(mesh):
    spec = P(("batch", "seq"), None)
    return jax.shard_map(
        body, mesh=mesh, in_specs=(spec, spec, spec, spec), out_specs=(spec, spec, spec, spec),
        check_vma=False,
    )
```

```python
import functools
import math

import jax
import jax.numpy as jnp
from jax import lax
from jax.experimental import pallas as pl
from jax.sharding import PartitionSpec as P

HEAD_DIM = 128
POOLED = 128
CHUNKS = 4


def partner_2(block, axis, stride):
    count = lax.axis_size(axis)
    route = []
    for low in range(count):
        high = low | 1 << stride
        if high != low and high < count:
            route += [(low, high), (high, low)]
    return lax.ppermute(block, axis, route)


def attention_kernel(bias_ref, q_ref, do_ref, *refs, scale, parts):
    part_refs = refs[:parts]
    o_ref, dq_ref = refs[parts:parts + 2]
    grad_refs = refs[parts + 2:]
    q = q_ref[...]
    do = do_ref[...]
    k = jnp.concatenate([r[0] for r in part_refs], axis=0)
    v = jnp.concatenate([r[1] for r in part_refs], axis=0)
    scores = (
        lax.dot_general(q, k, (((1,), (1,)), ((), ())), preferred_element_type=jnp.float32) * scale
        + bias_ref[...]
    )
    row_max = jnp.max(scores, axis=-1, keepdims=True)
    shifted = jnp.exp(scores - row_max)
    weights = shifted * (1.0 / jnp.sum(shifted, axis=-1, keepdims=True))
    weights_low = weights.astype(jnp.bfloat16)
    attended = jnp.dot(weights_low, v, preferred_element_type=jnp.float32).astype(jnp.bfloat16)
    o_ref[...] = attended
    row_dot = jnp.sum(
        do.astype(jnp.float32) * attended.astype(jnp.float32), axis=-1, keepdims=True
    )
    weight_grad = lax.dot_general(do, v, (((1,), (1,)), ((), ())), preferred_element_type=jnp.float32)
    score_grad = (weights * (weight_grad - row_dot)).astype(jnp.bfloat16)
    dq_ref[...] = (
        jnp.dot(score_grad, k, preferred_element_type=jnp.float32) * scale
    ).astype(jnp.bfloat16)
    by_query = (((0,), (0,)), ((), ()))
    dk = lax.dot_general(score_grad, q, by_query, preferred_element_type=jnp.float32) * scale
    dv = lax.dot_general(weights_low, do, by_query, preferred_element_type=jnp.float32)
    first = 0
    for r in grad_refs:
        rows = r.shape[1]
        r[0] = dk[first:first + rows]
        r[1] = dv[first:first + rows]
        first += rows


def attention(query_rows, out_grad, parts, key_bias, score_scale, head_offset):
    leaf_rows = query_rows.shape[0]
    width = parts[0].shape[2]
    key_count = sum(p.shape[1] for p in parts)
    heads = width // HEAD_DIM
    row_in = pl.BlockSpec((leaf_rows, HEAD_DIM), lambda h: (0, h + head_offset))
    row_out = pl.BlockSpec((leaf_rows, HEAD_DIM), lambda h: (0, h))
    part_specs = [pl.BlockSpec((2, p.shape[1], HEAD_DIM), lambda h: (0, 0, h)) for p in parts]
    flops = 12 * leaf_rows * key_count * width
    io_bytes = 2 * (4 * leaf_rows + 2 * key_count) * width + 8 * key_count * width
    return pl.pallas_call(
        functools.partial(attention_kernel, scale=score_scale, parts=len(parts)),
        grid=(heads,),
        in_specs=[pl.BlockSpec((1, key_count), lambda h: (0, 0)), row_in, row_in] + part_specs,
        out_specs=[row_out, row_out] + part_specs,
        out_shape=[
            jax.ShapeDtypeStruct((leaf_rows, width), jnp.bfloat16),
            jax.ShapeDtypeStruct((leaf_rows, width), jnp.bfloat16),
        ] + [jax.ShapeDtypeStruct(p.shape, jnp.float32) for p in parts],
        cost_estimate=pl.CostEstimate(
            flops=flops, transcendentals=2 * leaf_rows * key_count * heads, bytes_accessed=io_bytes
        ),
    )(key_bias.reshape(1, key_count), query_rows, out_grad, *parts)


def after(value, earlier):
    return lax.optimization_barrier((value, earlier))[0]


def inner_pairs(count, level):
    mask = (1 << level) | (1 << (level - 1))
    return [(b, b ^ mask) for b in range(count) if (b >> level & 1) != (b >> (level - 1) & 1)]


def outer_pairs(count, level):
    return [(b, b ^ (1 << (level - 1))) for b in range(count) if (b >> level & 1) != (b >> (level - 1) & 1)]


def placed_pool(rows_in, upper):
    run = rows_in // (POOLED // 2)
    out_row = lax.broadcasted_iota(jnp.int32, (POOLED, rows_in), 0)
    in_row = lax.broadcasted_iota(jnp.int32, (POOLED, rows_in), 1)
    offset = upper * (POOLED // 2)
    return jnp.where(out_row - offset == in_row // run, 1.0 / run, 0.0).astype(jnp.float32)


def apply(matrix, rows):
    return jnp.einsum(
        "pr,krw->kpw", matrix, rows.astype(jnp.float32), precision=lax.Precision.DEFAULT,
        preferred_element_type=jnp.float32,
    )


def body(query_rows, key_rows, value_rows, out_grad):
    leaf_rows, model_width = query_rows.shape
    seq_count = lax.axis_size("seq")
    levels = seq_count.bit_length() - 1
    position = lax.axis_index("seq")
    pool_ratio = leaf_rows // POOLED
    score_scale = HEAD_DIM ** (-0.5)
    chunk_width = model_width // CHUNKS
    bias_parts = [jnp.zeros((2 * leaf_rows,), jnp.float32)]
    for step_level in range(1, levels):
        bias_parts.append(jnp.full((POOLED,), math.log(pool_ratio * 2**step_level), jnp.float32))
    key_bias = jnp.concatenate(bias_parts, axis=0)
    bits = [position // 2**step_level % 2 for step_level in range(levels)]
    inner = [None] + [bits[s] != bits[s - 1] for s in range(1, levels)]
    mine = [placed_pool(leaf_rows if s == 0 else POOLED, bits[s]) for s in range(levels)]
    other = [placed_pool(leaf_rows if s == 0 else POOLED, 1 - bits[s]) for s in range(levels)]
    pool_own = placed_pool(leaf_rows, 0)[: POOLED // 2]
    own_pooled = jnp.stack([
        jnp.dot(pool_own.astype(jnp.bfloat16), rows, preferred_element_type=jnp.float32)
        for rows in (key_rows, value_rows)
    ])
    sibling_pooled = partner_2(own_pooled.astype(jnp.bfloat16), "seq", 0)
    pick_row = lax.broadcasted_iota(jnp.int32, (POOLED // 2, POOLED), 0)
    pick_col = lax.broadcasted_iota(jnp.int32, (POOLED // 2, POOLED), 1)
    pick_other = jnp.where(
        pick_col == pick_row + (1 - bits[0]) * (POOLED // 2), 1.0, 0.0
    ).astype(jnp.float32)
    spread_own = pool_own.T
    place_mine = placed_pool(POOLED // 2, bits[0])
    place_other = placed_pool(POOLED // 2, 1 - bits[0])
    pieces = [[], []]
    grads_out = [jnp.zeros((leaf_rows, model_width), jnp.bfloat16) for _ in range(2)]
    late = []
    for chunk in range(CHUNKS):
        columns = slice(chunk * chunk_width, (chunk + 1) * chunk_width)
        own = jnp.stack((key_rows[:, columns], value_rows[:, columns]))
        sibling = partner_2(after(own, sibling_pooled), "seq", 0)
        summary = apply(place_mine, own_pooled[:, :, columns]) + apply(
            place_other, sibling_pooled[:, :, columns]
        )
        far = []
        for step_level in range(1, levels):
            if step_level == 1:
                partner = partner_2(summary.astype(jnp.bfloat16), "seq", step_level)
            else:
                crossed = lax.ppermute(summary.astype(jnp.bfloat16), "seq", inner_pairs(seq_count, step_level))
                passed = lax.ppermute(crossed, "seq", outer_pairs(seq_count, step_level))
                partner = jnp.where(inner[step_level], crossed, passed)
            far.append(partner)
            if step_level + 1 < levels:
                summary = apply(mine[step_level], summary) + apply(other[step_level], partner)
        held = own
        if chunk >= 1:
            held = after(held, late[chunk - 1][2])
        if chunk >= 2:
            held = after(held, late[chunk - 2][1])
        if chunk >= 3:
            held = after(held, late[chunk - 3][0])
        outs = attention(
            query_rows, out_grad, [held, sibling] + far, key_bias, score_scale,
            chunk * (chunk_width // HEAD_DIM),
        )
        attended, query_grad, terms = outs[0], outs[1], outs[2:]
        grad = None
        sends = {}
        for step_level in reversed(range(1, levels)):
            outgoing = terms[1 + step_level]
            if grad is not None:
                outgoing = outgoing + apply(other[step_level].T, grad)
            sends[step_level] = outgoing.astype(jnp.bfloat16)
            if step_level == 1:
                returned = partner_2(sends[step_level], "seq", step_level)
            else:
                back = [(t, s) for s, t in outer_pairs(seq_count, step_level)]
                gathered = lax.ppermute(sends[step_level], "seq", back)
                total = outgoing + gathered.astype(jnp.float32)
                returned = lax.ppermute(total.astype(jnp.bfloat16), "seq", inner_pairs(seq_count, step_level))
            if grad is None:
                grad = returned.astype(jnp.float32)
            else:
                grad = apply(mine[step_level].T, grad) + returned
        to_sibling = terms[1]
        own_total = terms[0]
        split = chunk == CHUNKS - 1 and grad is not None
        if grad is not None:
            if not split:
                to_sibling = to_sibling + apply(other[0].T, grad)
            own_total = own_total + apply(mine[0].T, grad)
        sibling_send = to_sibling.astype(jnp.bfloat16)
        late.append((sibling_send, sends.get(1, sibling_send), sends.get(levels - 1, sibling_send)))
        from_sibling = partner_2(sibling_send, "seq", 0)
        if split:
            pooled_back = partner_2(apply(pick_other, grad).astype(jnp.bfloat16), "seq", 0)
            own_total = own_total + apply(spread_own, pooled_back)
        totals = own_total + from_sibling.astype(jnp.float32)
        for slot, piece in enumerate((attended, query_grad)):
            pieces[slot].append(piece)
        for slot in range(2):
            grads_out[slot] = lax.dynamic_update_slice(
                grads_out[slot], totals[slot].astype(jnp.bfloat16), (0, columns.start)
            )
    return tuple(jnp.concatenate(p, axis=1) for p in pieces[:2]) + tuple(grads_out)


def solution(mesh):
    spec = P(("batch", "seq"), None)
    return jax.shard_map(
        body, mesh=mesh, in_specs=(spec, spec, spec, spec), out_specs=(spec, spec, spec, spec),
        check_vma=False,
    )
```

```python
import functools
import math

import jax
import jax.numpy as jnp
from jax import lax
from jax.experimental import pallas as pl
from jax.sharding import PartitionSpec as P

HEAD_DIM = 128
POOLED = 128
CHUNKS = 4


def partner_2(block, axis, stride):
    count = lax.axis_size(axis)
    route = []
    for low in range(count):
        high = low | 1 << stride
        if high != low and high < count:
            route += [(low, high), (high, low)]
    return lax.ppermute(block, axis, route)


def attention_kernel(bias_ref, q_ref, do_ref, *refs, scale, parts):
    part_refs = refs[:parts]
    o_ref, dq_ref = refs[parts:parts + 2]
    grad_refs = refs[parts + 2:]
    q = q_ref[...]
    do = do_ref[...]
    k = jnp.concatenate([r[0] for r in part_refs], axis=0)
    v = jnp.concatenate([r[1] for r in part_refs], axis=0)
    scores = (
        lax.dot_general(q, k, (((1,), (1,)), ((), ())), preferred_element_type=jnp.float32) * scale
        + bias_ref[...]
    )
    row_max = jnp.max(scores, axis=-1, keepdims=True)
    shifted = jnp.exp(scores - row_max)
    weights = shifted * (1.0 / jnp.sum(shifted, axis=-1, keepdims=True))
    weights_low = weights.astype(jnp.bfloat16)
    attended = jnp.dot(weights_low, v, preferred_element_type=jnp.float32).astype(jnp.bfloat16)
    o_ref[...] = attended
    row_dot = jnp.sum(
        do.astype(jnp.float32) * attended.astype(jnp.float32), axis=-1, keepdims=True
    )
    weight_grad = lax.dot_general(do, v, (((1,), (1,)), ((), ())), preferred_element_type=jnp.float32)
    score_grad = (weights * (weight_grad - row_dot)).astype(jnp.bfloat16)
    dq_ref[...] = (
        jnp.dot(score_grad, k, preferred_element_type=jnp.float32) * scale
    ).astype(jnp.bfloat16)
    by_query = (((0,), (0,)), ((), ()))
    dk = lax.dot_general(score_grad, q, by_query, preferred_element_type=jnp.float32) * scale
    dv = lax.dot_general(weights_low, do, by_query, preferred_element_type=jnp.float32)
    first = 0
    for r in grad_refs:
        rows = r.shape[1]
        r[0] = dk[first:first + rows].astype(r.dtype)
        r[1] = dv[first:first + rows].astype(r.dtype)
        first += rows


def attention(query_rows, out_grad, parts, key_bias, score_scale, head_offset):
    leaf_rows = query_rows.shape[0]
    width = parts[0].shape[2]
    key_count = sum(p.shape[1] for p in parts)
    heads = width // HEAD_DIM
    row_in = pl.BlockSpec((leaf_rows, HEAD_DIM), lambda h: (0, h + head_offset))
    row_out = pl.BlockSpec((leaf_rows, HEAD_DIM), lambda h: (0, h))
    part_specs = [pl.BlockSpec((2, p.shape[1], HEAD_DIM), lambda h: (0, 0, h)) for p in parts]
    flops = 12 * leaf_rows * key_count * width
    io_bytes = 2 * (4 * leaf_rows + 2 * key_count) * width + 8 * key_count * width
    return pl.pallas_call(
        functools.partial(attention_kernel, scale=score_scale, parts=len(parts)),
        grid=(heads,),
        in_specs=[pl.BlockSpec((1, key_count), lambda h: (0, 0)), row_in, row_in] + part_specs,
        out_specs=[row_out, row_out] + part_specs,
        out_shape=[
            jax.ShapeDtypeStruct((leaf_rows, width), jnp.bfloat16),
            jax.ShapeDtypeStruct((leaf_rows, width), jnp.bfloat16),
        ] + [jax.ShapeDtypeStruct(p.shape, jnp.float32) for p in parts[:-1]]
        + [jax.ShapeDtypeStruct(parts[-1].shape, jnp.bfloat16)],
        cost_estimate=pl.CostEstimate(
            flops=flops, transcendentals=2 * leaf_rows * key_count * heads, bytes_accessed=io_bytes
        ),
    )(key_bias.reshape(1, key_count), query_rows, out_grad, *parts)


def after(value, earlier):
    return lax.optimization_barrier((value, earlier))[0]


def inner_pairs(count, level):
    mask = (1 << level) | (1 << (level - 1))
    return [(b, b ^ mask) for b in range(count) if (b >> level & 1) != (b >> (level - 1) & 1)]


def outer_pairs(count, level):
    return [(b, b ^ (1 << (level - 1))) for b in range(count) if (b >> level & 1) != (b >> (level - 1) & 1)]


def placed_pool(rows_in, upper):
    run = rows_in // (POOLED // 2)
    out_row = lax.broadcasted_iota(jnp.int32, (POOLED, rows_in), 0)
    in_row = lax.broadcasted_iota(jnp.int32, (POOLED, rows_in), 1)
    offset = upper * (POOLED // 2)
    return jnp.where(out_row - offset == in_row // run, 1.0 / run, 0.0).astype(jnp.float32)


def apply(matrix, rows):
    return jnp.einsum(
        "pr,krw->kpw", matrix, rows.astype(jnp.float32), precision=lax.Precision.DEFAULT,
        preferred_element_type=jnp.float32,
    )


def body(query_rows, key_rows, value_rows, out_grad):
    leaf_rows, model_width = query_rows.shape
    seq_count = lax.axis_size("seq")
    levels = seq_count.bit_length() - 1
    position = lax.axis_index("seq")
    pool_ratio = leaf_rows // POOLED
    score_scale = HEAD_DIM ** (-0.5)
    chunk_width = model_width // CHUNKS
    bias_parts = [jnp.zeros((2 * leaf_rows,), jnp.float32)]
    for step_level in range(1, levels):
        bias_parts.append(jnp.full((POOLED,), math.log(pool_ratio * 2**step_level), jnp.float32))
    key_bias = jnp.concatenate(bias_parts, axis=0)
    bits = [position // 2**step_level % 2 for step_level in range(levels)]
    inner = [None] + [bits[s] != bits[s - 1] for s in range(1, levels)]
    mine = [placed_pool(leaf_rows if s == 0 else POOLED, bits[s]) for s in range(levels)]
    other = [placed_pool(leaf_rows if s == 0 else POOLED, 1 - bits[s]) for s in range(levels)]
    pool_own = placed_pool(leaf_rows, 0)[: POOLED // 2]
    own_pooled = jnp.stack([
        jnp.dot(pool_own.astype(jnp.bfloat16), rows, preferred_element_type=jnp.float32)
        for rows in (key_rows, value_rows)
    ])
    sibling_pooled = partner_2(own_pooled.astype(jnp.bfloat16), "seq", 0)
    pick_row = lax.broadcasted_iota(jnp.int32, (POOLED // 2, POOLED), 0)
    pick_col = lax.broadcasted_iota(jnp.int32, (POOLED // 2, POOLED), 1)
    pick_other = jnp.where(
        pick_col == pick_row + (1 - bits[0]) * (POOLED // 2), 1.0, 0.0
    ).astype(jnp.float32)
    spread_own = pool_own.T
    place_mine = placed_pool(POOLED // 2, bits[0])
    place_other = placed_pool(POOLED // 2, 1 - bits[0])
    pieces = [[], []]
    grads_out = [jnp.zeros((leaf_rows, model_width), jnp.bfloat16) for _ in range(2)]
    late = []
    for chunk in range(CHUNKS):
        columns = slice(chunk * chunk_width, (chunk + 1) * chunk_width)
        own = jnp.stack((key_rows[:, columns], value_rows[:, columns]))
        sibling = partner_2(after(own, sibling_pooled), "seq", 0)
        summary = apply(place_mine, own_pooled[:, :, columns]) + apply(
            place_other, sibling_pooled[:, :, columns]
        )
        far = []
        for step_level in range(1, levels):
            if step_level == 1:
                partner = partner_2(summary.astype(jnp.bfloat16), "seq", step_level)
            else:
                crossed = lax.ppermute(summary.astype(jnp.bfloat16), "seq", inner_pairs(seq_count, step_level))
                passed = lax.ppermute(crossed, "seq", outer_pairs(seq_count, step_level))
                partner = jnp.where(inner[step_level], crossed, passed)
            far.append(partner)
            if step_level + 1 < levels:
                summary = apply(mine[step_level], summary) + apply(other[step_level], partner)
        held = own
        if chunk >= 2:
            held = after(held, late[chunk - 2][1])
        if chunk >= 3:
            held = after(held, late[chunk - 3][0])
        outs = attention(
            query_rows, out_grad, [held, sibling] + far, key_bias, score_scale,
            chunk * (chunk_width // HEAD_DIM),
        )
        attended, query_grad, terms = outs[0], outs[1], outs[2:]
        grad = None
        sends = {}
        for step_level in reversed(range(1, levels)):
            outgoing = terms[1 + step_level]
            if grad is not None:
                outgoing = outgoing + apply(other[step_level].T, grad)
            sends[step_level] = outgoing.astype(jnp.bfloat16)
            if step_level == 1:
                returned = partner_2(sends[step_level], "seq", step_level)
            else:
                back = [(t, s) for s, t in outer_pairs(seq_count, step_level)]
                gathered = lax.ppermute(sends[step_level], "seq", back)
                total = outgoing + gathered.astype(jnp.float32)
                returned = lax.ppermute(total.astype(jnp.bfloat16), "seq", inner_pairs(seq_count, step_level))
            if grad is None:
                grad = returned.astype(jnp.float32)
            else:
                grad = apply(mine[step_level].T, grad) + returned
        to_sibling = terms[1]
        own_total = terms[0]
        split = chunk == CHUNKS - 1 and grad is not None
        if grad is not None:
            if not split:
                to_sibling = to_sibling + apply(other[0].T, grad)
            own_total = own_total + apply(mine[0].T, grad)
        sibling_send = to_sibling.astype(jnp.bfloat16)
        late.append((sibling_send, sends.get(1, sibling_send)))
        from_sibling = partner_2(sibling_send, "seq", 0)
        if split:
            pooled_back = partner_2(apply(pick_other, grad).astype(jnp.bfloat16), "seq", 0)
            own_total = own_total + apply(spread_own, pooled_back)
        totals = own_total + from_sibling.astype(jnp.float32)
        for slot, piece in enumerate((attended, query_grad)):
            pieces[slot].append(piece)
        for slot in range(2):
            grads_out[slot] = lax.dynamic_update_slice(
                grads_out[slot], totals[slot].astype(jnp.bfloat16), (0, columns.start)
            )
    return tuple(jnp.concatenate(p, axis=1) for p in pieces[:2]) + tuple(grads_out)


def solution(mesh):
    spec = P(("batch", "seq"), None)
    return jax.shard_map(
        body, mesh=mesh, in_specs=(spec, spec, spec, spec), out_specs=(spec, spec, spec, spec),
        check_vma=False,
    )
```
